32 devices in a mesh: timepoin: 2 (over y), tile: 4 (over z), view: 4 (over x, core).
Axes of the slice: x: 2, y: 2, z: 4, core: 2. Of those that a mesh axis runs over, the one named last changes fastest.
Arguments:
- acquired: bfloat16 [512, 128, 128], P(('timepoin', 'view'), 'tile'), parts along dimension 0, may hold values from 0.19921875 to 5
- psf_taps: float32 [2, 3, 31], replicated, may hold values from 0.1 to 1
- block_source: int32 [8, 32], P(('timepoin', 'view')), parts along dimension 0, may hold values from 0 to 31, as said below
Outputs:
- estimate: float32 [256, 128, 128], P(('timepoin', 'view'), 'tile'), parts along dimension 0
The draws below stay inside these ranges and needn't reach their ends.
There are 2 independent parts, one for each index of `timepoin`. The reference program is written for one: setup_inputs(seed, part) draws one part's arguments, and reference() takes and returns one part's arrays. A program takes and returns all parts, laid end to end along the dimension named above; an argument that names none is the same for every part. Nothing has to cross between parts.
Inputs may be any that keep to these rules, and one draw needn't show every extreme that they name: `block_source`: entry (r, q) names the global view block of row r's stack that fills joined x-block q. With t the tile of q, blocks in the first half of tile t come from tile t or t - 1 and those in the second half from tile t or t + 1 (kept within the tiles), so at most 4 blocks of a tile come from one neighbouring tile; some tile takes exactly 4 from one neighbour.
All inputs are finite; a program needn't handle non-finite values.
Results may differ from the reference program's by a relative error of at most 0.00081.
Values may be sent and summed in bfloat16 or wider, within the bound.
No kernel may reach another device: no remote copies, remote signals or barrier semaphores. Data moves between devices by JAX's collectives and lax.ppermute only.
A program may use at most 64 MiB of HBM per device.

```python
import math
import jax
import jax.numpy as jnp
from jax import lax

CX = 32
NY = 128
CZ = 64
BX = 4
TAPS = 31
ITERS = 2
NX = 128
NZ = 128
ZV = 256
N_VIEW = 4


def draw_block_source(key, part):
    per_tile = CX // BX
    half_count = per_tile // 2
    tile_count = NX // CX
    row_count = ZV // CZ
    key_side, key_block = jax.random.split(key)
    shape = (row_count, tile_count, per_tile)
    sides = jax.random.randint(key_side, shape, 0, 2)
    row_ids = jnp.arange(row_count)[:, None, None]
    tile_ids = jnp.arange(tile_count)[None, :, None]
    slot_ids = jnp.arange(per_tile)[None, None, :]
    signs = jnp.where(slot_ids < half_count, -1, 1)
    tiles = tile_ids + sides * signs
    forced = (row_ids == 0) & (tile_ids == 1) & (slot_ids < half_count)
    tiles = jnp.where(forced, 0, tiles)
    tiles = jnp.clip(tiles, 0, tile_count - 1)
    chosen = jax.random.randint(key_block, shape, 0, per_tile)
    first_entry = (row_ids == 0) & (tile_ids == 0) & (slot_ids == 0)
    chosen = jnp.where(first_entry, 0, chosen)
    tiles = jnp.where(first_entry, 0, tiles)
    last_entry = (row_ids == 0) & (tile_ids == tile_count - 1) & (slot_ids == per_tile - 1)
    chosen = jnp.where(last_entry, per_tile - 1, chosen)
    tiles = jnp.where(last_entry, tile_count - 1, tiles)
    return (tiles * per_tile + chosen).reshape(row_count, tile_count * per_tile).astype(jnp.int32)


def steps_of(stream_key, extent, pieces, least, high):
    loudness = 1.0
    for dim, blocks in pieces:
        steps = jax.random.uniform(jax.random.fold_in(jax.random.fold_in(stream_key, 6), dim), (blocks,), jnp.float32, least / len(pieces), high / len(pieces))
        loudness = loudness * jnp.repeat(jnp.exp(steps), extent[dim] // blocks).reshape((-1,) + (1,) * (len(extent) - 1 - dim))
    return loudness


def setup_inputs(seed: int = 0, part: int = 0) -> dict:
    keys = jax.random.split(jax.random.key(seed), 4)
    part_keys = jax.random.split(jax.random.fold_in(keys[3], part), 4)
    acquired = jnp.clip(jnp.exp(math.log(5.0) - 3.2227897 * jax.random.uniform(part_keys[0], (ZV, NX, NY), jnp.float32) ** steps_of(part_keys[0], (ZV, NX, NY), ((0, 4), (1, 4)), -0.2, 0.2)), 0.19921875, 5.0).astype(jnp.bfloat16)
    psf_taps = jnp.clip(jnp.exp(jax.random.uniform(keys[1], (2, 3, TAPS), jnp.float32, math.log(0.1), math.log(1.0))), 0.1, 1.0)
    block_source = draw_block_source(jax.random.fold_in(jax.random.fold_in(keys[3], part), 71), part)
    return {"acquired": acquired, "psf_taps": psf_taps, "block_source": block_source}


def lower(volume):
    return lax.optimization_barrier(volume.astype(jnp.bfloat16)).astype(jnp.float32)


def correlate(volume, kernel, axis):
    reach = kernel.shape[0] // 2
    length = volume.shape[axis]
    widths = [(0, 0), (0, 0), (0, 0)]
    widths[axis] = (reach, reach)
    padded = jnp.pad(volume, widths)
    summed = jnp.zeros(volume.shape, jnp.float32)
    taps = kernel.astype(jnp.float32)
    for tap_index in range(kernel.shape[0]):
        summed = summed + taps[tap_index] * lax.slice_in_dim(padded, tap_index, tap_index + length, axis=axis)
    return summed


def blur(volume, kernels):
    first = lower(correlate(lower(volume), kernels[0], 1))
    second = lower(correlate(first, kernels[1], 2))
    return correlate(second, kernels[2], 0)


def pick_blocks(planes, sources):
    blocks = planes.reshape(planes.shape[0], sources.shape[0], BX, planes.shape[2])
    return jnp.take(blocks, sources, axis=1).reshape(planes.shape)


def reference(acquired, psf_taps, block_source):
    pair_count = N_VIEW // 2
    stacks = acquired.reshape(pair_count, 2, CZ, NX, NY)
    routes = block_source.reshape(pair_count, 2, NX // BX)
    measured = jax.vmap(jax.vmap(pick_blocks))(stacks, routes)
    measured = jnp.transpose(measured, (1, 0, 2, 3, 4)).reshape(2, NZ, NX, NY)
    view_zero = measured[0].astype(jnp.float32)
    view_one = measured[1].astype(jnp.float32)
    kernels = (psf_taps / jnp.sum(psf_taps, axis=2, keepdims=True)).astype(jnp.bfloat16)
    estimate = 0.5 * (view_zero + view_one)
    for iteration in range(ITERS):
        backs = []
        for view_index, observed in ((0, view_zero), (1, view_one)):
            blurred = blur(estimate, kernels[view_index])
            quotient = observed / blurred
            backs.append(blur(quotient, kernels[view_index][:, ::-1]))
        estimate = estimate * (0.5 * (backs[0] + backs[1]))
    return estimate
```

```python
import jax
import jax.numpy as jnp
from jax import lax
from jax.sharding import PartitionSpec as P

BX = 4
ITERS = 2


def shifted(block, axis, distance):
    devices = range(lax.axis_size(axis))
    route = [(i - distance, i) for i in devices if i - distance in devices]
    return lax.ppermute(block, axis, route)


def from_partner(block, axis, distance):
    count = lax.axis_size(axis)
    route = []
    for low in range(count):
        high = low | 1 << distance
        if high != low and high < count:
            route += [(low, high), (high, low)]
    return lax.ppermute(block, axis, route)


def extended_2(block, sides, width):
    for axis, dim in sides:
        count = lax.axis_size(axis)
        forward = [(i, i + 1) for i in range(count - 1)]
        backward = [(target, source) for source, target in forward]
        low = lax.ppermute(
            lax.slice_in_dim(block, block.shape[dim] - width, None, axis=dim), axis, forward
        )
        high = lax.ppermute(lax.slice_in_dim(block, 0, width, axis=dim), axis, backward)
        block = jnp.concatenate([low, block, high], axis=dim)
    return block


def band_matrix(kernel, row_count, col_count, base_shift):
    row_ids = lax.broadcasted_iota(jnp.int32, (row_count, col_count), 0)
    col_ids = lax.broadcasted_iota(jnp.int32, (row_count, col_count), 1)
    distance = row_ids - col_ids + base_shift
    taps = kernel.astype(jnp.float32)
    matrix = jnp.zeros((row_count, col_count), jnp.float32)
    for tap_index in range(kernel.shape[0]):
        matrix = matrix + jnp.where(distance == tap_index, taps[tap_index], jnp.float32(0.0))
    return matrix.astype(jnp.bfloat16)


def operators(kernels, plane_count, width_x, width_y):
    reach = kernels.shape[1] // 2
    along_x = band_matrix(kernels[0], width_x + 2 * reach, width_x, 0).T
    along_x = jnp.broadcast_to(along_x[None], (plane_count,) + along_x.shape)
    return lax.optimization_barrier((
        along_x,
        band_matrix(kernels[1], width_y, width_y, reach),
        band_matrix(kernels[2], plane_count + 2 * reach, plane_count, 0).T,
    ))


def along_z(volume, matrix, reach):
    below_rim = shifted(volume[volume.shape[0] - reach :], "view", 2)
    above_rim = shifted(volume[:reach], "view", -2)
    extended = jnp.concatenate([below_rim, volume, above_rim], axis=0)
    planes = extended.shape[0]
    flat = extended.reshape(planes, -1)
    out = jnp.dot(matrix, flat, preferred_element_type=jnp.float32)
    return out.reshape(volume.shape)


def separable(extended, matrices, reach):
    width_y = extended.shape[2]
    after_x = jnp.einsum(
        "zpa,zay->zpy", matrices[0], extended, preferred_element_type=jnp.float32
    ).astype(jnp.bfloat16)
    after_y = jnp.dot(after_x.reshape(-1, width_y), matrices[1], preferred_element_type=jnp.float32)
    after_y = after_y.reshape(after_x.shape).astype(jnp.bfloat16)
    return along_z(after_y, matrices[2], reach)


def local(acquired, psf_taps, block_source):
    planes, width_x, width_y = acquired.shape
    block_count = width_x // BX
    capacity = block_count // 2
    reach = psf_taps.shape[2] // 2
    tile_index = lax.axis_index("tile")
    tile_total = lax.axis_size("tile")
    view_bit = lax.axis_index("view") % 2
    sources = block_source[0]
    blocks = acquired.reshape(planes, block_count, BX, width_y)
    wanted_here = lax.dynamic_slice_in_dim(sources, tile_index * block_count, block_count)
    source_tiles = wanted_here // block_count
    source_blocks = wanted_here % block_count
    parcels = []
    for offset in (1, -1):
        target = jnp.clip(tile_index + offset, 0, tile_total - 1)
        wanted = lax.dynamic_slice_in_dim(sources, target * block_count, block_count)
        matches = wanted // block_count == tile_index
        ranks = jnp.cumsum(matches.astype(jnp.int32)) - 1
        slot_ids = jnp.arange(capacity, dtype=jnp.int32)
        selected = jnp.where(
            matches[None, :] & (ranks[None, :] == slot_ids[:, None]),
            wanted[None, :] % block_count,
            0,
        )
        picked = jnp.sum(selected, axis=1)
        parcel = jnp.take(blocks, picked, axis=1)
        parcels.append(shifted(parcel, "tile", offset))
    candidates = jnp.concatenate([blocks, parcels[0], parcels[1]], axis=1)
    from_left = source_tiles == tile_index - 1
    from_right = source_tiles == tile_index + 1
    left_order = jnp.cumsum(from_left.astype(jnp.int32)) - 1
    right_order = jnp.cumsum(from_right.astype(jnp.int32)) - 1
    chosen = jnp.where(
        from_left,
        block_count + left_order,
        jnp.where(from_right, block_count + capacity + right_order, source_blocks),
    )
    measured = jnp.take(candidates, chosen, axis=1).reshape(planes, width_x, width_y)
    partner_view = from_partner(measured, "view", 0)
    measured_own = measured.astype(jnp.float32)
    estimate = 0.5 * (measured_own + partner_view.astype(jnp.float32))
    kernels = (psf_taps / jnp.sum(psf_taps, axis=2, keepdims=True)).astype(jnp.bfloat16)
    own_kernels = lax.dynamic_index_in_dim(kernels, view_bit, 0, keepdims=False)
    forward_ops = operators(own_kernels, planes, width_x, width_y)
    adjoint_ops = operators(own_kernels[:, ::-1], planes, width_x, width_y)
    half_rows = planes // 2
    for iteration in range(ITERS):
        estimate_low = estimate.astype(jnp.bfloat16)
        own_half = lax.dynamic_slice_in_dim(estimate_low, view_bit * half_rows, half_rows, 0)
        widened = extended_2(own_half, (("tile", 1),), reach)
        rim_stack = jnp.concatenate([widened[:, :reach], widened[:, reach + width_x :]], axis=1)
        partner_rims = from_partner(rim_stack, "view", 0)
        all_rims = jnp.where(
            view_bit == 0,
            jnp.concatenate([rim_stack, partner_rims], axis=0),
            jnp.concatenate([partner_rims, rim_stack], axis=0),
        )
        extended = jnp.concatenate([all_rims[:, :reach], estimate_low, all_rims[:, reach:]], axis=1)
        blurred = separable(extended, forward_ops, reach)
        quotient = (measured_own / blurred).astype(jnp.bfloat16)
        widened_quotient = extended_2(quotient, (("tile", 1),), reach)
        back_own = separable(widened_quotient, adjoint_ops, reach)
        back_partner = from_partner(back_own, "view", 0)
        estimate = estimate * (0.5 * (back_own + back_partner))
    return lax.dynamic_slice_in_dim(estimate, view_bit * half_rows, half_rows, 0)


def solution(mesh):
    in_specs = (P(("timepoin", "view"), "tile", None), P(), P(("timepoin", "view"), None))
    out_specs = P(("timepoin", "view"), "tile", None)
    return jax.shard_map(local, mesh=mesh, in_specs=in_specs, out_specs=out_specs, check_vma=False)
```

```python
import jax
import jax.numpy as jnp
from jax import lax
from jax.sharding import PartitionSpec as P

BX = 4
ITERS = 2


def shifted(block, axis, distance):
    devices = range(lax.axis_size(axis))
    route = [(i - distance, i) for i in devices if i - distance in devices]
    return lax.ppermute(block, axis, route)


def from_partner(block, axis, distance):
    count = lax.axis_size(axis)
    route = []
    for low in range(count):
        high = low | 1 << distance
        if high != low and high < count:
            route += [(low, high), (high, low)]
    return lax.ppermute(block, axis, route)


def extended_2(block, sides, width):
    for axis, dim in sides:
        count = lax.axis_size(axis)
        forward = [(i, i + 1) for i in range(count - 1)]
        backward = [(target, source) for source, target in forward]
        low = lax.ppermute(
            lax.slice_in_dim(block, block.shape[dim] - width, None, axis=dim), axis, forward
        )
        high = lax.ppermute(lax.slice_in_dim(block, 0, width, axis=dim), axis, backward)
        block = jnp.concatenate([low, block, high], axis=dim)
    return block


def band_matrix(kernel, row_count, col_count, base_shift):
    row_ids = lax.broadcasted_iota(jnp.int32, (row_count, col_count, 1), 0)
    col_ids = lax.broadcasted_iota(jnp.int32, (row_count, col_count, 1), 1)
    tap_ids = lax.broadcasted_iota(jnp.int32, (1, 1, kernel.shape[0]), 2)
    hit = row_ids - col_ids + base_shift == tap_ids
    taps = kernel.astype(jnp.float32)[None, None, :]
    matrix = jnp.sum(jnp.where(hit, taps, jnp.float32(0.0)), axis=2)
    return matrix.astype(jnp.bfloat16)


def operators(kernels, plane_count, width_x, width_y):
    reach = kernels.shape[1] // 2
    along_x = band_matrix(kernels[0], width_x + 2 * reach, width_x, 0).T
    along_x = jnp.broadcast_to(along_x[None], (plane_count,) + along_x.shape)
    return lax.optimization_barrier((
        along_x,
        band_matrix(kernels[1], width_y, width_y, reach),
        band_matrix(kernels[2], plane_count + 2 * reach, plane_count, 0).T,
    ))


def along_z(volume, matrix, reach):
    below_rim = shifted(volume[volume.shape[0] - reach :], "view", 2)
    above_rim = shifted(volume[:reach], "view", -2)
    extended = jnp.concatenate([below_rim, volume, above_rim], axis=0)
    planes = extended.shape[0]
    flat = extended.reshape(planes, -1)
    out = jnp.dot(matrix, flat, preferred_element_type=jnp.float32)
    return out.reshape(volume.shape)


def separable(extended, matrices, reach):
    width_y = extended.shape[2]
    after_x = jnp.einsum(
        "zpa,zay->zpy", matrices[0], extended, preferred_element_type=jnp.float32
    ).astype(jnp.bfloat16)
    after_y = jnp.dot(after_x.reshape(-1, width_y), matrices[1], preferred_element_type=jnp.float32)
    after_y = after_y.reshape(after_x.shape).astype(jnp.bfloat16)
    return along_z(after_y, matrices[2], reach)


def local(acquired, psf_taps, block_source):
    planes, width_x, width_y = acquired.shape
    block_count = width_x // BX
    capacity = block_count // 2
    reach = psf_taps.shape[2] // 2
    tile_index = lax.axis_index("tile")
    tile_total = lax.axis_size("tile")
    view_bit = lax.axis_index("view") % 2
    sources = block_source[0]
    blocks = acquired.reshape(planes, block_count, BX, width_y)
    wanted_here = lax.dynamic_slice_in_dim(sources, tile_index * block_count, block_count)
    source_tiles = wanted_here // block_count
    source_blocks = wanted_here % block_count
    parcels = []
    for offset in (1, -1):
        target = jnp.clip(tile_index + offset, 0, tile_total - 1)
        wanted = lax.dynamic_slice_in_dim(sources, target * block_count, block_count)
        matches = wanted // block_count == tile_index
        ranks = jnp.cumsum(matches.astype(jnp.int32)) - 1
        slot_ids = jnp.arange(capacity, dtype=jnp.int32)
        selected = jnp.where(
            matches[None, :] & (ranks[None, :] == slot_ids[:, None]),
            wanted[None, :] % block_count,
            0,
        )
        picked = jnp.sum(selected, axis=1)
        parcel = jnp.take(blocks, picked, axis=1)
        parcels.append(shifted(parcel, "tile", offset))
    candidates = jnp.concatenate([blocks, parcels[0], parcels[1]], axis=1)
    from_left = source_tiles == tile_index - 1
    from_right = source_tiles == tile_index + 1
    left_order = jnp.cumsum(from_left.astype(jnp.int32)) - 1
    right_order = jnp.cumsum(from_right.astype(jnp.int32)) - 1
    chosen = jnp.where(
        from_left,
        block_count + left_order,
        jnp.where(from_right, block_count + capacity + right_order, source_blocks),
    )
    measured = jnp.take(candidates, chosen, axis=1).reshape(planes, width_x, width_y)
    partner_view = from_partner(measured, "view", 0)
    measured_own = measured.astype(jnp.float32)
    estimate = 0.5 * (measured_own + partner_view.astype(jnp.float32))
    kernels = (psf_taps / jnp.sum(psf_taps, axis=2, keepdims=True)).astype(jnp.bfloat16)
    own_kernels = lax.dynamic_index_in_dim(kernels, view_bit, 0, keepdims=False)
    forward_ops = operators(own_kernels, planes, width_x, width_y)
    adjoint_ops = operators(own_kernels[:, ::-1], planes, width_x, width_y)
    half_rows = planes // 2
    for iteration in range(ITERS):
        estimate_low = estimate.astype(jnp.bfloat16)
        own_half = lax.dynamic_slice_in_dim(estimate_low, view_bit * half_rows, half_rows, 0)
        widened = extended_2(own_half, (("tile", 1),), reach)
        rim_stack = jnp.concatenate([widened[:, :reach], widened[:, reach + width_x :]], axis=1)
        partner_rims = from_partner(rim_stack, "view", 0)
        all_rims = jnp.where(
            view_bit == 0,
            jnp.concatenate([rim_stack, partner_rims], axis=0),
            jnp.concatenate([partner_rims, rim_stack], axis=0),
        )
        extended = jnp.concatenate([all_rims[:, :reach], estimate_low, all_rims[:, reach:]], axis=1)
        blurred = separable(extended, forward_ops, reach)
        quotient = (measured_own / blurred).astype(jnp.bfloat16)
        widened_quotient = extended_2(quotient, (("tile", 1),), reach)
        back_own = separable(widened_quotient, adjoint_ops, reach)
        back_partner = from_partner(back_own, "view", 0)
        estimate = estimate * (0.5 * (back_own + back_partner))
    return lax.dynamic_slice_in_dim(estimate, view_bit * half_rows, half_rows, 0)


def solution(mesh):
    in_specs = (P(("timepoin", "view"), "tile", None), P(), P(("timepoin", "view"), None))
    out_specs = P(("timepoin", "view"), "tile", None)
    return jax.shard_map(local, mesh=mesh, in_specs=in_specs, out_specs=out_specs, check_vma=False)
```

```python
import jax
import jax.numpy as jnp
from jax import lax
from jax.sharding import PartitionSpec as P

BX = 4
ITERS = 2


def shifted(block, axis, distance):
    devices = range(lax.axis_size(axis))
    route = [(i - distance, i) for i in devices if i - distance in devices]
    return lax.ppermute(block, axis, route)


def from_partner(block, axis, distance):
    count = lax.axis_size(axis)
    route = []
    for low in range(count):
        high = low | 1 << distance
        if high != low and high < count:
            route += [(low, high), (high, low)]
    return lax.ppermute(block, axis, route)


def band_matrix(kernel, row_count, col_count, base_shift):
    row_ids = lax.broadcasted_iota(jnp.int32, (row_count, col_count, 1), 0)
    col_ids = lax.broadcasted_iota(jnp.int32, (row_count, col_count, 1), 1)
    tap_ids = lax.broadcasted_iota(jnp.int32, (1, 1, kernel.shape[0]), 2)
    hit = row_ids - col_ids + base_shift == tap_ids
    taps = kernel.astype(jnp.float32)[None, None, :]
    matrix = jnp.sum(jnp.where(hit, taps, jnp.float32(0.0)), axis=2)
    return matrix.astype(jnp.bfloat16)


def operators(kernels, x_planes, z_out, x_in, x_out, width_y):
    reach = kernels.shape[1] // 2
    along_x = band_matrix(kernels[0], x_in, x_out, 0).T
    along_x = jnp.broadcast_to(along_x[None], (x_planes,) + along_x.shape)
    return lax.optimization_barrier((
        along_x,
        band_matrix(kernels[1], width_y, width_y, reach),
        band_matrix(kernels[2], z_out + 2 * reach, z_out, 0).T,
    ))


def pass_xy(extended, matrices):
    width_y = extended.shape[2]
    after_x = jnp.einsum(
        "zpa,zay->zpy", matrices[0], extended, preferred_element_type=jnp.float32
    ).astype(jnp.bfloat16)
    after_y = jnp.dot(after_x.reshape(-1, width_y), matrices[1], preferred_element_type=jnp.float32)
    return after_y.reshape(after_x.shape).astype(jnp.bfloat16)


def pass_z(extended, matrix):
    planes = extended.shape[0]
    out = jnp.dot(matrix, extended.reshape(planes, -1), preferred_element_type=jnp.float32)
    return out.reshape((matrix.shape[0],) + extended.shape[1:])


def rims(block, axis, dim, width, distance):
    size = block.shape[dim]
    low = shifted(lax.slice_in_dim(block, size - width, size, axis=dim), axis, distance)
    high = shifted(lax.slice_in_dim(block, 0, width, axis=dim), axis, -distance)
    return low, high


def local(acquired, psf_taps, block_source):
    planes, width_x, width_y = acquired.shape
    block_count = width_x // BX
    capacity = block_count // 2
    reach = psf_taps.shape[2] // 2
    wide = 2 * reach
    tile_index = lax.axis_index("tile")
    tile_total = lax.axis_size("tile")
    view_index = lax.axis_index("view")
    view_total = lax.axis_size("view")
    view_bit = view_index % 2
    sources = block_source[0]
    blocks = acquired.reshape(planes, block_count, BX, width_y)
    wanted_here = lax.dynamic_slice_in_dim(sources, tile_index * block_count, block_count)
    source_tiles = wanted_here // block_count
    source_blocks = wanted_here % block_count
    parcels = []
    for offset in (1, -1):
        target = jnp.clip(tile_index + offset, 0, tile_total - 1)
        wanted = lax.dynamic_slice_in_dim(sources, target * block_count, block_count)
        matches = wanted // block_count == tile_index
        ranks = jnp.cumsum(matches.astype(jnp.int32)) - 1
        slot_ids = jnp.arange(capacity, dtype=jnp.int32)
        selected = jnp.where(
            matches[None, :] & (ranks[None, :] == slot_ids[:, None]),
            wanted[None, :] % block_count,
            0,
        )
        picked = jnp.sum(selected, axis=1)
        parcel = jnp.take(blocks, picked, axis=1)
        parcels.append(shifted(parcel, "tile", offset))
    candidates = jnp.concatenate([blocks, parcels[0], parcels[1]], axis=1)
    from_left = source_tiles == tile_index - 1
    from_right = source_tiles == tile_index + 1
    left_order = jnp.cumsum(from_left.astype(jnp.int32)) - 1
    right_order = jnp.cumsum(from_right.astype(jnp.int32)) - 1
    chosen = jnp.where(
        from_left,
        block_count + left_order,
        jnp.where(from_right, block_count + capacity + right_order, source_blocks),
    )
    measured = jnp.take(candidates, chosen, axis=1).reshape(planes, width_x, width_y)
    partner_view = from_partner(measured, "view", 0)
    measured_own = measured.astype(jnp.float32)
    estimate = 0.5 * (measured_own + partner_view.astype(jnp.float32))
    kernels = (psf_taps / jnp.sum(psf_taps, axis=2, keepdims=True)).astype(jnp.bfloat16)
    own_kernels = lax.dynamic_index_in_dim(kernels, view_bit, 0, keepdims=False)
    forward_ops = operators(
        own_kernels, planes, planes + wide, width_x + 2 * wide, width_x + wide, width_y
    )
    adjoint_ops = operators(
        own_kernels[:, ::-1], planes + wide, planes, width_x + wide, width_x, width_y
    )
    x_ids = tile_index * width_x + jnp.arange(-reach, width_x + reach)
    z_ids = (view_index // 2) * planes + jnp.arange(-reach, planes + reach)
    inside = (
        ((z_ids >= 0) & (z_ids < (view_total // 2) * planes))[:, None, None]
        & ((x_ids >= 0) & (x_ids < tile_total * width_x))[None, :, None]
    )
    measured_wide = None
    half_rows = planes // 2
    for iteration in range(ITERS):
        estimate_low = estimate.astype(jnp.bfloat16)
        if measured_wide is None:
            low, high = rims(jnp.stack([estimate_low, measured]), "tile", 2, wide, 1)
            est_x = jnp.concatenate([low[0], estimate_low, high[0]], axis=1)
            meas_x = jnp.concatenate([low[1][:, reach:], measured, high[1][:, :reach]], axis=1)
        else:
            low, high = rims(estimate_low, "tile", 1, wide, 1)
            est_x = jnp.concatenate([low, estimate_low, high], axis=1)
        after_xy = pass_xy(est_x, forward_ops)
        if measured_wide is None:
            below, above = rims(jnp.stack([after_xy, meas_x]), "view", 1, wide, 2)
            ext_z = jnp.concatenate([below[0], after_xy, above[0]], axis=0)
            measured_wide = jnp.concatenate(
                [below[1][reach:], meas_x, above[1][:reach]], axis=0
            ).astype(jnp.float32)
        else:
            below, above = rims(after_xy, "view", 0, wide, 2)
            ext_z = jnp.concatenate([below, after_xy, above], axis=0)
        blurred = pass_z(ext_z, forward_ops[2])
        quotient = jnp.where(inside, measured_wide / blurred, jnp.float32(0.0)).astype(jnp.bfloat16)
        back_own = pass_z(pass_xy(quotient, adjoint_ops), adjoint_ops[2])
        back_partner = from_partner(back_own, "view", 0)
        estimate = estimate * (0.5 * (back_own + back_partner))
    return lax.dynamic_slice_in_dim(estimate, view_bit * half_rows, half_rows, 0)


def solution(mesh):
    in_specs = (P(("timepoin", "view"), "tile", None), P(), P(("timepoin", "view"), None))
    out_specs = P(("timepoin", "view"), "tile", None)
    return jax.shard_map(local, mesh=mesh, in_specs=in_specs, out_specs=out_specs, check_vma=False)
```

```python
import jax
import jax.numpy as jnp
from jax import lax
from jax.sharding import PartitionSpec as P

BX = 4
ITERS = 2


def shifted(block, axis, distance):
    devices = range(lax.axis_size(axis))
    route = [(i - distance, i) for i in devices if i - distance in devices]
    return lax.ppermute(block, axis, route)


def from_partner(block, axis, distance):
    count = lax.axis_size(axis)
    route = []
    for low in range(count):
        high = low | 1 << distance
        if high != low and high < count:
            route += [(low, high), (high, low)]
    return lax.ppermute(block, axis, route)


def extended_2(block, sides, width):
    for axis, dim in sides:
        count = lax.axis_size(axis)
        forward = [(i, i + 1) for i in range(count - 1)]
        backward = [(target, source) for source, target in forward]
        low = lax.ppermute(
            lax.slice_in_dim(block, block.shape[dim] - width, None, axis=dim), axis, forward
        )
        high = lax.ppermute(lax.slice_in_dim(block, 0, width, axis=dim), axis, backward)
        block = jnp.concatenate([low, block, high], axis=dim)
    return block


def band_matrix(kernel, row_count, col_count, base_shift):
    row_ids = lax.broadcasted_iota(jnp.int32, (row_count, col_count, 1), 0)
    col_ids = lax.broadcasted_iota(jnp.int32, (row_count, col_count, 1), 1)
    tap_ids = lax.broadcasted_iota(jnp.int32, (1, 1, kernel.shape[0]), 2)
    hit = row_ids - col_ids + base_shift == tap_ids
    taps = kernel.astype(jnp.float32)[None, None, :]
    matrix = jnp.sum(jnp.where(hit, taps, jnp.float32(0.0)), axis=2)
    return matrix.astype(jnp.bfloat16)


def operators(kernels, plane_count, width_x, width_y):
    reach = kernels.shape[1] // 2
    along_x = band_matrix(kernels[0], width_x + 2 * reach, width_x, 0).T
    along_x = jnp.broadcast_to(along_x[None], (plane_count,) + along_x.shape)
    return lax.optimization_barrier((
        along_x,
        band_matrix(kernels[1], width_y, width_y, reach),
        band_matrix(kernels[2], plane_count + 2 * reach, plane_count, 0).T,
    ))


def z_rims(volume, reach):
    slabs = lax.axis_size("view") // 2
    slab = lax.axis_index("view") // 2
    planes = volume.shape[0]
    below = jnp.zeros((reach,) + volume.shape[1:], volume.dtype)
    above = below
    for phase in (0, 1):
        route = []
        for low in range(phase, slabs - 1, 2):
            for bit in (0, 1):
                route += [(2 * low + bit, 2 * low + 2 + bit), (2 * low + 2 + bit, 2 * low + bit)]
        if not route:
            continue
        is_lower = slab % 2 == phase
        start = jnp.where(is_lower, planes - reach, 0)
        payload = lax.dynamic_slice_in_dim(volume, start, reach, 0)
        got = lax.ppermute(payload, "view", route)
        below = jnp.where(is_lower, below, got)
        above = jnp.where(is_lower, got, above)
    return below, above


def along_z(volume, matrix, reach):
    below_rim, above_rim = z_rims(volume, reach)
    extended = jnp.concatenate([below_rim, volume, above_rim], axis=0)
    planes = extended.shape[0]
    flat = extended.reshape(planes, -1)
    out = jnp.dot(matrix, flat, preferred_element_type=jnp.float32)
    return out.reshape(volume.shape)


def separable(extended, matrices, reach):
    width_y = extended.shape[2]
    after_x = jnp.einsum(
        "zpa,zay->zpy", matrices[0], extended, preferred_element_type=jnp.float32
    ).astype(jnp.bfloat16)
    after_y = jnp.dot(after_x.reshape(-1, width_y), matrices[1], preferred_element_type=jnp.float32)
    after_y = after_y.reshape(after_x.shape).astype(jnp.bfloat16)
    return along_z(after_y, matrices[2], reach)


def local(acquired, psf_taps, block_source):
    planes, width_x, width_y = acquired.shape
    block_count = width_x // BX
    capacity = block_count // 2
    reach = psf_taps.shape[2] // 2
    tile_index = lax.axis_index("tile")
    tile_total = lax.axis_size("tile")
    view_bit = lax.axis_index("view") % 2
    sources = block_source[0]
    blocks = acquired.reshape(planes, block_count, BX, width_y)
    wanted_here = lax.dynamic_slice_in_dim(sources, tile_index * block_count, block_count)
    source_tiles = wanted_here // block_count
    source_blocks = wanted_here % block_count
    parcels = []
    for offset in (1, -1):
        target = jnp.clip(tile_index + offset, 0, tile_total - 1)
        wanted = lax.dynamic_slice_in_dim(sources, target * block_count, block_count)
        matches = wanted // block_count == tile_index
        ranks = jnp.cumsum(matches.astype(jnp.int32)) - 1
        slot_ids = jnp.arange(capacity, dtype=jnp.int32)
        selected = jnp.where(
            matches[None, :] & (ranks[None, :] == slot_ids[:, None]),
            wanted[None, :] % block_count,
            0,
        )
        picked = jnp.sum(selected, axis=1)
        parcel = jnp.take(blocks, picked, axis=1)
        parcels.append(shifted(parcel, "tile", offset))
    candidates = jnp.concatenate([blocks, parcels[0], parcels[1]], axis=1)
    from_left = source_tiles == tile_index - 1
    from_right = source_tiles == tile_index + 1
    left_order = jnp.cumsum(from_left.astype(jnp.int32)) - 1
    right_order = jnp.cumsum(from_right.astype(jnp.int32)) - 1
    chosen = jnp.where(
        from_left,
        block_count + left_order,
        jnp.where(from_right, block_count + capacity + right_order, source_blocks),
    )
    measured = jnp.take(candidates, chosen, axis=1).reshape(planes, width_x, width_y)
    partner_view = from_partner(measured, "view", 0)
    measured_own = measured.astype(jnp.float32)
    estimate = 0.5 * (measured_own + partner_view.astype(jnp.float32))
    kernels = (psf_taps / jnp.sum(psf_taps, axis=2, keepdims=True)).astype(jnp.bfloat16)
    own_kernels = lax.dynamic_index_in_dim(kernels, view_bit, 0, keepdims=False)
    forward_ops = operators(own_kernels, planes, width_x, width_y)
    adjoint_ops = operators(own_kernels[:, ::-1], planes, width_x, width_y)
    half_rows = planes // 2
    for iteration in range(ITERS):
        estimate_low = estimate.astype(jnp.bfloat16)
        own_half = lax.dynamic_slice_in_dim(estimate_low, view_bit * half_rows, half_rows, 0)
        widened = extended_2(own_half, (("tile", 1),), reach)
        rim_stack = jnp.concatenate([widened[:, :reach], widened[:, reach + width_x :]], axis=1)
        partner_rims = from_partner(rim_stack, "view", 0)
        all_rims = jnp.where(
            view_bit == 0,
            jnp.concatenate([rim_stack, partner_rims], axis=0),
            jnp.concatenate([partner_rims, rim_stack], axis=0),
        )
        extended = jnp.concatenate([all_rims[:, :reach], estimate_low, all_rims[:, reach:]], axis=1)
        blurred = separable(extended, forward_ops, reach)
        quotient = (measured_own / blurred).astype(jnp.bfloat16)
        widened_quotient = extended_2(quotient, (("tile", 1),), reach)
        back_own = separable(widened_quotient, adjoint_ops, reach)
        if iteration == ITERS - 1:
            partner_half = lax.dynamic_slice_in_dim(back_own, (1 - view_bit) * half_rows, half_rows, 0)
            own_half = lax.dynamic_slice_in_dim(back_own, view_bit * half_rows, half_rows, 0)
            back_partner = from_partner(partner_half, "view", 0)
            kept = lax.dynamic_slice_in_dim(estimate, view_bit * half_rows, half_rows, 0)
            return kept * (0.5 * (own_half + back_partner))
        back_partner = from_partner(back_own, "view", 0)
        estimate = estimate * (0.5 * (back_own + back_partner))


def solution(mesh):
    in_specs = (P(("timepoin", "view"), "tile", None), P(), P(("timepoin", "view"), None))
    out_specs = P(("timepoin", "view"), "tile", None)
    return jax.shard_map(local, mesh=mesh, in_specs=in_specs, out_specs=out_specs, check_vma=False)
```

```python
import jax
import jax.numpy as jnp
from jax import lax
from jax.sharding import PartitionSpec as P

BX = 4
ITERS = 2


def shifted(block, axis, distance):
    devices = range(lax.axis_size(axis))
    route = [(i - distance, i) for i in devices if i - distance in devices]
    return lax.ppermute(block, axis, route)


def from_partner(block, axis, distance):
    count = lax.axis_size(axis)
    route = []
    for low in range(count):
        high = low | 1 << distance
        if high != low and high < count:
            route += [(low, high), (high, low)]
    return lax.ppermute(block, axis, route)


def extended_2(block, sides, width):
    for axis, dim in sides:
        count = lax.axis_size(axis)
        forward = [(i, i + 1) for i in range(count - 1)]
        backward = [(target, source) for source, target in forward]
        low = lax.ppermute(
            lax.slice_in_dim(block, block.shape[dim] - width, None, axis=dim), axis, forward
        )
        high = lax.ppermute(lax.slice_in_dim(block, 0, width, axis=dim), axis, backward)
        block = jnp.concatenate([low, block, high], axis=dim)
    return block


def shared_x_rims(block, reach):
    tiles = lax.axis_size("tile")
    views = lax.axis_size("view")
    route = []
    for view in range(views):
        for left in range(view % 2, tiles - 1, 2):
            route += [(left * views + view, (left + 1) * views + view)]
            route += [((left + 1) * views + view, left * views + view)]
    is_left = lax.axis_index("tile") % 2 == lax.axis_index("view") % 2
    width = block.shape[1]
    start = jnp.where(is_left, width - reach, 0)
    payload = lax.dynamic_slice_in_dim(block, start, reach, 1)
    got = lax.ppermute(payload, ("tile", "view"), route)
    other = from_partner(got, "view", 0)
    low = jnp.where(is_left, other, got)
    high = jnp.where(is_left, got, other)
    return low, high


def band_matrix(kernel, row_count, col_count, base_shift):
    row_ids = lax.broadcasted_iota(jnp.int32, (row_count, col_count, 1), 0)
    col_ids = lax.broadcasted_iota(jnp.int32, (row_count, col_count, 1), 1)
    tap_ids = lax.broadcasted_iota(jnp.int32, (1, 1, kernel.shape[0]), 2)
    hit = row_ids - col_ids + base_shift == tap_ids
    taps = kernel.astype(jnp.float32)[None, None, :]
    matrix = jnp.sum(jnp.where(hit, taps, jnp.float32(0.0)), axis=2)
    return matrix.astype(jnp.bfloat16)


def operators(kernels, plane_count, width_x, width_y):
    reach = kernels.shape[1] // 2
    along_x = band_matrix(kernels[0], width_x + 2 * reach, width_x, 0).T
    along_x = jnp.broadcast_to(along_x[None], (plane_count,) + along_x.shape)
    return lax.optimization_barrier((
        along_x,
        band_matrix(kernels[1], width_y, width_y, reach),
        band_matrix(kernels[2], plane_count + 2 * reach, plane_count, 0).T,
    ))


def z_rims(volume, reach):
    slabs = lax.axis_size("view") // 2
    slab = lax.axis_index("view") // 2
    planes = volume.shape[0]
    below = jnp.zeros((reach,) + volume.shape[1:], volume.dtype)
    above = below
    for phase in (0, 1):
        route = []
        for low in range(phase, slabs - 1, 2):
            for bit in (0, 1):
                route += [(2 * low + bit, 2 * low + 2 + bit), (2 * low + 2 + bit, 2 * low + bit)]
        if not route:
            continue
        is_lower = slab % 2 == phase
        start = jnp.where(is_lower, planes - reach, 0)
        payload = lax.dynamic_slice_in_dim(volume, start, reach, 0)
        got = lax.ppermute(payload, "view", route)
        below = jnp.where(is_lower, below, got)
        above = jnp.where(is_lower, got, above)
    return below, above


def along_z(volume, matrix, reach):
    below_rim, above_rim = z_rims(volume, reach)
    extended = jnp.concatenate([below_rim, volume, above_rim], axis=0)
    planes = extended.shape[0]
    flat = extended.reshape(planes, -1)
    out = jnp.dot(matrix, flat, preferred_element_type=jnp.float32)
    return out.reshape(volume.shape)


def separable(extended, matrices, reach):
    width_y = extended.shape[2]
    after_x = jnp.einsum(
        "zpa,zay->zpy", matrices[0], extended, preferred_element_type=jnp.float32
    ).astype(jnp.bfloat16)
    after_y = jnp.dot(after_x.reshape(-1, width_y), matrices[1], preferred_element_type=jnp.float32)
    after_y = after_y.reshape(after_x.shape).astype(jnp.bfloat16)
    return along_z(after_y, matrices[2], reach)


def local(acquired, psf_taps, block_source):
    planes, width_x, width_y = acquired.shape
    block_count = width_x // BX
    capacity = block_count // 2
    reach = psf_taps.shape[2] // 2
    tile_index = lax.axis_index("tile")
    tile_total = lax.axis_size("tile")
    view_bit = lax.axis_index("view") % 2
    sources = block_source[0]
    blocks = acquired.reshape(planes, block_count, BX, width_y)
    wanted_here = lax.dynamic_slice_in_dim(sources, tile_index * block_count, block_count)
    source_tiles = wanted_here // block_count
    source_blocks = wanted_here % block_count
    parcels = []
    for offset in (1, -1):
        target = jnp.clip(tile_index + offset, 0, tile_total - 1)
        wanted = lax.dynamic_slice_in_dim(sources, target * block_count, block_count)
        matches = wanted // block_count == tile_index
        ranks = jnp.cumsum(matches.astype(jnp.int32)) - 1
        slot_ids = jnp.arange(capacity, dtype=jnp.int32)
        selected = jnp.where(
            matches[None, :] & (ranks[None, :] == slot_ids[:, None]),
            wanted[None, :] % block_count,
            0,
        )
        picked = jnp.sum(selected, axis=1)
        parcel = jnp.take(blocks, picked, axis=1)
        parcels.append(shifted(parcel, "tile", offset))
    candidates = jnp.concatenate([blocks, parcels[0], parcels[1]], axis=1)
    from_left = source_tiles == tile_index - 1
    from_right = source_tiles == tile_index + 1
    left_order = jnp.cumsum(from_left.astype(jnp.int32)) - 1
    right_order = jnp.cumsum(from_right.astype(jnp.int32)) - 1
    chosen = jnp.where(
        from_left,
        block_count + left_order,
        jnp.where(from_right, block_count + capacity + right_order, source_blocks),
    )
    measured = jnp.take(candidates, chosen, axis=1).reshape(planes, width_x, width_y)
    partner_view = from_partner(measured, "view", 0)
    measured_own = measured.astype(jnp.float32)
    estimate = 0.5 * (measured_own + partner_view.astype(jnp.float32))
    kernels = (psf_taps / jnp.sum(psf_taps, axis=2, keepdims=True)).astype(jnp.bfloat16)
    own_kernels = lax.dynamic_index_in_dim(kernels, view_bit, 0, keepdims=False)
    forward_ops = operators(own_kernels, planes, width_x, width_y)
    adjoint_ops = operators(own_kernels[:, ::-1], planes, width_x, width_y)
    half_rows = planes // 2
    for iteration in range(ITERS):
        estimate_low = estimate.astype(jnp.bfloat16)
        low, high = shared_x_rims(estimate_low, reach)
        extended = jnp.concatenate([low, estimate_low, high], axis=1)
        blurred = separable(extended, forward_ops, reach)
        quotient = (measured_own / blurred).astype(jnp.bfloat16)
        widened_quotient = extended_2(quotient, (("tile", 1),), reach)
        back_own = separable(widened_quotient, adjoint_ops, reach)
        if iteration == ITERS - 1:
            partner_half = lax.dynamic_slice_in_dim(back_own, (1 - view_bit) * half_rows, half_rows, 0)
            own_half = lax.dynamic_slice_in_dim(back_own, view_bit * half_rows, half_rows, 0)
            back_partner = from_partner(partner_half, "view", 0)
            kept = lax.dynamic_slice_in_dim(estimate, view_bit * half_rows, half_rows, 0)
            return kept * (0.5 * (own_half + back_partner))
        back_partner = from_partner(back_own, "view", 0)
        estimate = estimate * (0.5 * (back_own + back_partner))


def solution(mesh):
    in_specs = (P(("timepoin", "view"), "tile", None), P(), P(("timepoin", "view"), None))
    out_specs = P(("timepoin", "view"), "tile", None)
    return jax.shard_map(local, mesh=mesh, in_specs=in_specs, out_specs=out_specs, check_vma=False)
```

```python
import jax
import jax.numpy as jnp
from jax import lax
from jax.sharding import PartitionSpec as P

BX = 4
ITERS = 2


def shifted(block, axis, distance):
    devices = range(lax.axis_size(axis))
    route = [(i - distance, i) for i in devices if i - distance in devices]
    return lax.ppermute(block, axis, route)


def from_partner(block, axis, distance):
    count = lax.axis_size(axis)
    route = []
    for low in range(count):
        high = low | 1 << distance
        if high != low and high < count:
            route += [(low, high), (high, low)]
    return lax.ppermute(block, axis, route)


def extended_2(block, sides, width):
    for axis, dim in sides:
        count = lax.axis_size(axis)
        forward = [(i, i + 1) for i in range(count - 1)]
        backward = [(target, source) for source, target in forward]
        low = lax.ppermute(
            lax.slice_in_dim(block, block.shape[dim] - width, None, axis=dim), axis, forward
        )
        high = lax.ppermute(lax.slice_in_dim(block, 0, width, axis=dim), axis, backward)
        block = jnp.concatenate([low, block, high], axis=dim)
    return block


def band_matrix(kernel, row_count, col_count, base_shift):
    row_ids = lax.broadcasted_iota(jnp.int32, (row_count, col_count, 1), 0)
    col_ids = lax.broadcasted_iota(jnp.int32, (row_count, col_count, 1), 1)
    tap_ids = lax.broadcasted_iota(jnp.int32, (1, 1, kernel.shape[0]), 2)
    hit = row_ids - col_ids + base_shift == tap_ids
    taps = kernel.astype(jnp.float32)[None, None, :]
    matrix = jnp.sum(jnp.where(hit, taps, jnp.float32(0.0)), axis=2)
    return matrix.astype(jnp.bfloat16)


def operators(kernels, plane_count, width_x, width_y):
    reach = kernels.shape[1] // 2
    along_x = band_matrix(kernels[0], width_x + 2 * reach, width_x, 0).T
    along_x = jnp.broadcast_to(along_x[None], (plane_count,) + along_x.shape)
    return lax.optimization_barrier((
        along_x,
        band_matrix(kernels[1], width_y, width_y, reach),
        band_matrix(kernels[2], plane_count + 2 * reach, plane_count, 0).T,
    ))


def pass_xy(extended, matrices):
    width_y = extended.shape[2]
    after_x = jnp.einsum(
        "zpa,zay->zpy", matrices[0], extended, preferred_element_type=jnp.float32
    ).astype(jnp.bfloat16)
    after_y = jnp.dot(after_x.reshape(-1, width_y), matrices[1], preferred_element_type=jnp.float32)
    return after_y.reshape(after_x.shape).astype(jnp.bfloat16)


def pass_z(extended, matrix):
    planes = extended.shape[0]
    out = jnp.dot(matrix, extended.reshape(planes, -1), preferred_element_type=jnp.float32)
    return out.reshape((matrix.shape[0],) + extended.shape[1:])


def z_rims(volume, reach, axis):
    slabs = lax.axis_size("view") // 2
    slab = lax.axis_index("view") // 2
    planes = volume.shape[axis]
    shape = list(volume.shape)
    shape[axis] = reach
    below = jnp.zeros(shape, volume.dtype)
    above = below
    for phase in (0, 1):
        route = []
        for low in range(phase, slabs - 1, 2):
            for bit in (0, 1):
                route += [(2 * low + bit, 2 * low + 2 + bit), (2 * low + 2 + bit, 2 * low + bit)]
        if not route:
            continue
        is_lower = slab % 2 == phase
        start = jnp.where(is_lower, planes - reach, 0)
        payload = lax.dynamic_slice_in_dim(volume, start, reach, axis)
        got = lax.ppermute(payload, "view", route)
        below = jnp.where(is_lower, below, got)
        above = jnp.where(is_lower, got, above)
    return below, above


def x_rims(block, reach, axis):
    tiles = lax.axis_size("tile")
    views = lax.axis_size("view")
    route = []
    for tile in range(tiles - 1):
        for slab in range(views // 2):
            right_core = tile * views + 2 * slab + 1
            left_core = (tile + 1) * views + 2 * slab
            route += [(right_core, left_core), (left_core, right_core)]
    first = lax.axis_index("view") % 2 == 0
    width = block.shape[axis]
    outward = lax.dynamic_slice_in_dim(block, jnp.where(first, 0, width - reach), reach, axis)
    inward = lax.dynamic_slice_in_dim(block, jnp.where(first, width - reach, 0), reach, axis)
    across = lax.ppermute(outward, ("tile", "view"), route)
    beside = from_partner(inward, "view", 0)
    low = jnp.where(first, across, beside)
    high = jnp.where(first, beside, across)
    return low, high


def local(acquired, psf_taps, block_source):
    planes, width_x, width_y = acquired.shape
    block_count = width_x // BX
    capacity = block_count // 2
    reach = psf_taps.shape[2] // 2
    tile_index = lax.axis_index("tile")
    tile_total = lax.axis_size("tile")
    view_bit = lax.axis_index("view") % 2
    sources = block_source[0]
    blocks = acquired.reshape(planes, block_count, BX, width_y)
    wanted_here = lax.dynamic_slice_in_dim(sources, tile_index * block_count, block_count)
    source_tiles = wanted_here // block_count
    source_blocks = wanted_here % block_count
    parcels = []
    for offset in (1, -1):
        target = jnp.clip(tile_index + offset, 0, tile_total - 1)
        wanted = lax.dynamic_slice_in_dim(sources, target * block_count, block_count)
        matches = wanted // block_count == tile_index
        ranks = jnp.cumsum(matches.astype(jnp.int32)) - 1
        slot_ids = jnp.arange(capacity, dtype=jnp.int32)
        selected = jnp.where(
            matches[None, :] & (ranks[None, :] == slot_ids[:, None]),
            wanted[None, :] % block_count,
            0,
        )
        picked = jnp.sum(selected, axis=1)
        parcel = jnp.take(blocks, picked, axis=1)
        parcels.append(shifted(parcel, "tile", offset))
    candidates = jnp.concatenate([blocks, parcels[0], parcels[1]], axis=1)
    from_left = source_tiles == tile_index - 1
    from_right = source_tiles == tile_index + 1
    left_order = jnp.cumsum(from_left.astype(jnp.int32)) - 1
    right_order = jnp.cumsum(from_right.astype(jnp.int32)) - 1
    chosen = jnp.where(
        from_left,
        block_count + left_order,
        jnp.where(from_right, block_count + capacity + right_order, source_blocks),
    )
    measured = jnp.take(candidates, chosen, axis=1).reshape(planes, width_x, width_y)
    half_x = width_x // 2
    half_rows = planes // 2
    own_x = lax.dynamic_slice_in_dim(measured, view_bit * half_x, half_x, 1)
    give_x = lax.dynamic_slice_in_dim(measured, (1 - view_bit) * half_x, half_x, 1)
    got_x = from_partner(give_x, "view", 0)
    views_measured = jnp.where(view_bit == 0, jnp.stack([own_x, got_x]), jnp.stack([got_x, own_x]))
    observed = views_measured.astype(jnp.float32)
    estimate = 0.5 * (observed[0] + observed[1])
    kernels = (psf_taps / jnp.sum(psf_taps, axis=2, keepdims=True)).astype(jnp.bfloat16)
    view_count = kernels.shape[0]
    forward_ops = [operators(kernels[v], planes, half_x, width_y) for v in range(view_count)]
    adjoint_ops = [operators(kernels[v][:, ::-1], planes, half_x, width_y) for v in range(view_count)]
    for iteration in range(ITERS):
        estimate_low = estimate.astype(jnp.bfloat16)
        low, high = x_rims(estimate_low, reach, 1)
        extended = jnp.concatenate([low, estimate_low, high], axis=1)
        after_xy = jnp.stack([pass_xy(extended, forward_ops[v]) for v in range(view_count)])
        below, above = z_rims(after_xy, reach, 1)
        quotients = []
        for v in range(view_count):
            widened = jnp.concatenate([below[v], after_xy[v], above[v]], axis=0)
            blurred = pass_z(widened, forward_ops[v][2])
            quotients.append((observed[v] / blurred).astype(jnp.bfloat16))
        quotients = jnp.stack(quotients)
        low, high = x_rims(quotients, reach, 2)
        after_xy = jnp.stack([
            pass_xy(jnp.concatenate([low[v], quotients[v], high[v]], axis=1), adjoint_ops[v])
            for v in range(view_count)
        ])
        below, above = z_rims(after_xy, reach, 1)
        backs = [
            pass_z(jnp.concatenate([below[v], after_xy[v], above[v]], axis=0), adjoint_ops[v][2])
            for v in range(view_count)
        ]
        estimate = estimate * (0.5 * (backs[0] + backs[1]))
    keep = lax.dynamic_slice_in_dim(estimate, view_bit * half_rows, half_rows, 0)
    give = lax.dynamic_slice_in_dim(estimate, (1 - view_bit) * half_rows, half_rows, 0)
    got = from_partner(give, "view", 0)
    return jnp.where(
        view_bit == 0, jnp.concatenate([keep, got], axis=1), jnp.concatenate([got, keep], axis=1)
    )


def solution(mesh):
    in_specs = (P(("timepoin", "view"), "tile", None), P(), P(("timepoin", "view"), None))
    out_specs = P(("timepoin", "view"), "tile", None)
    return jax.shard_map(local, mesh=mesh, in_specs=in_specs, out_specs=out_specs, check_vma=False)
```

```python
import jax
import jax.numpy as jnp
from jax import lax
from jax.sharding import PartitionSpec as P

BX = 4
ITERS = 2


def shifted(block, axis, distance):
    devices = range(lax.axis_size(axis))
    route = [(i - distance, i) for i in devices if i - distance in devices]
    return lax.ppermute(block, axis, route)


def from_partner(block, axis, distance):
    count = lax.axis_size(axis)
    route = []
    for low in range(count):
        high = low | 1 << distance
        if high != low and high < count:
            route += [(low, high), (high, low)]
    return lax.ppermute(block, axis, route)


def extended_2(block, sides, width):
    for axis, dim in sides:
        count = lax.axis_size(axis)
        forward = [(i, i + 1) for i in range(count - 1)]
        backward = [(target, source) for source, target in forward]
        low = lax.ppermute(
            lax.slice_in_dim(block, block.shape[dim] - width, None, axis=dim), axis, forward
        )
        high = lax.ppermute(lax.slice_in_dim(block, 0, width, axis=dim), axis, backward)
        block = jnp.concatenate([low, block, high], axis=dim)
    return block


def band_matrix(kernel, row_count, col_count, base_shift):
    row_ids = lax.broadcasted_iota(jnp.int32, (row_count, col_count, 1), 0)
    col_ids = lax.broadcasted_iota(jnp.int32, (row_count, col_count, 1), 1)
    tap_ids = lax.broadcasted_iota(jnp.int32, (1, 1, kernel.shape[0]), 2)
    hit = row_ids - col_ids + base_shift == tap_ids
    taps = kernel.astype(jnp.float32)[None, None, :]
    matrix = jnp.sum(jnp.where(hit, taps, jnp.float32(0.0)), axis=2)
    return matrix.astype(jnp.bfloat16)


def operators(kernels, plane_count, width_x, width_y):
    reach = kernels.shape[1] // 2
    along_x = band_matrix(kernels[0], width_x + 2 * reach, width_x, 0).T
    along_x = jnp.broadcast_to(along_x[None], (plane_count,) + along_x.shape)
    return lax.optimization_barrier((
        along_x,
        band_matrix(kernels[1], width_y, width_y, reach),
        band_matrix(kernels[2], plane_count + 2 * reach, plane_count, 0).T,
    ))


def pass_xy(extended, matrices):
    width_y = extended.shape[2]
    after_x = jnp.einsum(
        "zpa,zay->zpy", matrices[0], extended, preferred_element_type=jnp.float32
    ).astype(jnp.bfloat16)
    after_y = jnp.dot(after_x.reshape(-1, width_y), matrices[1], preferred_element_type=jnp.float32)
    return after_y.reshape(after_x.shape).astype(jnp.bfloat16)


def pass_z(extended, matrix):
    planes = extended.shape[0]
    out = jnp.dot(matrix, extended.reshape(planes, -1), preferred_element_type=jnp.float32)
    return out.reshape((matrix.shape[0],) + extended.shape[1:])


def stacked_operators(kernels, plane_count, width_x, width_y):
    reach = kernels.shape[2] // 2
    views = range(kernels.shape[0])
    along_x = jnp.stack([band_matrix(kernels[v, 0], width_x + 2 * reach, width_x, 0).T for v in views])
    along_x = jnp.broadcast_to(along_x[:, None], (along_x.shape[0], plane_count) + along_x.shape[1:])
    return lax.optimization_barrier((
        along_x,
        jnp.stack([band_matrix(kernels[v, 1], width_y, width_y, reach) for v in views]),
        jnp.stack([band_matrix(kernels[v, 2], plane_count + 2 * reach, plane_count, 0).T for v in views]),
    ))


def pass_y_views(after_x, matrices):
    shape = after_x.shape
    flat = after_x.reshape(shape[0], -1, shape[-1])
    after_y = jnp.einsum("vmy,vyq->vmq", flat, matrices, preferred_element_type=jnp.float32)
    return after_y.reshape(shape).astype(jnp.bfloat16)


def pass_z_views(after_y, matrices, reach):
    below, above = z_rims(after_y, reach, 1)
    widened = jnp.concatenate([below, after_y, above], axis=1)
    shape = widened.shape
    flat = widened.reshape(shape[0], shape[1], -1)
    out = jnp.einsum("vpa,vam->vpm", matrices, flat, preferred_element_type=jnp.float32)
    return out.reshape((shape[0], matrices.shape[1]) + shape[2:])


def z_rims(volume, reach, axis):
    slabs = lax.axis_size("view") // 2
    slab = lax.axis_index("view") // 2
    planes = volume.shape[axis]
    shape = list(volume.shape)
    shape[axis] = reach
    below = jnp.zeros(shape, volume.dtype)
    above = below
    for phase in (0, 1):
        route = []
        for low in range(phase, slabs - 1, 2):
            for bit in (0, 1):
                route += [(2 * low + bit, 2 * low + 2 + bit), (2 * low + 2 + bit, 2 * low + bit)]
        if not route:
            continue
        is_lower = slab % 2 == phase
        start = jnp.where(is_lower, planes - reach, 0)
        payload = lax.dynamic_slice_in_dim(volume, start, reach, axis)
        got = lax.ppermute(payload, "view", route)
        below = jnp.where(is_lower, below, got)
        above = jnp.where(is_lower, got, above)
    return below, above


def x_rims(block, reach, axis):
    tiles = lax.axis_size("tile")
    views = lax.axis_size("view")
    route = []
    for tile in range(tiles - 1):
        for slab in range(views // 2):
            right_core = tile * views + 2 * slab + 1
            left_core = (tile + 1) * views + 2 * slab
            route += [(right_core, left_core), (left_core, right_core)]
    first = lax.axis_index("view") % 2 == 0
    width = block.shape[axis]
    outward = lax.dynamic_slice_in_dim(block, jnp.where(first, 0, width - reach), reach, axis)
    inward = lax.dynamic_slice_in_dim(block, jnp.where(first, width - reach, 0), reach, axis)
    across = lax.ppermute(outward, ("tile", "view"), route)
    beside = from_partner(inward, "view", 0)
    low = jnp.where(first, across, beside)
    high = jnp.where(first, beside, across)
    return low, high


def local(acquired, psf_taps, block_source):
    planes, width_x, width_y = acquired.shape
    block_count = width_x // BX
    capacity = block_count // 2
    reach = psf_taps.shape[2] // 2
    tile_index = lax.axis_index("tile")
    tile_total = lax.axis_size("tile")
    view_bit = lax.axis_index("view") % 2
    sources = block_source[0]
    blocks = acquired.reshape(planes, block_count, BX, width_y)
    wanted_here = lax.dynamic_slice_in_dim(sources, tile_index * block_count, block_count)
    source_tiles = wanted_here // block_count
    source_blocks = wanted_here % block_count
    parcels = []
    for offset in (1, -1):
        target = jnp.clip(tile_index + offset, 0, tile_total - 1)
        wanted = lax.dynamic_slice_in_dim(sources, target * block_count, block_count)
        matches = wanted // block_count == tile_index
        ranks = jnp.cumsum(matches.astype(jnp.int32)) - 1
        slot_ids = jnp.arange(capacity, dtype=jnp.int32)
        selected = jnp.where(
            matches[None, :] & (ranks[None, :] == slot_ids[:, None]),
            wanted[None, :] % block_count,
            0,
        )
        picked = jnp.sum(selected, axis=1)
        parcel = jnp.take(blocks, picked, axis=1)
        parcels.append(shifted(parcel, "tile", offset))
    candidates = jnp.concatenate([blocks, parcels[0], parcels[1]], axis=1)
    from_left = source_tiles == tile_index - 1
    from_right = source_tiles == tile_index + 1
    left_order = jnp.cumsum(from_left.astype(jnp.int32)) - 1
    right_order = jnp.cumsum(from_right.astype(jnp.int32)) - 1
    chosen = jnp.where(
        from_left,
        block_count + left_order,
        jnp.where(from_right, block_count + capacity + right_order, source_blocks),
    )
    measured = jnp.take(candidates, chosen, axis=1).reshape(planes, width_x, width_y)
    half_x = width_x // 2
    half_rows = planes // 2
    own_x = lax.dynamic_slice_in_dim(measured, view_bit * half_x, half_x, 1)
    give_x = lax.dynamic_slice_in_dim(measured, (1 - view_bit) * half_x, half_x, 1)
    got_x = from_partner(give_x, "view", 0)
    views_measured = jnp.where(view_bit == 0, jnp.stack([own_x, got_x]), jnp.stack([got_x, own_x]))
    observed = views_measured.astype(jnp.float32)
    estimate = 0.5 * (observed[0] + observed[1])
    kernels = (psf_taps / jnp.sum(psf_taps, axis=2, keepdims=True)).astype(jnp.bfloat16)
    view_count = kernels.shape[0]
    forward_ops = stacked_operators(kernels, planes, half_x, width_y)
    adjoint_ops = stacked_operators(kernels[:, :, ::-1], planes, half_x, width_y)
    for iteration in range(ITERS):
        estimate_low = estimate.astype(jnp.bfloat16)
        low, high = x_rims(estimate_low, reach, 1)
        extended = jnp.concatenate([low, estimate_low, high], axis=1)
        after_x = jnp.einsum(
            "vzpa,zay->vzpy", forward_ops[0], extended, preferred_element_type=jnp.float32
        ).astype(jnp.bfloat16)
        blurred = pass_z_views(pass_y_views(after_x, forward_ops[1]), forward_ops[2], reach)
        quotients = (observed / blurred).astype(jnp.bfloat16)
        low, high = x_rims(quotients, reach, 2)
        widened = jnp.concatenate([low, quotients, high], axis=2)
        after_x = jnp.einsum(
            "vzpa,vzay->vzpy", adjoint_ops[0], widened, preferred_element_type=jnp.float32
        ).astype(jnp.bfloat16)
        backs = pass_z_views(pass_y_views(after_x, adjoint_ops[1]), adjoint_ops[2], reach)
        estimate = estimate * (0.5 * (backs[0] + backs[1]))
    keep = lax.dynamic_slice_in_dim(estimate, view_bit * half_rows, half_rows, 0)
    give = lax.dynamic_slice_in_dim(estimate, (1 - view_bit) * half_rows, half_rows, 0)
    got = from_partner(give, "view", 0)
    return jnp.where(
        view_bit == 0, jnp.concatenate([keep, got], axis=1), jnp.concatenate([got, keep], axis=1)
    )


def solution(mesh):
    in_specs = (P(("timepoin", "view"), "tile", None), P(), P(("timepoin", "view"), None))
    out_specs = P(("timepoin", "view"), "tile", None)
    return jax.shard_map(local, mesh=mesh, in_specs=in_specs, out_specs=out_specs, check_vma=False)
```

```python
import jax
import jax.numpy as jnp
from jax import lax
from jax.sharding import PartitionSpec as P

BX = 4
ITERS = 2


def shifted(block, axis, distance):
    devices = range(lax.axis_size(axis))
    route = [(i - distance, i) for i in devices if i - distance in devices]
    return lax.ppermute(block, axis, route)


def from_partner(block, axis, distance):
    count = lax.axis_size(axis)
    route = []
    for low in range(count):
        high = low | 1 << distance
        if high != low and high < count:
            route += [(low, high), (high, low)]
    return lax.ppermute(block, axis, route)


def extended_2(block, sides, width):
    for axis, dim in sides:
        count = lax.axis_size(axis)
        forward = [(i, i + 1) for i in range(count - 1)]
        backward = [(target, source) for source, target in forward]
        low = lax.ppermute(
            lax.slice_in_dim(block, block.shape[dim] - width, None, axis=dim), axis, forward
        )
        high = lax.ppermute(lax.slice_in_dim(block, 0, width, axis=dim), axis, backward)
        block = jnp.concatenate([low, block, high], axis=dim)
    return block


def band_matrix(kernel, row_count, col_count, base_shift):
    row_ids = lax.broadcasted_iota(jnp.int32, (row_count, col_count, 1), 0)
    col_ids = lax.broadcasted_iota(jnp.int32, (row_count, col_count, 1), 1)
    tap_ids = lax.broadcasted_iota(jnp.int32, (1, 1, kernel.shape[0]), 2)
    hit = row_ids - col_ids + base_shift == tap_ids
    taps = kernel.astype(jnp.float32)[None, None, :]
    matrix = jnp.sum(jnp.where(hit, taps, jnp.float32(0.0)), axis=2)
    return matrix.astype(jnp.bfloat16)


def operators(kernels, plane_count, width_x, width_y):
    reach = kernels.shape[1] // 2
    along_x = band_matrix(kernels[0], width_x + 2 * reach, width_x, 0).T
    along_x = jnp.broadcast_to(along_x[None], (plane_count,) + along_x.shape)
    return lax.optimization_barrier((
        along_x,
        band_matrix(kernels[1], width_y, width_y, reach),
        band_matrix(kernels[2], plane_count + 2 * reach, plane_count, 0).T,
    ))


def pass_xy(extended, matrices):
    width_y = extended.shape[2]
    after_x = jnp.einsum(
        "zpa,zay->zpy", matrices[0], extended, preferred_element_type=jnp.float32
    ).astype(jnp.bfloat16)
    after_y = jnp.dot(after_x.reshape(-1, width_y), matrices[1], preferred_element_type=jnp.float32)
    return after_y.reshape(after_x.shape).astype(jnp.bfloat16)


def pass_z(extended, matrix):
    planes = extended.shape[0]
    out = jnp.dot(matrix, extended.reshape(planes, -1), preferred_element_type=jnp.float32)
    return out.reshape((matrix.shape[0],) + extended.shape[1:])


def stacked_operators(kernels, plane_count, width_x, width_y):
    reach = kernels.shape[2] // 2
    views = range(kernels.shape[0])
    along_x = jnp.stack([band_matrix(kernels[v, 0], width_x + 2 * reach, width_x, 0).T for v in views])
    along_x = jnp.broadcast_to(along_x[:, None], (along_x.shape[0], plane_count) + along_x.shape[1:])
    return lax.optimization_barrier((
        along_x,
        jnp.stack([band_matrix(kernels[v, 1], width_y, width_y, reach) for v in views]),
        jnp.stack([band_matrix(kernels[v, 2], plane_count + 2 * reach, plane_count, 0).T for v in views]),
    ))


def pass_y_views(after_x, matrices):
    shape = after_x.shape
    flat = after_x.reshape(shape[0], -1, shape[-1])
    after_y = jnp.einsum("vmy,vyq->vmq", flat, matrices, preferred_element_type=jnp.float32)
    return after_y.reshape(shape).astype(jnp.bfloat16)


def pass_z_views(after_y, matrices, reach):
    below, above = z_rims(after_y, reach, 1)
    widened = jnp.concatenate([below, after_y, above], axis=1)
    shape = widened.shape
    flat = widened.reshape(shape[0], shape[1], -1)
    out = jnp.einsum("vpa,vam->vpm", matrices, flat, preferred_element_type=jnp.float32)
    return out.reshape((shape[0], matrices.shape[1]) + shape[2:])


def z_rims(volume, reach, axis):
    slabs = lax.axis_size("view") // 2
    slab = lax.axis_index("view") // 2
    planes = volume.shape[axis]
    shape = list(volume.shape)
    shape[axis] = reach
    below = jnp.zeros(shape, volume.dtype)
    above = below
    for phase in (0, 1):
        route = []
        for low in range(phase, slabs - 1, 2):
            for bit in (0, 1):
                route += [(2 * low + bit, 2 * low + 2 + bit), (2 * low + 2 + bit, 2 * low + bit)]
        if not route:
            continue
        is_lower = slab % 2 == phase
        start = jnp.where(is_lower, planes - reach, 0)
        payload = lax.dynamic_slice_in_dim(volume, start, reach, axis)
        got = lax.ppermute(payload, "view", route)
        below = jnp.where(is_lower, below, got)
        above = jnp.where(is_lower, got, above)
    return below, above


def x_rims(block, reach, axis):
    tiles = lax.axis_size("tile")
    views = lax.axis_size("view")
    route = []
    for tile in range(tiles - 1):
        for slab in range(views // 2):
            right_core = tile * views + 2 * slab + 1
            left_core = (tile + 1) * views + 2 * slab
            route += [(right_core, left_core), (left_core, right_core)]
    first = lax.axis_index("view") % 2 == 0
    width = block.shape[axis]
    outward = lax.dynamic_slice_in_dim(block, jnp.where(first, 0, width - reach), reach, axis)
    inward = lax.dynamic_slice_in_dim(block, jnp.where(first, width - reach, 0), reach, axis)
    across = lax.ppermute(outward, ("tile", "view"), route)
    beside = from_partner(inward, "view", 0)
    low = jnp.where(first, across, beside)
    high = jnp.where(first, beside, across)
    return low, high


def local(acquired, psf_taps, block_source):
    planes, width_x, width_y = acquired.shape
    block_count = width_x // BX
    capacity = block_count // 2
    reach = psf_taps.shape[2] // 2
    tile_index = lax.axis_index("tile")
    tile_total = lax.axis_size("tile")
    view_bit = lax.axis_index("view") % 2
    sources = block_source[0]
    blocks = acquired.reshape(planes, block_count, BX, width_y)
    half_x = width_x // 2
    half_rows = planes // 2
    half_blocks = block_count // 2
    first = view_bit == 0
    starts = []
    for target, half in ((tile_index, 0), (tile_index, 1), (tile_index + 1, 0), (tile_index - 1, 1)):
        target = jnp.clip(target, 0, tile_total - 1)
        starts.append(target * block_count + half * half_blocks)
    slots = jnp.concatenate([lax.dynamic_slice_in_dim(sources, st, half_blocks) for st in starts])
    picked = jnp.take(blocks, slots % block_count, axis=1)
    mine = (slots // block_count == tile_index)[None, :, None, None]
    partials = jnp.where(mine, picked, jnp.zeros((), picked.dtype))
    partials = partials.reshape(planes, 4, half_x, width_y)
    own_keep = jnp.where(first, partials[:, 0], partials[:, 1])
    own_give = jnp.where(first, partials[:, 1], partials[:, 0])
    cross_keep = jnp.where(first, partials[:, 3], partials[:, 2])
    cross_pass = jnp.where(first, partials[:, 2], partials[:, 3])
    got = from_partner(jnp.stack([own_give, cross_pass]), "view", 0)
    tiles = lax.axis_size("tile")
    views = lax.axis_size("view")
    route = []
    for tile in range(tiles - 1):
        for slab in range(views // 2):
            right_core = tile * views + 2 * slab + 1
            left_core = (tile + 1) * views + 2 * slab
            route += [(right_core, left_core), (left_core, right_core)]
    outgoing = jnp.where(first, jnp.stack([cross_keep, got[1]]), jnp.stack([got[1], cross_keep]))
    incoming = lax.ppermute(outgoing, ("tile", "view"), route)
    own_parts = jnp.where(first, jnp.stack([own_keep, got[0]]), jnp.stack([got[0], own_keep]))
    views_measured = own_parts + incoming
    observed = views_measured.astype(jnp.float32)
    estimate = 0.5 * (observed[0] + observed[1])
    kernels = (psf_taps / jnp.sum(psf_taps, axis=2, keepdims=True)).astype(jnp.bfloat16)
    view_count = kernels.shape[0]
    forward_ops = stacked_operators(kernels, planes, half_x, width_y)
    adjoint_ops = stacked_operators(kernels[:, :, ::-1], planes, half_x, width_y)
    for iteration in range(ITERS):
        estimate_low = estimate.astype(jnp.bfloat16)
        low, high = x_rims(estimate_low, reach, 1)
        extended = jnp.concatenate([low, estimate_low, high], axis=1)
        after_x = jnp.einsum(
            "vzpa,zay->vzpy", forward_ops[0], extended, preferred_element_type=jnp.float32
        ).astype(jnp.bfloat16)
        blurred = pass_z_views(pass_y_views(after_x, forward_ops[1]), forward_ops[2], reach)
        quotients = (observed / blurred).astype(jnp.bfloat16)
        low, high = x_rims(quotients, reach, 2)
        widened = jnp.concatenate([low, quotients, high], axis=2)
        after_x = jnp.einsum(
            "vzpa,vzay->vzpy", adjoint_ops[0], widened, preferred_element_type=jnp.float32
        ).astype(jnp.bfloat16)
        backs = pass_z_views(pass_y_views(after_x, adjoint_ops[1]), adjoint_ops[2], reach)
        estimate = estimate * (0.5 * (backs[0] + backs[1]))
    keep = lax.dynamic_slice_in_dim(estimate, view_bit * half_rows, half_rows, 0)
    give = lax.dynamic_slice_in_dim(estimate, (1 - view_bit) * half_rows, half_rows, 0)
    got = from_partner(give, "view", 0)
    return jnp.where(
        view_bit == 0, jnp.concatenate([keep, got], axis=1), jnp.concatenate([got, keep], axis=1)
    )


def solution(mesh):
    in_specs = (P(("timepoin", "view"), "tile", None), P(), P(("timepoin", "view"), None))
    out_specs = P(("timepoin", "view"), "tile", None)
    return jax.shard_map(local, mesh=mesh, in_specs=in_specs, out_specs=out_specs, check_vma=False)
```

```python
import jax
import jax.numpy as jnp
from jax import lax
from jax.sharding import PartitionSpec as P

BX = 4
ITERS = 2


def shifted(block, axis, distance):
    devices = range(lax.axis_size(axis))
    route = [(i - distance, i) for i in devices if i - distance in devices]
    return lax.ppermute(block, axis, route)


def from_partner(block, axis, distance):
    count = lax.axis_size(axis)
    route = []
    for low in range(count):
        high = low | 1 << distance
        if high != low and high < count:
            route += [(low, high), (high, low)]
    return lax.ppermute(block, axis, route)


def extended_2(block, sides, width):
    for axis, dim in sides:
        count = lax.axis_size(axis)
        forward = [(i, i + 1) for i in range(count - 1)]
        backward = [(target, source) for source, target in forward]
        low = lax.ppermute(
            lax.slice_in_dim(block, block.shape[dim] - width, None, axis=dim), axis, forward
        )
        high = lax.ppermute(lax.slice_in_dim(block, 0, width, axis=dim), axis, backward)
        block = jnp.concatenate([low, block, high], axis=dim)
    return block


def band_matrix(kernel, row_count, col_count, base_shift):
    row_ids = lax.broadcasted_iota(jnp.int32, (row_count, col_count, 1), 0)
    col_ids = lax.broadcasted_iota(jnp.int32, (row_count, col_count, 1), 1)
    tap_ids = lax.broadcasted_iota(jnp.int32, (1, 1, kernel.shape[0]), 2)
    hit = row_ids - col_ids + base_shift == tap_ids
    taps = kernel.astype(jnp.float32)[None, None, :]
    matrix = jnp.sum(jnp.where(hit, taps, jnp.float32(0.0)), axis=2)
    return matrix.astype(jnp.bfloat16)


def operators(kernels, plane_count, width_x, width_y):
    reach = kernels.shape[1] // 2
    along_x = band_matrix(kernels[0], width_x + 2 * reach, width_x, 0).T
    along_x = jnp.broadcast_to(along_x[None], (plane_count,) + along_x.shape)
    return lax.optimization_barrier((
        along_x,
        band_matrix(kernels[1], width_y, width_y, reach),
        band_matrix(kernels[2], plane_count + 2 * reach, plane_count, 0).T,
    ))


def pass_xy(extended, matrices):
    width_y = extended.shape[2]
    after_x = jnp.einsum(
        "zpa,zay->zpy", matrices[0], extended, preferred_element_type=jnp.float32
    ).astype(jnp.bfloat16)
    after_y = jnp.dot(after_x.reshape(-1, width_y), matrices[1], preferred_element_type=jnp.float32)
    return after_y.reshape(after_x.shape).astype(jnp.bfloat16)


def pass_z(extended, matrix):
    planes = extended.shape[0]
    out = jnp.dot(matrix, extended.reshape(planes, -1), preferred_element_type=jnp.float32)
    return out.reshape((matrix.shape[0],) + extended.shape[1:])


def stacked_operators(kernels, plane_count, width_x, width_y):
    reach = kernels.shape[2] // 2
    views = range(kernels.shape[0])
    along_x = jnp.stack([band_matrix(kernels[v, 0], width_x + 2 * reach, width_x, 0).T for v in views])
    along_x = jnp.broadcast_to(along_x[:, None], (along_x.shape[0], plane_count) + along_x.shape[1:])
    return lax.optimization_barrier((
        along_x,
        jnp.stack([band_matrix(kernels[v, 1], width_y, width_y, reach) for v in views]),
        jnp.stack([band_matrix(kernels[v, 2], plane_count + 2 * reach, plane_count, 0).T for v in views]),
    ))


def pass_y_views(after_x, matrices):
    shape = after_x.shape
    flat = after_x.reshape(shape[0], -1, shape[-1])
    after_y = jnp.einsum("vmy,vyq->vmq", flat, matrices, preferred_element_type=jnp.float32)
    return after_y.reshape(shape).astype(jnp.bfloat16)


def pass_z_views(after_y, matrices, reach):
    below, above = z_rims(after_y, reach, 1)
    widened = jnp.concatenate([below, after_y, above], axis=1)
    return jnp.einsum("vpa,vaxy->vpxy", matrices, widened, preferred_element_type=jnp.float32)


def z_rims(volume, reach, axis):
    slabs = lax.axis_size("view") // 2
    slab = lax.axis_index("view") // 2
    planes = volume.shape[axis]
    shape = list(volume.shape)
    shape[axis] = reach
    below = jnp.zeros(shape, volume.dtype)
    above = below
    for phase in (0, 1):
        route = []
        for low in range(phase, slabs - 1, 2):
            for bit in (0, 1):
                route += [(2 * low + bit, 2 * low + 2 + bit), (2 * low + 2 + bit, 2 * low + bit)]
        if not route:
            continue
        is_lower = slab % 2 == phase
        start = jnp.where(is_lower, planes - reach, 0)
        payload = lax.dynamic_slice_in_dim(volume, start, reach, axis)
        got = lax.ppermute(payload, "view", route)
        below = jnp.where(is_lower, below, got)
        above = jnp.where(is_lower, got, above)
    return below, above


def x_rims(block, reach, axis):
    tiles = lax.axis_size("tile")
    views = lax.axis_size("view")
    route = []
    for tile in range(tiles - 1):
        for slab in range(views // 2):
            right_core = tile * views + 2 * slab + 1
            left_core = (tile + 1) * views + 2 * slab
            route += [(right_core, left_core), (left_core, right_core)]
    first = lax.axis_index("view") % 2 == 0
    width = block.shape[axis]
    outward = lax.dynamic_slice_in_dim(block, jnp.where(first, 0, width - reach), reach, axis)
    inward = lax.dynamic_slice_in_dim(block, jnp.where(first, width - reach, 0), reach, axis)
    across = lax.ppermute(outward, ("tile", "view"), route)
    beside = from_partner(inward, "view", 0)
    low = jnp.where(first, across, beside)
    high = jnp.where(first, beside, across)
    return low, high


def local(acquired, psf_taps, block_source):
    planes, width_x, width_y = acquired.shape
    block_count = width_x // BX
    capacity = block_count // 2
    reach = psf_taps.shape[2] // 2
    tile_index = lax.axis_index("tile")
    tile_total = lax.axis_size("tile")
    view_bit = lax.axis_index("view") % 2
    sources = block_source[0]
    blocks = acquired.reshape(planes, block_count, BX, width_y)
    half_x = width_x // 2
    half_rows = planes // 2
    half_blocks = block_count // 2
    first = view_bit == 0
    starts = []
    for target, half in ((tile_index, 0), (tile_index, 1), (tile_index + 1, 0), (tile_index - 1, 1)):
        target = jnp.clip(target, 0, tile_total - 1)
        starts.append(target * block_count + half * half_blocks)
    slots = jnp.concatenate([lax.dynamic_slice_in_dim(sources, st, half_blocks) for st in starts])
    picked = jnp.take(blocks, slots % block_count, axis=1)
    mine = (slots // block_count == tile_index)[None, :, None, None]
    partials = jnp.where(mine, picked, jnp.zeros((), picked.dtype))
    partials = partials.reshape(planes, 4, half_x, width_y)
    own_keep = jnp.where(first, partials[:, 0], partials[:, 1])
    own_give = jnp.where(first, partials[:, 1], partials[:, 0])
    cross_keep = jnp.where(first, partials[:, 3], partials[:, 2])
    cross_pass = jnp.where(first, partials[:, 2], partials[:, 3])
    got = from_partner(jnp.stack([own_give, cross_pass]), "view", 0)
    tiles = lax.axis_size("tile")
    views = lax.axis_size("view")
    route = []
    for tile in range(tiles - 1):
        for slab in range(views // 2):
            right_core = tile * views + 2 * slab + 1
            left_core = (tile + 1) * views + 2 * slab
            route += [(right_core, left_core), (left_core, right_core)]
    outgoing = jnp.where(first, jnp.stack([cross_keep, got[1]]), jnp.stack([got[1], cross_keep]))
    incoming = lax.ppermute(outgoing, ("tile", "view"), route)
    own_parts = jnp.where(first, jnp.stack([own_keep, got[0]]), jnp.stack([got[0], own_keep]))
    views_measured = own_parts + incoming
    observed = views_measured.astype(jnp.float32)
    estimate = 0.5 * (observed[0] + observed[1])
    kernels = (psf_taps / jnp.sum(psf_taps, axis=2, keepdims=True)).astype(jnp.bfloat16)
    view_count = kernels.shape[0]
    forward_ops = stacked_operators(kernels, planes, half_x, width_y)
    adjoint_ops = stacked_operators(kernels[:, :, ::-1], planes, half_x, width_y)
    for iteration in range(ITERS):
        estimate_low = estimate.astype(jnp.bfloat16)
        low, high = x_rims(estimate_low, reach, 1)
        extended = jnp.concatenate([low, estimate_low, high], axis=1)
        after_x = jnp.einsum(
            "vzpa,zay->vzpy", forward_ops[0], extended, preferred_element_type=jnp.float32
        ).astype(jnp.bfloat16)
        blurred = pass_z_views(pass_y_views(after_x, forward_ops[1]), forward_ops[2], reach)
        quotients = (observed / blurred).astype(jnp.bfloat16)
        low, high = x_rims(quotients, reach, 2)
        widened = jnp.concatenate([low, quotients, high], axis=2)
        after_x = jnp.einsum(
            "vzpa,vzay->vzpy", adjoint_ops[0], widened, preferred_element_type=jnp.float32
        ).astype(jnp.bfloat16)
        backs = pass_z_views(pass_y_views(after_x, adjoint_ops[1]), adjoint_ops[2], reach)
        estimate = estimate * (0.5 * (backs[0] + backs[1]))
    keep = lax.dynamic_slice_in_dim(estimate, view_bit * half_rows, half_rows, 0)
    give = lax.dynamic_slice_in_dim(estimate, (1 - view_bit) * half_rows, half_rows, 0)
    got = from_partner(give, "view", 0)
    return jnp.where(
        view_bit == 0, jnp.concatenate([keep, got], axis=1), jnp.concatenate([got, keep], axis=1)
    )


def solution(mesh):
    in_specs = (P(("timepoin", "view"), "tile", None), P(), P(("timepoin", "view"), None))
    out_specs = P(("timepoin", "view"), "tile", None)
    return jax.shard_map(local, mesh=mesh, in_specs=in_specs, out_specs=out_specs, check_vma=False)
```

```python
import jax
import jax.numpy as jnp
from jax import lax
from jax.sharding import PartitionSpec as P

BX = 4
ITERS = 2


def shifted(block, axis, distance):
    devices = range(lax.axis_size(axis))
    route = [(i - distance, i) for i in devices if i - distance in devices]
    return lax.ppermute(block, axis, route)


def from_partner(block, axis, distance):
    count = lax.axis_size(axis)
    route = []
    for low in range(count):
        high = low | 1 << distance
        if high != low and high < count:
            route += [(low, high), (high, low)]
    return lax.ppermute(block, axis, route)


def extended_2(block, sides, width):
    for axis, dim in sides:
        count = lax.axis_size(axis)
        forward = [(i, i + 1) for i in range(count - 1)]
        backward = [(target, source) for source, target in forward]
        low = lax.ppermute(
            lax.slice_in_dim(block, block.shape[dim] - width, None, axis=dim), axis, forward
        )
        high = lax.ppermute(lax.slice_in_dim(block, 0, width, axis=dim), axis, backward)
        block = jnp.concatenate([low, block, high], axis=dim)
    return block


def band_matrix(kernel, row_count, col_count, base_shift):
    row_ids = lax.broadcasted_iota(jnp.int32, (row_count, col_count, 1), 0)
    col_ids = lax.broadcasted_iota(jnp.int32, (row_count, col_count, 1), 1)
    tap_ids = lax.broadcasted_iota(jnp.int32, (1, 1, kernel.shape[0]), 2)
    hit = row_ids - col_ids + base_shift == tap_ids
    taps = kernel.astype(jnp.float32)[None, None, :]
    matrix = jnp.sum(jnp.where(hit, taps, jnp.float32(0.0)), axis=2)
    return matrix.astype(jnp.bfloat16)


def operators(kernels, plane_count, width_x, width_y):
    reach = kernels.shape[1] // 2
    along_x = band_matrix(kernels[0], width_x + 2 * reach, width_x, 0).T
    along_x = jnp.broadcast_to(along_x[None], (plane_count,) + along_x.shape)
    return lax.optimization_barrier((
        along_x,
        band_matrix(kernels[1], width_y, width_y, reach),
        band_matrix(kernels[2], plane_count + 2 * reach, plane_count, 0).T,
    ))


def pass_xy(extended, matrices):
    width_y = extended.shape[2]
    after_x = jnp.einsum(
        "zpa,zay->zpy", matrices[0], extended, preferred_element_type=jnp.float32
    ).astype(jnp.bfloat16)
    after_y = jnp.dot(after_x.reshape(-1, width_y), matrices[1], preferred_element_type=jnp.float32)
    return after_y.reshape(after_x.shape).astype(jnp.bfloat16)


def pass_z(extended, matrix):
    planes = extended.shape[0]
    out = jnp.dot(matrix, extended.reshape(planes, -1), preferred_element_type=jnp.float32)
    return out.reshape((matrix.shape[0],) + extended.shape[1:])


def stacked_operators(kernels, plane_count, width_x, width_y):
    reach = kernels.shape[2] // 2
    views = range(kernels.shape[0])
    along_x = jnp.stack([band_matrix(kernels[v, 0], width_x + 2 * reach, width_x, 0).T for v in views])
    along_x = jnp.broadcast_to(along_x[:, None], (along_x.shape[0], plane_count) + along_x.shape[1:])
    return lax.optimization_barrier((
        along_x,
        jnp.stack([band_matrix(kernels[v, 1], width_y, width_y, reach) for v in views]),
        jnp.stack([band_matrix(kernels[v, 2], plane_count + 2 * reach, plane_count, 0).T for v in views]),
    ))


def pass_y_views(after_x, matrices):
    shape = after_x.shape
    flat = after_x.reshape(shape[0], -1, shape[-1])
    after_y = jnp.einsum("vmy,vyq->vmq", flat, matrices, preferred_element_type=jnp.float32)
    return after_y.reshape(shape).astype(jnp.bfloat16)


def pass_z_views(after_y, matrices, reach):
    below, above = z_rims(after_y, reach, 1)
    widened = jnp.concatenate([below, after_y, above], axis=1)
    return jnp.einsum("vpa,vaxy->vpxy", matrices, widened, preferred_element_type=jnp.float32)


def z_rims(volume, reach, axis):
    slabs = lax.axis_size("view") // 2
    slab = lax.axis_index("view") // 2
    planes = volume.shape[axis]
    shape = list(volume.shape)
    shape[axis] = reach
    below = jnp.zeros(shape, volume.dtype)
    above = below
    for phase in (0, 1):
        route = []
        for low in range(phase, slabs - 1, 2):
            for bit in (0, 1):
                route += [(2 * low + bit, 2 * low + 2 + bit), (2 * low + 2 + bit, 2 * low + bit)]
        if not route:
            continue
        is_lower = slab % 2 == phase
        start = jnp.where(is_lower, planes - reach, 0)
        payload = lax.dynamic_slice_in_dim(volume, start, reach, axis)
        got = lax.ppermute(payload, "view", route)
        below = jnp.where(is_lower, below, got)
        above = jnp.where(is_lower, got, above)
    return below, above


def x_rims(block, reach, axis):
    tiles = lax.axis_size("tile")
    views = lax.axis_size("view")
    route = []
    for tile in range(tiles - 1):
        for slab in range(views // 2):
            right_core = tile * views + 2 * slab + 1
            left_core = (tile + 1) * views + 2 * slab
            route += [(right_core, left_core), (left_core, right_core)]
    first = lax.axis_index("view") % 2 == 0
    width = block.shape[axis]
    outward = lax.dynamic_slice_in_dim(block, jnp.where(first, 0, width - reach), reach, axis)
    inward = lax.dynamic_slice_in_dim(block, jnp.where(first, width - reach, 0), reach, axis)
    across = lax.ppermute(outward, ("tile", "view"), route)
    beside = from_partner(inward, "view", 0)
    low = jnp.where(first, across, beside)
    high = jnp.where(first, beside, across)
    return low, high


def local(acquired, psf_taps, block_source):
    planes, width_x, width_y = acquired.shape
    block_count = width_x // BX
    capacity = block_count // 2
    reach = psf_taps.shape[2] // 2
    tile_index = lax.axis_index("tile")
    tile_total = lax.axis_size("tile")
    view_bit = lax.axis_index("view") % 2
    sources = block_source[0]
    blocks = acquired.reshape(planes, block_count, BX, width_y)
    half_x = width_x // 2
    half_rows = planes // 2
    half_blocks = block_count // 2
    first = view_bit == 0
    starts = []
    for target, half in ((tile_index, 0), (tile_index, 1), (tile_index + 1, 0), (tile_index - 1, 1)):
        target = jnp.clip(target, 0, tile_total - 1)
        starts.append(target * block_count + half * half_blocks)
    slots = jnp.concatenate([lax.dynamic_slice_in_dim(sources, st, half_blocks) for st in starts])
    picked = jnp.concatenate(
        [lax.dynamic_slice_in_dim(acquired, (slots[i] % block_count) * BX, BX, 1) for i in range(slots.shape[0])],
        axis=1,
    )
    mine = jnp.repeat(slots // block_count == tile_index, BX)[None, :, None]
    partials = jnp.where(mine, picked, jnp.zeros((), picked.dtype))
    partials = partials.reshape(planes, 4, half_x, width_y)
    own_keep = jnp.where(first, partials[:, 0], partials[:, 1])
    own_give = jnp.where(first, partials[:, 1], partials[:, 0])
    cross_keep = jnp.where(first, partials[:, 3], partials[:, 2])
    cross_pass = jnp.where(first, partials[:, 2], partials[:, 3])
    got = from_partner(jnp.stack([own_give, cross_pass]), "view", 0)
    tiles = lax.axis_size("tile")
    views = lax.axis_size("view")
    route = []
    for tile in range(tiles - 1):
        for slab in range(views // 2):
            right_core = tile * views + 2 * slab + 1
            left_core = (tile + 1) * views + 2 * slab
            route += [(right_core, left_core), (left_core, right_core)]
    outgoing = jnp.where(first, jnp.stack([cross_keep, got[1]]), jnp.stack([got[1], cross_keep]))
    incoming = lax.ppermute(outgoing, ("tile", "view"), route)
    own_parts = jnp.where(first, jnp.stack([own_keep, got[0]]), jnp.stack([got[0], own_keep]))
    views_measured = own_parts + incoming
    observed = views_measured.astype(jnp.float32)
    estimate = 0.5 * (observed[0] + observed[1])
    kernels = (psf_taps / jnp.sum(psf_taps, axis=2, keepdims=True)).astype(jnp.bfloat16)
    view_count = kernels.shape[0]
    forward_ops = stacked_operators(kernels, planes, half_x, width_y)
    adjoint_ops = tuple(jnp.flip(m, axis=(-2, -1)) for m in forward_ops)
    for iteration in range(ITERS):
        estimate_low = estimate.astype(jnp.bfloat16)
        low, high = x_rims(estimate_low, reach, 1)
        extended = jnp.concatenate([low, estimate_low, high], axis=1)
        after_x = jnp.einsum(
            "vzpa,zay->vzpy", forward_ops[0], extended, preferred_element_type=jnp.float32
        ).astype(jnp.bfloat16)
        blurred = pass_z_views(pass_y_views(after_x, forward_ops[1]), forward_ops[2], reach)
        quotients = (observed / blurred).astype(jnp.bfloat16)
        low, high = x_rims(quotients, reach, 2)
        widened = jnp.concatenate([low, quotients, high], axis=2)
        after_x = jnp.einsum(
            "vzpa,vzay->vzpy", adjoint_ops[0], widened, preferred_element_type=jnp.float32
        ).astype(jnp.bfloat16)
        backs = pass_z_views(pass_y_views(after_x, adjoint_ops[1]), adjoint_ops[2], reach)
        estimate = estimate * (0.5 * (backs[0] + backs[1]))
    keep = lax.dynamic_slice_in_dim(estimate, view_bit * half_rows, half_rows, 0)
    give = lax.dynamic_slice_in_dim(estimate, (1 - view_bit) * half_rows, half_rows, 0)
    got = from_partner(give, "view", 0)
    return jnp.where(
        view_bit == 0, jnp.concatenate([keep, got], axis=1), jnp.concatenate([got, keep], axis=1)
    )


def solution(mesh):
    in_specs = (P(("timepoin", "view"), "tile", None), P(), P(("timepoin", "view"), None))
    out_specs = P(("timepoin", "view"), "tile", None)
    return jax.shard_map(local, mesh=mesh, in_specs=in_specs, out_specs=out_specs, check_vma=False)
```

```python
import jax
import jax.numpy as jnp
from jax import lax
from jax.sharding import PartitionSpec as P

BX = 4
ITERS = 2


def shifted(block, axis, distance):
    devices = range(lax.axis_size(axis))
    route = [(i - distance, i) for i in devices if i - distance in devices]
    return lax.ppermute(block, axis, route)


def from_partner(block, axis, distance):
    count = lax.axis_size(axis)
    route = []
    for low in range(count):
        high = low | 1 << distance
        if high != low and high < count:
            route += [(low, high), (high, low)]
    return lax.ppermute(block, axis, route)


def extended_2(block, sides, width):
    for axis, dim in sides:
        count = lax.axis_size(axis)
        forward = [(i, i + 1) for i in range(count - 1)]
        backward = [(target, source) for source, target in forward]
        low = lax.ppermute(
            lax.slice_in_dim(block, block.shape[dim] - width, None, axis=dim), axis, forward
        )
        high = lax.ppermute(lax.slice_in_dim(block, 0, width, axis=dim), axis, backward)
        block = jnp.concatenate([low, block, high], axis=dim)
    return block


def band_matrix(kernel, row_count, col_count, base_shift):
    row_ids = lax.broadcasted_iota(jnp.int32, (row_count, col_count, 1), 0)
    col_ids = lax.broadcasted_iota(jnp.int32, (row_count, col_count, 1), 1)
    tap_ids = lax.broadcasted_iota(jnp.int32, (1, 1, kernel.shape[0]), 2)
    hit = row_ids - col_ids + base_shift == tap_ids
    taps = kernel.astype(jnp.float32)[None, None, :]
    matrix = jnp.sum(jnp.where(hit, taps, jnp.float32(0.0)), axis=2)
    return matrix.astype(jnp.bfloat16)


def operators(kernels, plane_count, width_x, width_y):
    reach = kernels.shape[1] // 2
    along_x = band_matrix(kernels[0], width_x + 2 * reach, width_x, 0).T
    along_x = jnp.broadcast_to(along_x[None], (plane_count,) + along_x.shape)
    return lax.optimization_barrier((
        along_x,
        band_matrix(kernels[1], width_y, width_y, reach),
        band_matrix(kernels[2], plane_count + 2 * reach, plane_count, 0).T,
    ))


def pass_xy(extended, matrices):
    width_y = extended.shape[2]
    after_x = jnp.einsum(
        "zpa,zay->zpy", matrices[0], extended, preferred_element_type=jnp.float32
    ).astype(jnp.bfloat16)
    after_y = jnp.dot(after_x.reshape(-1, width_y), matrices[1], preferred_element_type=jnp.float32)
    return after_y.reshape(after_x.shape).astype(jnp.bfloat16)


def pass_z(extended, matrix):
    planes = extended.shape[0]
    out = jnp.dot(matrix, extended.reshape(planes, -1), preferred_element_type=jnp.float32)
    return out.reshape((matrix.shape[0],) + extended.shape[1:])


def stacked_operators(kernels, plane_count, width_x, width_y):
    reach = kernels.shape[2] // 2
    views = range(kernels.shape[0])
    along_x = jnp.stack([band_matrix(kernels[v, 0], width_x + 2 * reach, width_x, 0).T for v in views])
    along_x = jnp.broadcast_to(along_x[:, None], (along_x.shape[0], plane_count) + along_x.shape[1:])
    return lax.optimization_barrier((
        along_x,
        jnp.stack([band_matrix(kernels[v, 1], width_y, width_y, reach) for v in views]),
        jnp.stack([band_matrix(kernels[v, 2], plane_count + 2 * reach, plane_count, 0).T for v in views]),
    ))


def pass_y_views(after_x, matrices):
    shape = after_x.shape
    flat = after_x.reshape(shape[0], -1, shape[-1])
    after_y = jnp.einsum("vmy,vyq->vmq", flat, matrices, preferred_element_type=jnp.float32)
    return after_y.reshape(shape).astype(jnp.bfloat16)


def pass_z_views(after_y, matrices, reach):
    below, above = z_rims(after_y, reach, 1)
    widened = jnp.concatenate([below, after_y, above], axis=1)
    return jnp.einsum("vpa,vaxy->vpxy", matrices, widened, preferred_element_type=jnp.float32)


def z_rims(volume, reach, axis):
    slabs = lax.axis_size("view") // 2
    slab = lax.axis_index("view") // 2
    planes = volume.shape[axis]
    shape = list(volume.shape)
    shape[axis] = reach
    below = jnp.zeros(shape, volume.dtype)
    above = below
    for phase in (0, 1):
        route = []
        for low in range(phase, slabs - 1, 2):
            for bit in (0, 1):
                route += [(2 * low + bit, 2 * low + 2 + bit), (2 * low + 2 + bit, 2 * low + bit)]
        if not route:
            continue
        is_lower = slab % 2 == phase
        start = jnp.where(is_lower, planes - reach, 0)
        payload = lax.dynamic_slice_in_dim(volume, start, reach, axis)
        got = lax.ppermute(payload, "view", route)
        below = jnp.where(is_lower, below, got)
        above = jnp.where(is_lower, got, above)
    return below, above


def x_rims(block, reach, axis):
    tiles = lax.axis_size("tile")
    views = lax.axis_size("view")
    route = []
    for tile in range(tiles - 1):
        for slab in range(views // 2):
            right_core = tile * views + 2 * slab + 1
            left_core = (tile + 1) * views + 2 * slab
            route += [(right_core, left_core), (left_core, right_core)]
    first = lax.axis_index("view") % 2 == 0
    width = block.shape[axis]
    outward = lax.dynamic_slice_in_dim(block, jnp.where(first, 0, width - reach), reach, axis)
    inward = lax.dynamic_slice_in_dim(block, jnp.where(first, width - reach, 0), reach, axis)
    across = lax.ppermute(outward, ("tile", "view"), route)
    beside = from_partner(inward, "view", 0)
    low = jnp.where(first, across, beside)
    high = jnp.where(first, beside, across)
    return low, high


def local(acquired, psf_taps, block_source):
    planes, width_x, width_y = acquired.shape
    block_count = width_x // BX
    capacity = block_count // 2
    reach = psf_taps.shape[2] // 2
    tile_index = lax.axis_index("tile")
    tile_total = lax.axis_size("tile")
    view_bit = lax.axis_index("view") % 2
    sources = block_source[0]
    blocks = acquired.reshape(planes, block_count, BX, width_y)
    half_x = width_x // 2
    half_rows = planes // 2
    half_blocks = block_count // 2
    first = view_bit == 0
    starts = []
    for target, half in ((tile_index, 0), (tile_index, 1), (tile_index + 1, 0), (tile_index - 1, 1)):
        target = jnp.clip(target, 0, tile_total - 1)
        starts.append(target * block_count + half * half_blocks)
    slots = jnp.concatenate([lax.dynamic_slice_in_dim(sources, st, half_blocks) for st in starts])
    picked = jnp.concatenate(
        [lax.dynamic_slice_in_dim(acquired, (slots[i] % block_count) * BX, BX, 1) for i in range(slots.shape[0])],
        axis=1,
    )
    mine = jnp.repeat(slots // block_count == tile_index, BX)[None, :, None]
    partials = jnp.where(mine, picked, jnp.zeros((), picked.dtype))
    partials = partials.reshape(planes, 4, half_x, width_y)
    own_keep = jnp.where(first, partials[:, 0], partials[:, 1])
    own_give = jnp.where(first, partials[:, 1], partials[:, 0])
    cross_keep = jnp.where(first, partials[:, 3], partials[:, 2])
    cross_pass = jnp.where(first, partials[:, 2], partials[:, 3])
    got = from_partner(jnp.stack([own_give, cross_pass]), "view", 0)
    tiles = lax.axis_size("tile")
    views = lax.axis_size("view")
    route = []
    for tile in range(tiles - 1):
        for slab in range(views // 2):
            right_core = tile * views + 2 * slab + 1
            left_core = (tile + 1) * views + 2 * slab
            route += [(right_core, left_core), (left_core, right_core)]
    outgoing = jnp.where(first, jnp.stack([cross_keep, got[1]]), jnp.stack([got[1], cross_keep]))
    incoming = lax.ppermute(outgoing, ("tile", "view"), route)
    own_parts = jnp.where(first, jnp.stack([own_keep, got[0]]), jnp.stack([got[0], own_keep]))
    views_measured = own_parts + incoming
    observed = views_measured.astype(jnp.float32)
    estimate = 0.5 * (observed[0] + observed[1])
    kernels = (psf_taps / jnp.sum(psf_taps, axis=2, keepdims=True)).astype(jnp.bfloat16)
    view_count = kernels.shape[0]
    forward_ops = stacked_operators(kernels, planes, half_x, width_y)
    adjoint_ops = stacked_operators(kernels[:, :, ::-1], planes, half_x, width_y)
    for iteration in range(ITERS):
        estimate_low = estimate.astype(jnp.bfloat16)
        low, high = x_rims(estimate_low, reach, 1)
        extended = jnp.concatenate([low, estimate_low, high], axis=1)
        after_x = jnp.einsum(
            "vzpa,zay->vzpy", forward_ops[0], extended, preferred_element_type=jnp.float32
        ).astype(jnp.bfloat16)
        blurred = pass_z_views(pass_y_views(after_x, forward_ops[1]), forward_ops[2], reach)
        quotients = (observed / blurred).astype(jnp.bfloat16)
        low, high = x_rims(quotients, reach, 2)
        widened = jnp.concatenate([low, quotients, high], axis=2)
        after_x = jnp.einsum(
            "vzpa,vzay->vzpy", adjoint_ops[0], widened, preferred_element_type=jnp.float32
        ).astype(jnp.bfloat16)
        backs = pass_z_views(pass_y_views(after_x, adjoint_ops[1]), adjoint_ops[2], reach)
        estimate = estimate * (0.5 * (backs[0] + backs[1]))
    keep = lax.dynamic_slice_in_dim(estimate, view_bit * half_rows, half_rows, 0)
    give = lax.dynamic_slice_in_dim(estimate, (1 - view_bit) * half_rows, half_rows, 0)
    got = from_partner(give, "view", 0)
    return jnp.where(
        view_bit == 0, jnp.concatenate([keep, got], axis=1), jnp.concatenate([got, keep], axis=1)
    )


def solution(mesh):
    in_specs = (P(("timepoin", "view"), "tile", None), P(), P(("timepoin", "view"), None))
    out_specs = P(("timepoin", "view"), "tile", None)
    return jax.shard_map(local, mesh=mesh, in_specs=in_specs, out_specs=out_specs, check_vma=False)
```

```python
import jax
import jax.numpy as jnp
from jax import lax
from jax.sharding import PartitionSpec as P

BX = 4
ITERS = 2


def shifted(block, axis, distance):
    devices = range(lax.axis_size(axis))
    route = [(i - distance, i) for i in devices if i - distance in devices]
    return lax.ppermute(block, axis, route)


def from_partner(block, axis, distance):
    count = lax.axis_size(axis)
    route = []
    for low in range(count):
        high = low | 1 << distance
        if high != low and high < count:
            route += [(low, high), (high, low)]
    return lax.ppermute(block, axis, route)


def extended_2(block, sides, width):
    for axis, dim in sides:
        count = lax.axis_size(axis)
        forward = [(i, i + 1) for i in range(count - 1)]
        backward = [(target, source) for source, target in forward]
        low = lax.ppermute(
            lax.slice_in_dim(block, block.shape[dim] - width, None, axis=dim), axis, forward
        )
        high = lax.ppermute(lax.slice_in_dim(block, 0, width, axis=dim), axis, backward)
        block = jnp.concatenate([low, block, high], axis=dim)
    return block


def band_matrix(kernel, row_count, col_count, base_shift):
    row_ids = lax.broadcasted_iota(jnp.int32, (row_count, col_count, 1), 0)
    col_ids = lax.broadcasted_iota(jnp.int32, (row_count, col_count, 1), 1)
    tap_ids = lax.broadcasted_iota(jnp.int32, (1, 1, kernel.shape[0]), 2)
    hit = row_ids - col_ids + base_shift == tap_ids
    taps = kernel.astype(jnp.float32)[None, None, :]
    matrix = jnp.sum(jnp.where(hit, taps, jnp.float32(0.0)), axis=2)
    return matrix.astype(jnp.bfloat16)


def operators(kernels, plane_count, width_x, width_y):
    reach = kernels.shape[1] // 2
    along_x = band_matrix(kernels[0], width_x + 2 * reach, width_x, 0).T
    along_x = jnp.broadcast_to(along_x[None], (plane_count,) + along_x.shape)
    return lax.optimization_barrier((
        along_x,
        band_matrix(kernels[1], width_y, width_y, reach),
        band_matrix(kernels[2], plane_count + 2 * reach, plane_count, 0).T,
    ))


def pass_xy(extended, matrices):
    width_y = extended.shape[2]
    after_x = jnp.einsum(
        "zpa,zay->zpy", matrices[0], extended, preferred_element_type=jnp.float32
    ).astype(jnp.bfloat16)
    after_y = jnp.dot(after_x.reshape(-1, width_y), matrices[1], preferred_element_type=jnp.float32)
    return after_y.reshape(after_x.shape).astype(jnp.bfloat16)


def pass_z(extended, matrix):
    planes = extended.shape[0]
    out = jnp.dot(matrix, extended.reshape(planes, -1), preferred_element_type=jnp.float32)
    return out.reshape((matrix.shape[0],) + extended.shape[1:])


def stacked_operators(kernels, plane_count, width_x, width_y):
    reach = kernels.shape[2] // 2
    views = range(kernels.shape[0])
    along_x = jnp.stack([band_matrix(kernels[v, 0], width_x + 2 * reach, width_x, 0).T for v in views])
    along_x = jnp.broadcast_to(along_x[:, None], (along_x.shape[0], plane_count) + along_x.shape[1:])
    return lax.optimization_barrier((
        along_x,
        jnp.stack([band_matrix(kernels[v, 1], width_y, width_y, reach) for v in views]),
        jnp.stack([band_matrix(kernels[v, 2], plane_count + 2 * reach, plane_count, 0).T for v in views]),
    ))


def pass_y_views(after_x, matrices):
    shape = after_x.shape
    flat = after_x.reshape(shape[0], -1, shape[-1])
    after_y = jnp.einsum("vmy,vyq->vmq", flat, matrices, preferred_element_type=jnp.float32)
    return after_y.reshape(shape).astype(jnp.bfloat16)


def pass_z_views(after_y, matrices, reach):
    below, above = z_rims(after_y, reach, 1)
    widened = jnp.concatenate([below, after_y, above], axis=1)
    return jnp.einsum("vpa,vaxy->vpxy", matrices, widened, preferred_element_type=jnp.float32)


def z_rims(volume, reach, axis):
    slabs = lax.axis_size("view") // 2
    slab = lax.axis_index("view") // 2
    planes = volume.shape[axis]
    shape = list(volume.shape)
    shape[axis] = reach
    below = jnp.zeros(shape, volume.dtype)
    above = below
    for phase in (0, 1):
        route = []
        for low in range(phase, slabs - 1, 2):
            for bit in (0, 1):
                route += [(2 * low + bit, 2 * low + 2 + bit), (2 * low + 2 + bit, 2 * low + bit)]
        if not route:
            continue
        is_lower = slab % 2 == phase
        start = jnp.where(is_lower, planes - reach, 0)
        payload = lax.dynamic_slice_in_dim(volume, start, reach, axis)
        got = lax.ppermute(payload, "view", route)
        below = jnp.where(is_lower, below, got)
        above = jnp.where(is_lower, got, above)
    return below, above


def x_rims(block, reach, axis):
    tiles = lax.axis_size("tile")
    views = lax.axis_size("view")
    route = []
    for tile in range(tiles - 1):
        for slab in range(views // 2):
            right_core = tile * views + 2 * slab + 1
            left_core = (tile + 1) * views + 2 * slab
            route += [(right_core, left_core), (left_core, right_core)]
    first = lax.axis_index("view") % 2 == 0
    width = block.shape[axis]
    outward = lax.dynamic_slice_in_dim(block, jnp.where(first, 0, width - reach), reach, axis)
    inward = lax.dynamic_slice_in_dim(block, jnp.where(first, width - reach, 0), reach, axis)
    across = lax.ppermute(outward, ("tile", "view"), route)
    beside = from_partner(inward, "view", 0)
    low = jnp.where(first, across, beside)
    high = jnp.where(first, beside, across)
    return low, high


def local(acquired, psf_taps, block_source):
    planes, width_x, width_y = acquired.shape
    block_count = width_x // BX
    capacity = block_count // 2
    reach = psf_taps.shape[2] // 2
    tile_index = lax.axis_index("tile")
    tile_total = lax.axis_size("tile")
    view_bit = lax.axis_index("view") % 2
    sources = block_source[0]
    blocks = acquired.reshape(planes, block_count, BX, width_y)
    half_x = width_x // 2
    half_rows = planes // 2
    half_blocks = block_count // 2
    first = view_bit == 0
    starts = []
    for target, half in ((tile_index, 0), (tile_index, 1), (tile_index + 1, 0), (tile_index - 1, 1)):
        target = jnp.clip(target, 0, tile_total - 1)
        starts.append(target * block_count + half * half_blocks)
    slots = jnp.concatenate([lax.dynamic_slice_in_dim(sources, st, half_blocks) for st in starts])
    picked = jnp.take(blocks, slots % block_count, axis=1)
    mine = (slots // block_count == tile_index)[None, :, None, None]
    partials = jnp.where(mine, picked, jnp.zeros((), picked.dtype))
    partials = partials.reshape(planes, 4, half_x, width_y)
    own_keep = jnp.where(first, partials[:, 0], partials[:, 1])
    own_give = jnp.where(first, partials[:, 1], partials[:, 0])
    cross_keep = jnp.where(first, partials[:, 3], partials[:, 2])
    cross_pass = jnp.where(first, partials[:, 2], partials[:, 3])
    got = from_partner(jnp.stack([own_give, cross_pass]), "view", 0)
    tiles = lax.axis_size("tile")
    views = lax.axis_size("view")
    route = []
    for tile in range(tiles - 1):
        for slab in range(views // 2):
            right_core = tile * views + 2 * slab + 1
            left_core = (tile + 1) * views + 2 * slab
            route += [(right_core, left_core), (left_core, right_core)]
    outgoing = jnp.where(first, jnp.stack([cross_keep, got[1]]), jnp.stack([got[1], cross_keep]))
    outgoing, psf_taps = lax.optimization_barrier((outgoing, psf_taps))
    incoming = lax.ppermute(outgoing, ("tile", "view"), route)
    own_parts = jnp.where(first, jnp.stack([own_keep, got[0]]), jnp.stack([got[0], own_keep]))
    views_measured = own_parts + incoming
    observed = views_measured.astype(jnp.float32)
    estimate = 0.5 * (observed[0] + observed[1])
    kernels = (psf_taps / jnp.sum(psf_taps, axis=2, keepdims=True)).astype(jnp.bfloat16)
    view_count = kernels.shape[0]
    forward_ops = stacked_operators(kernels, planes, half_x, width_y)
    adjoint_ops = stacked_operators(kernels[:, :, ::-1], planes, half_x, width_y)
    for iteration in range(ITERS):
        estimate_low = estimate.astype(jnp.bfloat16)
        low, high = x_rims(estimate_low, reach, 1)
        extended = jnp.concatenate([low, estimate_low, high], axis=1)
        after_x = jnp.einsum(
            "vzpa,zay->vzpy", forward_ops[0], extended, preferred_element_type=jnp.float32
        ).astype(jnp.bfloat16)
        blurred = pass_z_views(pass_y_views(after_x, forward_ops[1]), forward_ops[2], reach)
        quotients = (observed / blurred).astype(jnp.bfloat16)
        low, high = x_rims(quotients, reach, 2)
        widened = jnp.concatenate([low, quotients, high], axis=2)
        after_x = jnp.einsum(
            "vzpa,vzay->vzpy", adjoint_ops[0], widened, preferred_element_type=jnp.float32
        ).astype(jnp.bfloat16)
        backs = pass_z_views(pass_y_views(after_x, adjoint_ops[1]), adjoint_ops[2], reach)
        estimate = estimate * (0.5 * (backs[0] + backs[1]))
    keep = lax.dynamic_slice_in_dim(estimate, view_bit * half_rows, half_rows, 0)
    give = lax.dynamic_slice_in_dim(estimate, (1 - view_bit) * half_rows, half_rows, 0)
    got = from_partner(give, "view", 0)
    return jnp.where(
        view_bit == 0, jnp.concatenate([keep, got], axis=1), jnp.concatenate([got, keep], axis=1)
    )


def solution(mesh):
    in_specs = (P(("timepoin", "view"), "tile", None), P(), P(("timepoin", "view"), None))
    out_specs = P(("timepoin", "view"), "tile", None)
    return jax.shard_map(local, mesh=mesh, in_specs=in_specs, out_specs=out_specs, check_vma=False)
```

```python
import jax
import jax.numpy as jnp
from jax import lax
from jax.sharding import PartitionSpec as P

BX = 4
ITERS = 2


def shifted(block, axis, distance):
    devices = range(lax.axis_size(axis))
    route = [(i - distance, i) for i in devices if i - distance in devices]
    return lax.ppermute(block, axis, route)


def from_partner(block, axis, distance):
    count = lax.axis_size(axis)
    route = []
    for low in range(count):
        high = low | 1 << distance
        if high != low and high < count:
            route += [(low, high), (high, low)]
    return lax.ppermute(block, axis, route)


def extended_2(block, sides, width):
    for axis, dim in sides:
        count = lax.axis_size(axis)
        forward = [(i, i + 1) for i in range(count - 1)]
        backward = [(target, source) for source, target in forward]
        low = lax.ppermute(
            lax.slice_in_dim(block, block.shape[dim] - width, None, axis=dim), axis, forward
        )
        high = lax.ppermute(lax.slice_in_dim(block, 0, width, axis=dim), axis, backward)
        block = jnp.concatenate([low, block, high], axis=dim)
    return block


def band_matrix(kernel, row_count, col_count, base_shift):
    row_ids = lax.broadcasted_iota(jnp.int32, (row_count, col_count, 1), 0)
    col_ids = lax.broadcasted_iota(jnp.int32, (row_count, col_count, 1), 1)
    tap_ids = lax.broadcasted_iota(jnp.int32, (1, 1, kernel.shape[0]), 2)
    hit = row_ids - col_ids + base_shift == tap_ids
    taps = kernel.astype(jnp.float32)[None, None, :]
    matrix = jnp.sum(jnp.where(hit, taps, jnp.float32(0.0)), axis=2)
    return matrix.astype(jnp.bfloat16)


def operators(kernels, plane_count, width_x, width_y):
    reach = kernels.shape[1] // 2
    along_x = band_matrix(kernels[0], width_x + 2 * reach, width_x, 0).T
    along_x = jnp.broadcast_to(along_x[None], (plane_count,) + along_x.shape)
    return lax.optimization_barrier((
        along_x,
        band_matrix(kernels[1], width_y, width_y, reach),
        band_matrix(kernels[2], plane_count + 2 * reach, plane_count, 0).T,
    ))


def pass_xy(extended, matrices):
    width_y = extended.shape[2]
    after_x = jnp.einsum(
        "zpa,zay->zpy", matrices[0], extended, preferred_element_type=jnp.float32
    ).astype(jnp.bfloat16)
    after_y = jnp.dot(after_x.reshape(-1, width_y), matrices[1], preferred_element_type=jnp.float32)
    return after_y.reshape(after_x.shape).astype(jnp.bfloat16)


def pass_z(extended, matrix):
    planes = extended.shape[0]
    out = jnp.dot(matrix, extended.reshape(planes, -1), preferred_element_type=jnp.float32)
    return out.reshape((matrix.shape[0],) + extended.shape[1:])


def stacked_operators(kernels, plane_count, width_x, width_y):
    reach = kernels.shape[2] // 2
    views = range(kernels.shape[0])
    along_x = jnp.stack([band_matrix(kernels[v, 0], width_x + 2 * reach, width_x, 0).T for v in views])
    along_x = jnp.broadcast_to(along_x[:, None], (along_x.shape[0], plane_count) + along_x.shape[1:])
    return lax.optimization_barrier((
        along_x,
        jnp.stack([band_matrix(kernels[v, 1], width_y, width_y, reach) for v in views]),
        jnp.stack([band_matrix(kernels[v, 2], plane_count + 2 * reach, plane_count, 0).T for v in views]),
    ))


def pass_y_views(after_x, matrices):
    shape = after_x.shape
    flat = after_x.reshape(shape[0], -1, shape[-1])
    after_y = jnp.einsum("vmy,vyq->vmq", flat, matrices, preferred_element_type=jnp.float32)
    return after_y.reshape(shape).astype(jnp.bfloat16)


def pass_z_views(after_y, matrices, reach):
    below, above = z_rims(after_y, reach, 1)
    widened = jnp.concatenate([below, after_y, above], axis=1)
    return jnp.einsum("vpa,vaxy->vpxy", matrices, widened, preferred_element_type=jnp.float32)


def z_rims(volume, reach, axis):
    slabs = lax.axis_size("view") // 2
    slab = lax.axis_index("view") // 2
    planes = volume.shape[axis]
    shape = list(volume.shape)
    shape[axis] = reach
    below = jnp.zeros(shape, volume.dtype)
    above = below
    for phase in (0, 1):
        route = []
        for low in range(phase, slabs - 1, 2):
            for bit in (0, 1):
                route += [(2 * low + bit, 2 * low + 2 + bit), (2 * low + 2 + bit, 2 * low + bit)]
        if not route:
            continue
        is_lower = slab % 2 == phase
        start = jnp.where(is_lower, planes - reach, 0)
        payload = lax.dynamic_slice_in_dim(volume, start, reach, axis)
        got = lax.ppermute(payload, "view", route)
        below = jnp.where(is_lower, below, got)
        above = jnp.where(is_lower, got, above)
    return below, above


def x_rims(block, reach, axis):
    tiles = lax.axis_size("tile")
    views = lax.axis_size("view")
    route = []
    for tile in range(tiles - 1):
        for slab in range(views // 2):
            right_core = tile * views + 2 * slab + 1
            left_core = (tile + 1) * views + 2 * slab
            route += [(right_core, left_core), (left_core, right_core)]
    first = lax.axis_index("view") % 2 == 0
    width = block.shape[axis]
    outward = lax.dynamic_slice_in_dim(block, jnp.where(first, 0, width - reach), reach, axis)
    inward = lax.dynamic_slice_in_dim(block, jnp.where(first, width - reach, 0), reach, axis)
    across = lax.ppermute(outward, ("tile", "view"), route)
    beside = from_partner(inward, "view", 0)
    low = jnp.where(first, across, beside)
    high = jnp.where(first, beside, across)
    return low, high


def local(acquired, psf_taps, block_source):
    planes, width_x, width_y = acquired.shape
    block_count = width_x // BX
    capacity = block_count // 2
    reach = psf_taps.shape[2] // 2
    tile_index = lax.axis_index("tile")
    tile_total = lax.axis_size("tile")
    view_bit = lax.axis_index("view") % 2
    sources = block_source[0]
    blocks = acquired.reshape(planes, block_count, BX, width_y)
    half_x = width_x // 2
    half_rows = planes // 2
    half_blocks = block_count // 2
    first = view_bit == 0
    starts = []
    for target, half in ((tile_index, 0), (tile_index, 1), (tile_index + 1, 0), (tile_index - 1, 1)):
        target = jnp.clip(target, 0, tile_total - 1)
        starts.append(target * block_count + half * half_blocks)
    slots = jnp.concatenate([lax.dynamic_slice_in_dim(sources, st, half_blocks) for st in starts])
    picked = jnp.zeros((planes, slots.shape[0], BX, width_y), acquired.dtype)
    for block in range(block_count):
        hit = (slots % block_count == block)[None, :, None, None]
        picked = jnp.where(hit, blocks[:, block : block + 1], picked)
    mine = (slots // block_count == tile_index)[None, :, None, None]
    partials = jnp.where(mine, picked, jnp.zeros((), picked.dtype))
    partials = partials.reshape(planes, 4, half_x, width_y)
    own_keep = jnp.where(first, partials[:, 0], partials[:, 1])
    own_give = jnp.where(first, partials[:, 1], partials[:, 0])
    cross_keep = jnp.where(first, partials[:, 3], partials[:, 2])
    cross_pass = jnp.where(first, partials[:, 2], partials[:, 3])
    got = from_partner(jnp.stack([own_give, cross_pass]), "view", 0)
    tiles = lax.axis_size("tile")
    views = lax.axis_size("view")
    route = []
    for tile in range(tiles - 1):
        for slab in range(views // 2):
            right_core = tile * views + 2 * slab + 1
            left_core = (tile + 1) * views + 2 * slab
            route += [(right_core, left_core), (left_core, right_core)]
    outgoing = jnp.where(first, jnp.stack([cross_keep, got[1]]), jnp.stack([got[1], cross_keep]))
    outgoing, psf_taps = lax.optimization_barrier((outgoing, psf_taps))
    incoming = lax.ppermute(outgoing, ("tile", "view"), route)
    own_parts = jnp.where(first, jnp.stack([own_keep, got[0]]), jnp.stack([got[0], own_keep]))
    views_measured = own_parts + incoming
    observed = views_measured.astype(jnp.float32)
    estimate = 0.5 * (observed[0] + observed[1])
    kernels = (psf_taps / jnp.sum(psf_taps, axis=2, keepdims=True)).astype(jnp.bfloat16)
    view_count = kernels.shape[0]
    forward_ops = stacked_operators(kernels, planes, half_x, width_y)
    adjoint_ops = stacked_operators(kernels[:, :, ::-1], planes, half_x, width_y)
    for iteration in range(ITERS):
        estimate_low = estimate.astype(jnp.bfloat16)
        low, high = x_rims(estimate_low, reach, 1)
        extended = jnp.concatenate([low, estimate_low, high], axis=1)
        after_x = jnp.einsum(
            "vzpa,zay->vzpy", forward_ops[0], extended, preferred_element_type=jnp.float32
        ).astype(jnp.bfloat16)
        blurred = pass_z_views(pass_y_views(after_x, forward_ops[1]), forward_ops[2], reach)
        quotients = (observed / blurred).astype(jnp.bfloat16)
        low, high = x_rims(quotients, reach, 2)
        widened = jnp.concatenate([low, quotients, high], axis=2)
        after_x = jnp.einsum(
            "vzpa,vzay->vzpy", adjoint_ops[0], widened, preferred_element_type=jnp.float32
        ).astype(jnp.bfloat16)
        backs = pass_z_views(pass_y_views(after_x, adjoint_ops[1]), adjoint_ops[2], reach)
        estimate = estimate * (0.5 * (backs[0] + backs[1]))
    keep = lax.dynamic_slice_in_dim(estimate, view_bit * half_rows, half_rows, 0)
    give = lax.dynamic_slice_in_dim(estimate, (1 - view_bit) * half_rows, half_rows, 0)
    got = from_partner(give, "view", 0)
    return jnp.where(
        view_bit == 0, jnp.concatenate([keep, got], axis=1), jnp.concatenate([got, keep], axis=1)
    )


def solution(mesh):
    in_specs = (P(("timepoin", "view"), "tile", None), P(), P(("timepoin", "view"), None))
    out_specs = P(("timepoin", "view"), "tile", None)
    return jax.shard_map(local, mesh=mesh, in_specs=in_specs, out_specs=out_specs, check_vma=False)
```

```python
import jax
import jax.numpy as jnp
from jax import lax
from jax.sharding import PartitionSpec as P

BX = 4
ITERS = 2


def shifted(block, axis, distance):
    devices = range(lax.axis_size(axis))
    route = [(i - distance, i) for i in devices if i - distance in devices]
    return lax.ppermute(block, axis, route)


def from_partner(block, axis, distance):
    count = lax.axis_size(axis)
    route = []
    for low in range(count):
        high = low | 1 << distance
        if high != low and high < count:
            route += [(low, high), (high, low)]
    return lax.ppermute(block, axis, route)


def extended_2(block, sides, width):
    for axis, dim in sides:
        count = lax.axis_size(axis)
        forward = [(i, i + 1) for i in range(count - 1)]
        backward = [(target, source) for source, target in forward]
        low = lax.ppermute(
            lax.slice_in_dim(block, block.shape[dim] - width, None, axis=dim), axis, forward
        )
        high = lax.ppermute(lax.slice_in_dim(block, 0, width, axis=dim), axis, backward)
        block = jnp.concatenate([low, block, high], axis=dim)
    return block


def band_matrix(kernel, row_count, col_count, base_shift):
    row_ids = lax.broadcasted_iota(jnp.int32, (row_count, col_count, 1), 0)
    col_ids = lax.broadcasted_iota(jnp.int32, (row_count, col_count, 1), 1)
    tap_ids = lax.broadcasted_iota(jnp.int32, (1, 1, kernel.shape[0]), 2)
    hit = row_ids - col_ids + base_shift == tap_ids
    taps = kernel.astype(jnp.float32)[None, None, :]
    matrix = jnp.sum(jnp.where(hit, taps, jnp.float32(0.0)), axis=2)
    return matrix.astype(jnp.bfloat16)


def operators(kernels, plane_count, width_x, width_y):
    reach = kernels.shape[1] // 2
    along_x = band_matrix(kernels[0], width_x + 2 * reach, width_x, 0).T
    along_x = jnp.broadcast_to(along_x[None], (plane_count,) + along_x.shape)
    return lax.optimization_barrier((
        along_x,
        band_matrix(kernels[1], width_y, width_y, reach),
        band_matrix(kernels[2], plane_count + 2 * reach, plane_count, 0).T,
    ))


def pass_xy(extended, matrices):
    width_y = extended.shape[2]
    after_x = jnp.einsum(
        "zpa,zay->zpy", matrices[0], extended, preferred_element_type=jnp.float32
    ).astype(jnp.bfloat16)
    after_y = jnp.dot(after_x.reshape(-1, width_y), matrices[1], preferred_element_type=jnp.float32)
    return after_y.reshape(after_x.shape).astype(jnp.bfloat16)


def pass_z(extended, matrix):
    planes = extended.shape[0]
    out = jnp.dot(matrix, extended.reshape(planes, -1), preferred_element_type=jnp.float32)
    return out.reshape((matrix.shape[0],) + extended.shape[1:])


def stacked_operators(kernels, plane_count, width_x, width_y):
    reach = kernels.shape[2] // 2
    views = range(kernels.shape[0])
    along_x = jnp.stack([band_matrix(kernels[v, 0], width_x + 2 * reach, width_x, 0).T for v in views])
    along_x = jnp.broadcast_to(along_x[:, None], (along_x.shape[0], plane_count) + along_x.shape[1:])
    return lax.optimization_barrier((
        along_x,
        jnp.stack([band_matrix(kernels[v, 1], width_y, width_y, reach) for v in views]),
        jnp.stack([band_matrix(kernels[v, 2], plane_count + 2 * reach, plane_count, 0).T for v in views]),
    ))


def pass_y_views(after_x, matrices):
    shape = after_x.shape
    flat = after_x.reshape(shape[0], -1, shape[-1])
    after_y = jnp.einsum("vmy,vyq->vmq", flat, matrices, preferred_element_type=jnp.float32)
    return after_y.reshape(shape).astype(jnp.bfloat16)


def pass_z_views(after_y, matrices, reach):
    below, above = z_rims(after_y, reach, 1)
    widened = jnp.concatenate([below, after_y, above], axis=1)
    return jnp.einsum("vpa,vaxy->vpxy", matrices, widened, preferred_element_type=jnp.float32)


def z_rims(volume, reach, axis):
    slabs = lax.axis_size("view") // 2
    slab = lax.axis_index("view") // 2
    planes = volume.shape[axis]
    shape = list(volume.shape)
    shape[axis] = reach
    below = jnp.zeros(shape, volume.dtype)
    above = below
    for phase in (0, 1):
        route = []
        for low in range(phase, slabs - 1, 2):
            for bit in (0, 1):
                route += [(2 * low + bit, 2 * low + 2 + bit), (2 * low + 2 + bit, 2 * low + bit)]
        if not route:
            continue
        is_lower = slab % 2 == phase
        start = jnp.where(is_lower, planes - reach, 0)
        payload = lax.dynamic_slice_in_dim(volume, start, reach, axis)
        got = lax.ppermute(payload, "view", route)
        below = jnp.where(is_lower, below, got)
        above = jnp.where(is_lower, got, above)
    return below, above


def x_rims(block, reach, axis, across=None):
    tiles = lax.axis_size("tile")
    views = lax.axis_size("view")
    route = []
    for tile in range(tiles - 1):
        for slab in range(views // 2):
            right_core = tile * views + 2 * slab + 1
            left_core = (tile + 1) * views + 2 * slab
            route += [(right_core, left_core), (left_core, right_core)]
    first = lax.axis_index("view") % 2 == 0
    width = block.shape[axis]
    outward = lax.dynamic_slice_in_dim(block, jnp.where(first, 0, width - reach), reach, axis)
    inward = lax.dynamic_slice_in_dim(block, jnp.where(first, width - reach, 0), reach, axis)
    if across is None:
        across = lax.ppermute(outward, ("tile", "view"), route)
    beside = from_partner(inward, "view", 0)
    low = jnp.where(first, across, beside)
    high = jnp.where(first, beside, across)
    return low, high


def local(acquired, psf_taps, block_source):
    planes, width_x, width_y = acquired.shape
    block_count = width_x // BX
    capacity = block_count // 2
    reach = psf_taps.shape[2] // 2
    tile_index = lax.axis_index("tile")
    tile_total = lax.axis_size("tile")
    view_bit = lax.axis_index("view") % 2
    sources = block_source[0]
    blocks = acquired.reshape(planes, block_count, BX, width_y)
    half_x = width_x // 2
    half_rows = planes // 2
    half_blocks = block_count // 2
    first = view_bit == 0
    starts = []
    for target, half in ((tile_index, 0), (tile_index, 1), (tile_index + 1, 0), (tile_index - 1, 1)):
        target = jnp.clip(target, 0, tile_total - 1)
        starts.append(target * block_count + half * half_blocks)
    slots = jnp.concatenate([lax.dynamic_slice_in_dim(sources, st, half_blocks) for st in starts])
    picked = jnp.take(blocks, slots % block_count, axis=1)
    mine = (slots // block_count == tile_index)[None, :, None, None]
    partials = jnp.where(mine, picked, jnp.zeros((), picked.dtype))
    partials = partials.reshape(planes, 4, half_x, width_y)
    own_keep = jnp.where(first, partials[:, 0], partials[:, 1])
    own_give = jnp.where(first, partials[:, 1], partials[:, 0])
    cross_keep = jnp.where(first, partials[:, 3], partials[:, 2])
    cross_pass = jnp.where(first, partials[:, 2], partials[:, 3])
    got = from_partner(jnp.stack([own_give, cross_pass]), "view", 0)
    tiles = lax.axis_size("tile")
    views = lax.axis_size("view")
    route = []
    for tile in range(tiles - 1):
        for slab in range(views // 2):
            right_core = tile * views + 2 * slab + 1
            left_core = (tile + 1) * views + 2 * slab
            route += [(right_core, left_core), (left_core, right_core)]
    outgoing = jnp.where(first, jnp.stack([cross_keep, got[1]]), jnp.stack([got[1], cross_keep]))
    outgoing, psf_taps = lax.optimization_barrier((outgoing, psf_taps))
    own_parts = jnp.where(first, jnp.stack([own_keep, got[0]]), jnp.stack([got[0], own_keep]))
    arrived = lax.ppermute(jnp.stack([outgoing, own_parts]), ("tile", "view"), route)
    incoming = arrived[0]
    views_measured = own_parts + incoming
    neighbour_low = (
        0.5 * ((arrived[1][0] + outgoing[0]).astype(jnp.float32) + (arrived[1][1] + outgoing[1]).astype(jnp.float32))
    ).astype(jnp.bfloat16)
    has_neighbour = jnp.where(first, tile_index > 0, tile_index < tile_total - 1)
    across_first = jnp.where(
        has_neighbour,
        lax.dynamic_slice_in_dim(neighbour_low, jnp.where(first, 1, 0), reach, 1),
        jnp.zeros((), neighbour_low.dtype),
    )
    observed = views_measured.astype(jnp.float32)
    estimate = 0.5 * (observed[0] + observed[1])
    kernels = (psf_taps / jnp.sum(psf_taps, axis=2, keepdims=True)).astype(jnp.bfloat16)
    view_count = kernels.shape[0]
    forward_ops = stacked_operators(kernels, planes, half_x, width_y)
    adjoint_ops = stacked_operators(kernels[:, :, ::-1], planes, half_x, width_y)
    for iteration in range(ITERS):
        estimate_low = estimate.astype(jnp.bfloat16)
        low, high = x_rims(estimate_low, reach, 1, across_first if iteration == 0 else None)
        extended = jnp.concatenate([low, estimate_low, high], axis=1)
        after_x = jnp.einsum(
            "vzpa,zay->vzpy", forward_ops[0], extended, preferred_element_type=jnp.float32
        ).astype(jnp.bfloat16)
        blurred = pass_z_views(pass_y_views(after_x, forward_ops[1]), forward_ops[2], reach)
        quotients = (observed / blurred).astype(jnp.bfloat16)
        low, high = x_rims(quotients, reach, 2)
        widened = jnp.concatenate([low, quotients, high], axis=2)
        after_x = jnp.einsum(
            "vzpa,vzay->vzpy", adjoint_ops[0], widened, preferred_element_type=jnp.float32
        ).astype(jnp.bfloat16)
        backs = pass_z_views(pass_y_views(after_x, adjoint_ops[1]), adjoint_ops[2], reach)
        estimate = estimate * (0.5 * (backs[0] + backs[1]))
    keep = lax.dynamic_slice_in_dim(estimate, view_bit * half_rows, half_rows, 0)
    give = lax.dynamic_slice_in_dim(estimate, (1 - view_bit) * half_rows, half_rows, 0)
    got = from_partner(give, "view", 0)
    return jnp.where(
        view_bit == 0, jnp.concatenate([keep, got], axis=1), jnp.concatenate([got, keep], axis=1)
    )


def solution(mesh):
    in_specs = (P(("timepoin", "view"), "tile", None), P(), P(("timepoin", "view"), None))
    out_specs = P(("timepoin", "view"), "tile", None)
    return jax.shard_map(local, mesh=mesh, in_specs=in_specs, out_specs=out_specs, check_vma=False)
```

```python
import jax
import jax.numpy as jnp
from jax import lax
from jax.sharding import PartitionSpec as P

BX = 4
ITERS = 2


def shifted(block, axis, distance):
    devices = range(lax.axis_size(axis))
    route = [(i - distance, i) for i in devices if i - distance in devices]
    return lax.ppermute(block, axis, route)


def from_partner(block, axis, distance):
    count = lax.axis_size(axis)
    route = []
    for low in range(count):
        high = low | 1 << distance
        if high != low and high < count:
            route += [(low, high), (high, low)]
    return lax.ppermute(block, axis, route)


def extended_2(block, sides, width):
    for axis, dim in sides:
        count = lax.axis_size(axis)
        forward = [(i, i + 1) for i in range(count - 1)]
        backward = [(target, source) for source, target in forward]
        low = lax.ppermute(
            lax.slice_in_dim(block, block.shape[dim] - width, None, axis=dim), axis, forward
        )
        high = lax.ppermute(lax.slice_in_dim(block, 0, width, axis=dim), axis, backward)
        block = jnp.concatenate([low, block, high], axis=dim)
    return block


def band_matrix(kernel, row_count, col_count, base_shift):
    row_ids = lax.broadcasted_iota(jnp.int32, (row_count, col_count, 1), 0)
    col_ids = lax.broadcasted_iota(jnp.int32, (row_count, col_count, 1), 1)
    tap_ids = lax.broadcasted_iota(jnp.int32, (1, 1, kernel.shape[0]), 2)
    hit = row_ids - col_ids + base_shift == tap_ids
    taps = kernel.astype(jnp.float32)[None, None, :]
    matrix = jnp.sum(jnp.where(hit, taps, jnp.float32(0.0)), axis=2)
    return matrix.astype(jnp.bfloat16)


def operators(kernels, plane_count, width_x, width_y):
    reach = kernels.shape[1] // 2
    along_x = band_matrix(kernels[0], width_x + 2 * reach, width_x, 0).T
    along_x = jnp.broadcast_to(along_x[None], (plane_count,) + along_x.shape)
    return lax.optimization_barrier((
        along_x,
        band_matrix(kernels[1], width_y, width_y, reach),
        band_matrix(kernels[2], plane_count + 2 * reach, plane_count, 0).T,
    ))


def pass_xy(extended, matrices):
    width_y = extended.shape[2]
    after_x = jnp.einsum(
        "zpa,zay->zpy", matrices[0], extended, preferred_element_type=jnp.float32
    ).astype(jnp.bfloat16)
    after_y = jnp.dot(after_x.reshape(-1, width_y), matrices[1], preferred_element_type=jnp.float32)
    return after_y.reshape(after_x.shape).astype(jnp.bfloat16)


def pass_z(extended, matrix):
    planes = extended.shape[0]
    out = jnp.dot(matrix, extended.reshape(planes, -1), preferred_element_type=jnp.float32)
    return out.reshape((matrix.shape[0],) + extended.shape[1:])


def stacked_operators(kernels, plane_count, width_x, width_y):
    reach = kernels.shape[2] // 2
    views = range(kernels.shape[0])
    along_x = jnp.stack([band_matrix(kernels[v, 0], width_x + 2 * reach, width_x, 0).T for v in views])
    along_x = jnp.broadcast_to(along_x[:, None], (along_x.shape[0], plane_count) + along_x.shape[1:])
    return lax.optimization_barrier((
        along_x,
        jnp.stack([band_matrix(kernels[v, 1], width_y, width_y, reach) for v in views]),
        jnp.stack([band_matrix(kernels[v, 2], plane_count + 2 * reach, plane_count, 0).T for v in views]),
    ))


def pass_y_views(after_x, matrices):
    shape = after_x.shape
    flat = after_x.reshape(shape[0], -1, shape[-1])
    after_y = jnp.einsum("vmy,vyq->vmq", flat, matrices, preferred_element_type=jnp.float32)
    return after_y.reshape(shape).astype(jnp.bfloat16)


def pass_z_views(after_y, matrices, reach):
    below, above = z_rims(after_y, reach, 1)
    widened = jnp.concatenate([below, after_y, above], axis=1)
    return jnp.einsum("vpa,vaxy->vpxy", matrices, widened, preferred_element_type=jnp.float32)


def z_rims(volume, reach, axis):
    slabs = lax.axis_size("view") // 2
    slab = lax.axis_index("view") // 2
    planes = volume.shape[axis]
    shape = list(volume.shape)
    shape[axis] = reach
    below = jnp.zeros(shape, volume.dtype)
    above = below
    for phase in (0, 1):
        route = []
        for low in range(phase, slabs - 1, 2):
            for bit in (0, 1):
                route += [(2 * low + bit, 2 * low + 2 + bit), (2 * low + 2 + bit, 2 * low + bit)]
        if not route:
            continue
        is_lower = slab % 2 == phase
        start = jnp.where(is_lower, planes - reach, 0)
        payload = lax.dynamic_slice_in_dim(volume, start, reach, axis)
        got = lax.ppermute(payload, "view", route)
        below = jnp.where(is_lower, below, got)
        above = jnp.where(is_lower, got, above)
    return below, above


def x_rims(block, reach, axis):
    tiles = lax.axis_size("tile")
    views = lax.axis_size("view")
    route = []
    for tile in range(tiles - 1):
        for slab in range(views // 2):
            right_core = tile * views + 2 * slab + 1
            left_core = (tile + 1) * views + 2 * slab
            route += [(right_core, left_core), (left_core, right_core)]
    first = lax.axis_index("view") % 2 == 0
    width = block.shape[axis]
    front = lax.slice_in_dim(block, 0, reach, axis=axis)
    back = lax.slice_in_dim(block, width - reach, width, axis=axis)
    outward = jnp.where(first, front, back)
    inward = jnp.where(first, back, front)
    across = lax.ppermute(outward, ("tile", "view"), route)
    beside = from_partner(inward, "view", 0)
    low = jnp.where(first, across, beside)
    high = jnp.where(first, beside, across)
    return low, high


def local(acquired, psf_taps, block_source):
    planes, width_x, width_y = acquired.shape
    block_count = width_x // BX
    capacity = block_count // 2
    reach = psf_taps.shape[2] // 2
    tile_index = lax.axis_index("tile")
    tile_total = lax.axis_size("tile")
    view_bit = lax.axis_index("view") % 2
    sources = block_source[0]
    blocks = acquired.reshape(planes, block_count, BX, width_y)
    half_x = width_x // 2
    half_rows = planes // 2
    half_blocks = block_count // 2
    first = view_bit == 0
    starts = []
    for target, half in ((tile_index, 0), (tile_index, 1), (tile_index + 1, 0), (tile_index - 1, 1)):
        target = jnp.clip(target, 0, tile_total - 1)
        starts.append(target * block_count + half * half_blocks)
    slots = jnp.concatenate([lax.dynamic_slice_in_dim(sources, st, half_blocks) for st in starts])
    picked = jnp.take(blocks, slots % block_count, axis=1)
    mine = (slots // block_count == tile_index)[None, :, None, None]
    partials = jnp.where(mine, picked, jnp.zeros((), picked.dtype))
    partials = partials.reshape(planes, 4, half_x, width_y)
    own_keep = jnp.where(first, partials[:, 0], partials[:, 1])
    own_give = jnp.where(first, partials[:, 1], partials[:, 0])
    cross_keep = jnp.where(first, partials[:, 3], partials[:, 2])
    cross_pass = jnp.where(first, partials[:, 2], partials[:, 3])
    got = from_partner(jnp.stack([own_give, cross_pass]), "view", 0)
    tiles = lax.axis_size("tile")
    views = lax.axis_size("view")
    route = []
    for tile in range(tiles - 1):
        for slab in range(views // 2):
            right_core = tile * views + 2 * slab + 1
            left_core = (tile + 1) * views + 2 * slab
            route += [(right_core, left_core), (left_core, right_core)]
    outgoing = jnp.where(first, jnp.stack([cross_keep, got[1]]), jnp.stack([got[1], cross_keep]))
    outgoing, psf_taps = lax.optimization_barrier((outgoing, psf_taps))
    incoming = lax.ppermute(outgoing, ("tile", "view"), route)
    own_parts = jnp.where(first, jnp.stack([own_keep, got[0]]), jnp.stack([got[0], own_keep]))
    views_measured = own_parts + incoming
    observed = views_measured.astype(jnp.float32)
    estimate = 0.5 * (observed[0] + observed[1])
    kernels = (psf_taps / jnp.sum(psf_taps, axis=2, keepdims=True)).astype(jnp.bfloat16)
    view_count = kernels.shape[0]
    forward_ops = stacked_operators(kernels, planes, half_x, width_y)
    adjoint_ops = stacked_operators(kernels[:, :, ::-1], planes, half_x, width_y)
    for iteration in range(ITERS):
        estimate_low = estimate.astype(jnp.bfloat16)
        low, high = x_rims(estimate_low, reach, 1)
        extended = jnp.concatenate([low, estimate_low, high], axis=1)
        after_x = jnp.einsum(
            "vzpa,zay->vzpy", forward_ops[0], extended, preferred_element_type=jnp.float32
        ).astype(jnp.bfloat16)
        blurred = pass_z_views(pass_y_views(after_x, forward_ops[1]), forward_ops[2], reach)
        quotients = (observed / blurred).astype(jnp.bfloat16)
        low, high = x_rims(quotients, reach, 2)
        widened = jnp.concatenate([low, quotients, high], axis=2)
        after_x = jnp.einsum(
            "vzpa,vzay->vzpy", adjoint_ops[0], widened, preferred_element_type=jnp.float32
        ).astype(jnp.bfloat16)
        backs = pass_z_views(pass_y_views(after_x, adjoint_ops[1]), adjoint_ops[2], reach)
        estimate = estimate * (0.5 * (backs[0] + backs[1]))
    keep = lax.dynamic_slice_in_dim(estimate, view_bit * half_rows, half_rows, 0)
    give = lax.dynamic_slice_in_dim(estimate, (1 - view_bit) * half_rows, half_rows, 0)
    got = from_partner(give, "view", 0)
    first_half = jnp.where(view_bit == 0, keep, got)
    second_half = jnp.where(view_bit == 0, got, keep)
    return jnp.concatenate([first_half, second_half], axis=1)


def solution(mesh):
    in_specs = (P(("timepoin", "view"), "tile", None), P(), P(("timepoin", "view"), None))
    out_specs = P(("timepoin", "view"), "tile", None)
    return jax.shard_map(local, mesh=mesh, in_specs=in_specs, out_specs=out_specs, check_vma=False)
```

```python
import jax
import jax.numpy as jnp
from jax import lax
from jax.sharding import PartitionSpec as P

BX = 4
ITERS = 2


def shifted(block, axis, distance):
    devices = range(lax.axis_size(axis))
    route = [(i - distance, i) for i in devices if i - distance in devices]
    return lax.ppermute(block, axis, route)


def from_partner(block, axis, distance):
    count = lax.axis_size(axis)
    route = []
    for low in range(count):
        high = low | 1 << distance
        if high != low and high < count:
            route += [(low, high), (high, low)]
    return lax.ppermute(block, axis, route)


def extended_2(block, sides, width):
    for axis, dim in sides:
        count = lax.axis_size(axis)
        forward = [(i, i + 1) for i in range(count - 1)]
        backward = [(target, source) for source, target in forward]
        low = lax.ppermute(
            lax.slice_in_dim(block, block.shape[dim] - width, None, axis=dim), axis, forward
        )
        high = lax.ppermute(lax.slice_in_dim(block, 0, width, axis=dim), axis, backward)
        block = jnp.concatenate([low, block, high], axis=dim)
    return block


def band_matrix(kernel, row_count, col_count, base_shift):
    row_ids = lax.broadcasted_iota(jnp.int32, (row_count, col_count, 1), 0)
    col_ids = lax.broadcasted_iota(jnp.int32, (row_count, col_count, 1), 1)
    tap_ids = lax.broadcasted_iota(jnp.int32, (1, 1, kernel.shape[0]), 2)
    hit = row_ids - col_ids + base_shift == tap_ids
    taps = kernel.astype(jnp.float32)[None, None, :]
    matrix = jnp.sum(jnp.where(hit, taps, jnp.float32(0.0)), axis=2)
    return matrix.astype(jnp.bfloat16)


def operators(kernels, plane_count, width_x, width_y):
    reach = kernels.shape[1] // 2
    along_x = band_matrix(kernels[0], width_x + 2 * reach, width_x, 0).T
    along_x = jnp.broadcast_to(along_x[None], (plane_count,) + along_x.shape)
    return lax.optimization_barrier((
        along_x,
        band_matrix(kernels[1], width_y, width_y, reach),
        band_matrix(kernels[2], plane_count + 2 * reach, plane_count, 0).T,
    ))


def pass_xy(extended, matrices):
    width_y = extended.shape[2]
    after_x = jnp.einsum(
        "zpa,zay->zpy", matrices[0], extended, preferred_element_type=jnp.float32
    ).astype(jnp.bfloat16)
    after_y = jnp.dot(after_x.reshape(-1, width_y), matrices[1], preferred_element_type=jnp.float32)
    return after_y.reshape(after_x.shape).astype(jnp.bfloat16)


def pass_z(extended, matrix):
    planes = extended.shape[0]
    out = jnp.dot(matrix, extended.reshape(planes, -1), preferred_element_type=jnp.float32)
    return out.reshape((matrix.shape[0],) + extended.shape[1:])


def stacked_operators(kernels, plane_count, width_x, width_y):
    reach = kernels.shape[2] // 2
    views = range(kernels.shape[0])
    along_x = jnp.stack([band_matrix(kernels[v, 0], width_x + 2 * reach, width_x, 0).T for v in views])
    along_x = jnp.broadcast_to(along_x[:, None], (along_x.shape[0], plane_count) + along_x.shape[1:])
    return lax.optimization_barrier((
        along_x,
        jnp.stack([band_matrix(kernels[v, 1], width_y, width_y, reach) for v in views]),
        jnp.stack([band_matrix(kernels[v, 2], plane_count + 2 * reach, plane_count, 0).T for v in views]),
    ))


def pass_y_views(after_x, matrices):
    shape = after_x.shape
    flat = after_x.reshape(shape[0], -1, shape[-1])
    after_y = jnp.einsum("vmy,vyq->vmq", flat, matrices, preferred_element_type=jnp.float32)
    return after_y.reshape(shape).astype(jnp.bfloat16)


def pass_z_views(after_y, matrices, reach):
    below, above = z_rims(after_y, reach, 1)
    widened = jnp.concatenate([below, after_y, above], axis=1)
    return jnp.einsum("vpa,vaxy->vpxy", matrices, widened, preferred_element_type=jnp.float32)


def z_rims(volume, reach, axis):
    slabs = lax.axis_size("view") // 2
    slab = lax.axis_index("view") // 2
    planes = volume.shape[axis]
    shape = list(volume.shape)
    shape[axis] = reach
    below = jnp.zeros(shape, volume.dtype)
    above = below
    for phase in (0, 1):
        route = []
        for low in range(phase, slabs - 1, 2):
            for bit in (0, 1):
                route += [(2 * low + bit, 2 * low + 2 + bit), (2 * low + 2 + bit, 2 * low + bit)]
        if not route:
            continue
        is_lower = slab % 2 == phase
        start = jnp.where(is_lower, planes - reach, 0)
        payload = lax.dynamic_slice_in_dim(volume, start, reach, axis)
        got = lax.ppermute(payload, "view", route)
        below = jnp.where(is_lower, below, got)
        above = jnp.where(is_lower, got, above)
    return below, above


def x_rims(block, reach, axis):
    tiles = lax.axis_size("tile")
    views = lax.axis_size("view")
    route = []
    for tile in range(tiles - 1):
        for slab in range(views // 2):
            right_core = tile * views + 2 * slab + 1
            left_core = (tile + 1) * views + 2 * slab
            route += [(right_core, left_core), (left_core, right_core)]
    first = lax.axis_index("view") % 2 == 0
    width = block.shape[axis]
    front = lax.slice_in_dim(block, 0, reach, axis=axis)
    back = lax.slice_in_dim(block, width - reach, width, axis=axis)
    outward = jnp.where(first, front, back)
    inward = jnp.where(first, back, front)
    across = lax.ppermute(outward, ("tile", "view"), route)
    beside = from_partner(inward, "view", 0)
    low = jnp.where(first, across, beside)
    high = jnp.where(first, beside, across)
    return low, high


def local(acquired, psf_taps, block_source):
    planes, width_x, width_y = acquired.shape
    block_count = width_x // BX
    capacity = block_count // 2
    reach = psf_taps.shape[2] // 2
    tile_index = lax.axis_index("tile")
    tile_total = lax.axis_size("tile")
    view_bit = lax.axis_index("view") % 2
    sources = block_source[0]
    blocks = acquired.reshape(planes, block_count, BX, width_y)
    half_x = width_x // 2
    half_rows = planes // 2
    half_blocks = block_count // 2
    first = view_bit == 0
    starts = []
    for target, half in ((tile_index, 0), (tile_index, 1), (tile_index + 1, 0), (tile_index - 1, 1)):
        target = jnp.clip(target, 0, tile_total - 1)
        starts.append(target * block_count + half * half_blocks)
    slots = jnp.concatenate([lax.dynamic_slice_in_dim(sources, st, half_blocks) for st in starts])
    row_ids = jnp.arange(slots.shape[0] * BX, dtype=jnp.int32)
    row_slots = slots[row_ids // BX]
    source_x = (row_slots % block_count) * BX + row_ids % BX
    chosen_rows = (row_slots // block_count == tile_index)[:, None] & (
        source_x[:, None] == jnp.arange(width_x, dtype=jnp.int32)[None, :]
    )
    selection = jnp.broadcast_to(chosen_rows.astype(acquired.dtype)[None], (planes,) + chosen_rows.shape)
    partials = jnp.einsum(
        "zrx,zxy->zry", selection, acquired, preferred_element_type=jnp.float32
    ).astype(acquired.dtype)
    partials = partials.reshape(planes, 4, half_x, width_y)
    own_keep = jnp.where(first, partials[:, 0], partials[:, 1])
    own_give = jnp.where(first, partials[:, 1], partials[:, 0])
    cross_keep = jnp.where(first, partials[:, 3], partials[:, 2])
    cross_pass = jnp.where(first, partials[:, 2], partials[:, 3])
    got = from_partner(jnp.stack([own_give, cross_pass]), "view", 0)
    tiles = lax.axis_size("tile")
    views = lax.axis_size("view")
    route = []
    for tile in range(tiles - 1):
        for slab in range(views // 2):
            right_core = tile * views + 2 * slab + 1
            left_core = (tile + 1) * views + 2 * slab
            route += [(right_core, left_core), (left_core, right_core)]
    outgoing = jnp.where(first, jnp.stack([cross_keep, got[1]]), jnp.stack([got[1], cross_keep]))
    outgoing, psf_taps = lax.optimization_barrier((outgoing, psf_taps))
    incoming = lax.ppermute(outgoing, ("tile", "view"), route)
    own_parts = jnp.where(first, jnp.stack([own_keep, got[0]]), jnp.stack([got[0], own_keep]))
    views_measured = own_parts + incoming
    observed = views_measured.astype(jnp.float32)
    estimate = 0.5 * (observed[0] + observed[1])
    kernels = (psf_taps / jnp.sum(psf_taps, axis=2, keepdims=True)).astype(jnp.bfloat16)
    view_count = kernels.shape[0]
    forward_ops = stacked_operators(kernels, planes, half_x, width_y)
    adjoint_ops = stacked_operators(kernels[:, :, ::-1], planes, half_x, width_y)
    for iteration in range(ITERS):
        estimate_low = estimate.astype(jnp.bfloat16)
        low, high = x_rims(estimate_low, reach, 1)
        extended = jnp.concatenate([low, estimate_low, high], axis=1)
        after_x = jnp.einsum(
            "vzpa,zay->vzpy", forward_ops[0], extended, preferred_element_type=jnp.float32
        ).astype(jnp.bfloat16)
        blurred = pass_z_views(pass_y_views(after_x, forward_ops[1]), forward_ops[2], reach)
        quotients = (observed / blurred).astype(jnp.bfloat16)
        low, high = x_rims(quotients, reach, 2)
        widened = jnp.concatenate([low, quotients, high], axis=2)
        after_x = jnp.einsum(
            "vzpa,vzay->vzpy", adjoint_ops[0], widened, preferred_element_type=jnp.float32
        ).astype(jnp.bfloat16)
        backs = pass_z_views(pass_y_views(after_x, adjoint_ops[1]), adjoint_ops[2], reach)
        estimate = estimate * (0.5 * (backs[0] + backs[1]))
    keep = lax.dynamic_slice_in_dim(estimate, view_bit * half_rows, half_rows, 0)
    give = lax.dynamic_slice_in_dim(estimate, (1 - view_bit) * half_rows, half_rows, 0)
    got = from_partner(give, "view", 0)
    first_half = jnp.where(view_bit == 0, keep, got)
    second_half = jnp.where(view_bit == 0, got, keep)
    return jnp.concatenate([first_half, second_half], axis=1)


def solution(mesh):
    in_specs = (P(("timepoin", "view"), "tile", None), P(), P(("timepoin", "view"), None))
    out_specs = P(("timepoin", "view"), "tile", None)
    return jax.shard_map(local, mesh=mesh, in_specs=in_specs, out_specs=out_specs, check_vma=False)
```

```python
import jax
import jax.numpy as jnp
from jax import lax
from jax.sharding import PartitionSpec as P

BX = 4
ITERS = 2


def shifted(block, axis, distance):
    devices = range(lax.axis_size(axis))
    route = [(i - distance, i) for i in devices if i - distance in devices]
    return lax.ppermute(block, axis, route)


def from_partner(block, axis, distance):
    count = lax.axis_size(axis)
    route = []
    for low in range(count):
        high = low | 1 << distance
        if high != low and high < count:
            route += [(low, high), (high, low)]
    return lax.ppermute(block, axis, route)


def extended_2(block, sides, width):
    for axis, dim in sides:
        count = lax.axis_size(axis)
        forward = [(i, i + 1) for i in range(count - 1)]
        backward = [(target, source) for source, target in forward]
        low = lax.ppermute(
            lax.slice_in_dim(block, block.shape[dim] - width, None, axis=dim), axis, forward
        )
        high = lax.ppermute(lax.slice_in_dim(block, 0, width, axis=dim), axis, backward)
        block = jnp.concatenate([low, block, high], axis=dim)
    return block


def band_matrix(kernel, row_count, col_count, base_shift):
    row_ids = lax.broadcasted_iota(jnp.int32, (row_count, col_count, 1), 0)
    col_ids = lax.broadcasted_iota(jnp.int32, (row_count, col_count, 1), 1)
    tap_ids = lax.broadcasted_iota(jnp.int32, (1, 1, kernel.shape[0]), 2)
    hit = row_ids - col_ids + base_shift == tap_ids
    taps = kernel.astype(jnp.float32)[None, None, :]
    matrix = jnp.sum(jnp.where(hit, taps, jnp.float32(0.0)), axis=2)
    return matrix.astype(jnp.bfloat16)


def operators(kernels, plane_count, width_x, width_y):
    reach = kernels.shape[1] // 2
    along_x = band_matrix(kernels[0], width_x + 2 * reach, width_x, 0).T
    along_x = jnp.broadcast_to(along_x[None], (plane_count,) + along_x.shape)
    return lax.optimization_barrier((
        along_x,
        band_matrix(kernels[1], width_y, width_y, reach),
        band_matrix(kernels[2], plane_count + 2 * reach, plane_count, 0).T,
    ))


def pass_xy(extended, matrices):
    width_y = extended.shape[2]
    after_x = jnp.einsum(
        "zpa,zay->zpy", matrices[0], extended, preferred_element_type=jnp.float32
    ).astype(jnp.bfloat16)
    after_y = jnp.dot(after_x.reshape(-1, width_y), matrices[1], preferred_element_type=jnp.float32)
    return after_y.reshape(after_x.shape).astype(jnp.bfloat16)


def pass_z(extended, matrix):
    planes = extended.shape[0]
    out = jnp.dot(matrix, extended.reshape(planes, -1), preferred_element_type=jnp.float32)
    return out.reshape((matrix.shape[0],) + extended.shape[1:])


def stacked_operators(kernels, plane_count, width_x, width_y):
    reach = kernels.shape[2] // 2
    views = range(kernels.shape[0])
    along_x = jnp.stack([band_matrix(kernels[v, 0], width_x + 2 * reach, width_x, 0).T for v in views])
    along_x = jnp.broadcast_to(along_x[:, None], (along_x.shape[0], plane_count) + along_x.shape[1:])
    return lax.optimization_barrier((
        along_x,
        jnp.stack([band_matrix(kernels[v, 1], width_y, width_y, reach) for v in views]),
        jnp.stack([band_matrix(kernels[v, 2], plane_count + 2 * reach, plane_count, 0).T for v in views]),
    ))


def pass_y_views(after_x, matrices):
    shape = after_x.shape
    flat = after_x.reshape(shape[0], -1, shape[-1])
    after_y = jnp.einsum("vmy,vyq->vmq", flat, matrices, preferred_element_type=jnp.float32)
    return after_y.reshape(shape).astype(jnp.bfloat16)


def pass_z_views(after_y, matrices, reach):
    below, above = z_rims(after_y, reach, 1)
    widened = jnp.concatenate([below, after_y, above], axis=1)
    return jnp.einsum("vpa,vaxy->vpxy", matrices, widened, preferred_element_type=jnp.float32)


def z_rims(volume, reach, axis):
    slabs = lax.axis_size("view") // 2
    slab = lax.axis_index("view") // 2
    planes = volume.shape[axis]
    shape = list(volume.shape)
    shape[axis] = reach
    below = jnp.zeros(shape, volume.dtype)
    above = below
    for phase in (0, 1):
        route = []
        for low in range(phase, slabs - 1, 2):
            for bit in (0, 1):
                route += [(2 * low + bit, 2 * low + 2 + bit), (2 * low + 2 + bit, 2 * low + bit)]
        if not route:
            continue
        is_lower = slab % 2 == phase
        start = jnp.where(is_lower, planes - reach, 0)
        payload = lax.dynamic_slice_in_dim(volume, start, reach, axis)
        got = lax.ppermute(payload, "view", route)
        below = jnp.where(is_lower, below, got)
        above = jnp.where(is_lower, got, above)
    return below, above


def x_rims(block, reach, axis):
    tiles = lax.axis_size("tile")
    views = lax.axis_size("view")
    route = []
    for tile in range(tiles - 1):
        for slab in range(views // 2):
            right_core = tile * views + 2 * slab + 1
            left_core = (tile + 1) * views + 2 * slab
            route += [(right_core, left_core), (left_core, right_core)]
    first = lax.axis_index("view") % 2 == 0
    width = block.shape[axis]
    front = lax.slice_in_dim(block, 0, reach, axis=axis)
    back = lax.slice_in_dim(block, width - reach, width, axis=axis)
    outward = jnp.where(first, front, back)
    inward = jnp.where(first, back, front)
    across = lax.ppermute(outward, ("tile", "view"), route)
    beside = from_partner(inward, "view", 0)
    low = jnp.where(first, across, beside)
    high = jnp.where(first, beside, across)
    return low, high


def local(acquired, psf_taps, block_source):
    planes, width_x, width_y = acquired.shape
    block_count = width_x // BX
    capacity = block_count // 2
    reach = psf_taps.shape[2] // 2
    tile_index = lax.axis_index("tile")
    tile_total = lax.axis_size("tile")
    view_bit = lax.axis_index("view") % 2
    sources = block_source[0]
    blocks = acquired.reshape(planes, block_count, BX, width_y)
    half_x = width_x // 2
    half_rows = planes // 2
    half_blocks = block_count // 2
    first = view_bit == 0
    table = jnp.pad(sources.reshape(tile_total, block_count), ((1, 1), (0, 0)))
    near = lax.dynamic_slice_in_dim(table, tile_index, 3, 0)
    slots = jnp.concatenate([near[1], near[2, :half_blocks], near[0, half_blocks:]])
    row_ids = jnp.arange(slots.shape[0] * BX, dtype=jnp.int32)
    row_slots = jnp.repeat(slots, BX)
    source_x = (row_slots % block_count) * BX + row_ids % BX
    chosen_rows = (row_slots // block_count == tile_index)[:, None] & (
        source_x[:, None] == jnp.arange(width_x, dtype=jnp.int32)[None, :]
    )
    selection = jnp.broadcast_to(chosen_rows.astype(acquired.dtype)[None], (planes,) + chosen_rows.shape)
    partials = jnp.einsum(
        "zrx,zxy->zry", selection, acquired, preferred_element_type=jnp.float32
    ).astype(acquired.dtype)
    partials = partials.reshape(planes, 4, half_x, width_y)
    own_keep = jnp.where(first, partials[:, 0], partials[:, 1])
    own_give = jnp.where(first, partials[:, 1], partials[:, 0])
    cross_keep = jnp.where(first, partials[:, 3], partials[:, 2])
    cross_pass = jnp.where(first, partials[:, 2], partials[:, 3])
    got = from_partner(jnp.stack([own_give, cross_pass]), "view", 0)
    tiles = lax.axis_size("tile")
    views = lax.axis_size("view")
    route = []
    for tile in range(tiles - 1):
        for slab in range(views // 2):
            right_core = tile * views + 2 * slab + 1
            left_core = (tile + 1) * views + 2 * slab
            route += [(right_core, left_core), (left_core, right_core)]
    outgoing = jnp.where(first, jnp.stack([cross_keep, got[1]]), jnp.stack([got[1], cross_keep]))
    outgoing, psf_taps = lax.optimization_barrier((outgoing, psf_taps))
    incoming = lax.ppermute(outgoing, ("tile", "view"), route)
    own_parts = jnp.where(first, jnp.stack([own_keep, got[0]]), jnp.stack([got[0], own_keep]))
    views_measured = own_parts + incoming
    observed = views_measured.astype(jnp.float32)
    estimate = 0.5 * (observed[0] + observed[1])
    kernels = (psf_taps / jnp.sum(psf_taps, axis=2, keepdims=True)).astype(jnp.bfloat16)
    view_count = kernels.shape[0]
    forward_ops = stacked_operators(kernels, planes, half_x, width_y)
    adjoint_ops = stacked_operators(kernels[:, :, ::-1], planes, half_x, width_y)
    for iteration in range(ITERS):
        estimate_low = estimate.astype(jnp.bfloat16)
        low, high = x_rims(estimate_low, reach, 1)
        extended = jnp.concatenate([low, estimate_low, high], axis=1)
        after_x = jnp.einsum(
            "vzpa,zay->vzpy", forward_ops[0], extended, preferred_element_type=jnp.float32
        ).astype(jnp.bfloat16)
        blurred = pass_z_views(pass_y_views(after_x, forward_ops[1]), forward_ops[2], reach)
        quotients = (observed / blurred).astype(jnp.bfloat16)
        low, high = x_rims(quotients, reach, 2)
        widened = jnp.concatenate([low, quotients, high], axis=2)
        after_x = jnp.einsum(
            "vzpa,vzay->vzpy", adjoint_ops[0], widened, preferred_element_type=jnp.float32
        ).astype(jnp.bfloat16)
        backs = pass_z_views(pass_y_views(after_x, adjoint_ops[1]), adjoint_ops[2], reach)
        estimate = estimate * (0.5 * (backs[0] + backs[1]))
    keep = lax.dynamic_slice_in_dim(estimate, view_bit * half_rows, half_rows, 0)
    give = lax.dynamic_slice_in_dim(estimate, (1 - view_bit) * half_rows, half_rows, 0)
    got = from_partner(give, "view", 0)
    first_half = jnp.where(view_bit == 0, keep, got)
    second_half = jnp.where(view_bit == 0, got, keep)
    return jnp.concatenate([first_half, second_half], axis=1)


def solution(mesh):
    in_specs = (P(("timepoin", "view"), "tile", None), P(), P(("timepoin", "view"), None))
    out_specs = P(("timepoin", "view"), "tile", None)
    return jax.shard_map(local, mesh=mesh, in_specs=in_specs, out_specs=out_specs, check_vma=False)
```

```python
import jax
import jax.numpy as jnp
from jax import lax
from jax.sharding import PartitionSpec as P

BX = 4
ITERS = 2


def shifted(block, axis, distance):
    devices = range(lax.axis_size(axis))
    route = [(i - distance, i) for i in devices if i - distance in devices]
    return lax.ppermute(block, axis, route)


def from_partner(block, axis, distance):
    count = lax.axis_size(axis)
    route = []
    for low in range(count):
        high = low | 1 << distance
        if high != low and high < count:
            route += [(low, high), (high, low)]
    return lax.ppermute(block, axis, route)


def extended_2(block, sides, width):
    for axis, dim in sides:
        count = lax.axis_size(axis)
        forward = [(i, i + 1) for i in range(count - 1)]
        backward = [(target, source) for source, target in forward]
        low = lax.ppermute(
            lax.slice_in_dim(block, block.shape[dim] - width, None, axis=dim), axis, forward
        )
        high = lax.ppermute(lax.slice_in_dim(block, 0, width, axis=dim), axis, backward)
        block = jnp.concatenate([low, block, high], axis=dim)
    return block


def band_matrix(kernel, row_count, col_count, base_shift):
    row_ids = lax.broadcasted_iota(jnp.int32, (row_count, col_count, 1), 0)
    col_ids = lax.broadcasted_iota(jnp.int32, (row_count, col_count, 1), 1)
    tap_ids = lax.broadcasted_iota(jnp.int32, (1, 1, kernel.shape[0]), 2)
    hit = row_ids - col_ids + base_shift == tap_ids
    taps = kernel.astype(jnp.float32)[None, None, :]
    matrix = jnp.sum(jnp.where(hit, taps, jnp.float32(0.0)), axis=2)
    return matrix.astype(jnp.bfloat16)


def operators(kernels, plane_count, width_x, width_y):
    reach = kernels.shape[1] // 2
    along_x = band_matrix(kernels[0], width_x + 2 * reach, width_x, 0).T
    along_x = jnp.broadcast_to(along_x[None], (plane_count,) + along_x.shape)
    return lax.optimization_barrier((
        along_x,
        band_matrix(kernels[1], width_y, width_y, reach),
        band_matrix(kernels[2], plane_count + 2 * reach, plane_count, 0).T,
    ))


def pass_xy(extended, matrices):
    width_y = extended.shape[2]
    after_x = jnp.einsum(
        "zpa,zay->zpy", matrices[0], extended, preferred_element_type=jnp.float32
    ).astype(jnp.bfloat16)
    after_y = jnp.dot(after_x.reshape(-1, width_y), matrices[1], preferred_element_type=jnp.float32)
    return after_y.reshape(after_x.shape).astype(jnp.bfloat16)


def pass_z(extended, matrix):
    planes = extended.shape[0]
    out = jnp.dot(matrix, extended.reshape(planes, -1), preferred_element_type=jnp.float32)
    return out.reshape((matrix.shape[0],) + extended.shape[1:])


def stacked_operators(kernels, plane_count, width_x, width_y):
    reach = kernels.shape[2] // 2
    views = range(kernels.shape[0])
    along_x = jnp.stack([band_matrix(kernels[v, 0], width_x + 2 * reach, width_x, 0).T for v in views])
    along_x = jnp.broadcast_to(along_x[:, None], (along_x.shape[0], plane_count) + along_x.shape[1:])
    return lax.optimization_barrier((
        along_x,
        jnp.stack([band_matrix(kernels[v, 1], width_y, width_y, reach) for v in views]),
        jnp.stack([band_matrix(kernels[v, 2], plane_count + 2 * reach, plane_count, 0).T for v in views]),
    ))


def pass_y_views(after_x, matrices):
    shape = after_x.shape
    flat = after_x.reshape(shape[0], -1, shape[-1])
    after_y = jnp.einsum("vmy,vyq->vmq", flat, matrices, preferred_element_type=jnp.float32)
    return after_y.reshape(shape).astype(jnp.bfloat16)


def pass_z_views(after_y, matrices, reach):
    below, above = z_rims(after_y, reach, 1)
    widened = jnp.concatenate([below, after_y, above], axis=1)
    return jnp.einsum("vpa,vaxy->vpxy", matrices, widened, preferred_element_type=jnp.float32)


def z_rims(volume, reach, axis):
    slabs = lax.axis_size("view") // 2
    slab = lax.axis_index("view") // 2
    planes = volume.shape[axis]
    shape = list(volume.shape)
    shape[axis] = reach
    below = jnp.zeros(shape, volume.dtype)
    above = below
    for phase in (0, 1):
        route = []
        for low in range(phase, slabs - 1, 2):
            for bit in (0, 1):
                route += [(2 * low + bit, 2 * low + 2 + bit), (2 * low + 2 + bit, 2 * low + bit)]
        if not route:
            continue
        is_lower = slab % 2 == phase
        start = jnp.where(is_lower, planes - reach, 0)
        payload = lax.dynamic_slice_in_dim(volume, start, reach, axis)
        got = lax.ppermute(payload, "view", route)
        below = jnp.where(is_lower, below, got)
        above = jnp.where(is_lower, got, above)
    return below, above


def x_rims(block, reach, axis):
    tiles = lax.axis_size("tile")
    views = lax.axis_size("view")
    route = []
    for tile in range(tiles - 1):
        for slab in range(views // 2):
            right_core = tile * views + 2 * slab + 1
            left_core = (tile + 1) * views + 2 * slab
            route += [(right_core, left_core), (left_core, right_core)]
    first = lax.axis_index("view") % 2 == 0
    width = block.shape[axis]
    front = lax.slice_in_dim(block, 0, reach, axis=axis)
    back = lax.slice_in_dim(block, width - reach, width, axis=axis)
    outward = jnp.where(first, front, back)
    inward = jnp.where(first, back, front)
    across = lax.ppermute(outward, ("tile", "view"), route)
    beside = from_partner(inward, "view", 0)
    low = jnp.where(first, across, beside)
    high = jnp.where(first, beside, across)
    return low, high


def local(acquired, psf_taps, block_source):
    planes, width_x, width_y = acquired.shape
    block_count = width_x // BX
    capacity = block_count // 2
    reach = psf_taps.shape[2] // 2
    tile_index = lax.axis_index("tile")
    tile_total = lax.axis_size("tile")
    view_bit = lax.axis_index("view") % 2
    sources = block_source[0]
    blocks = acquired.reshape(planes, block_count, BX, width_y)
    half_x = width_x // 2
    half_rows = planes // 2
    half_blocks = block_count // 2
    first = view_bit == 0
    starts = []
    for target, half in ((tile_index, 0), (tile_index, 1), (tile_index + 1, 0), (tile_index - 1, 1)):
        target = jnp.clip(target, 0, tile_total - 1)
        starts.append(target * block_count + half * half_blocks)
    slots = jnp.concatenate([lax.dynamic_slice_in_dim(sources, st, half_blocks) for st in starts])
    row_ids = jnp.arange(slots.shape[0] * BX, dtype=jnp.int32)
    row_slots = slots[row_ids // BX]
    source_x = (row_slots % block_count) * BX + row_ids % BX
    chosen_rows = (row_slots // block_count == tile_index)[:, None] & (
        source_x[:, None] == jnp.arange(width_x, dtype=jnp.int32)[None, :]
    )
    selection = jnp.broadcast_to(chosen_rows.astype(acquired.dtype)[None], (planes,) + chosen_rows.shape)
    partials = jnp.einsum(
        "zrx,zxy->zry", selection, acquired, preferred_element_type=jnp.float32
    ).astype(acquired.dtype)
    partials = partials.reshape(planes, 4, half_x, width_y)
    own_keep = jnp.where(first, partials[:, 0], partials[:, 1])
    own_give = jnp.where(first, partials[:, 1], partials[:, 0])
    cross_keep = jnp.where(first, partials[:, 3], partials[:, 2])
    cross_pass = jnp.where(first, partials[:, 2], partials[:, 3])
    got_pass = from_partner(cross_pass, "view", 0)
    tiles = lax.axis_size("tile")
    views = lax.axis_size("view")
    route = []
    for tile in range(tiles - 1):
        for slab in range(views // 2):
            right_core = tile * views + 2 * slab + 1
            left_core = (tile + 1) * views + 2 * slab
            route += [(right_core, left_core), (left_core, right_core)]
    outgoing = jnp.where(first, jnp.stack([cross_keep, got_pass]), jnp.stack([got_pass, cross_keep]))
    outgoing, psf_taps, own_give = lax.optimization_barrier((outgoing, psf_taps, own_give))
    incoming = lax.ppermute(outgoing, ("tile", "view"), route)
    got_own = from_partner(own_give, "view", 0)
    own_parts = jnp.where(first, jnp.stack([own_keep, got_own]), jnp.stack([got_own, own_keep]))
    views_measured = own_parts + incoming
    observed = views_measured.astype(jnp.float32)
    estimate = 0.5 * (observed[0] + observed[1])
    kernels = (psf_taps / jnp.sum(psf_taps, axis=2, keepdims=True)).astype(jnp.bfloat16)
    view_count = kernels.shape[0]
    forward_ops = stacked_operators(kernels, planes, half_x, width_y)
    adjoint_ops = stacked_operators(kernels[:, :, ::-1], planes, half_x, width_y)
    for iteration in range(ITERS):
        estimate_low = estimate.astype(jnp.bfloat16)
        low, high = x_rims(estimate_low, reach, 1)
        extended = jnp.concatenate([low, estimate_low, high], axis=1)
        after_x = jnp.einsum(
            "vzpa,zay->vzpy", forward_ops[0], extended, preferred_element_type=jnp.float32
        ).astype(jnp.bfloat16)
        blurred = pass_z_views(pass_y_views(after_x, forward_ops[1]), forward_ops[2], reach)
        quotients = (observed / blurred).astype(jnp.bfloat16)
        low, high = x_rims(quotients, reach, 2)
        widened = jnp.concatenate([low, quotients, high], axis=2)
        after_x = jnp.einsum(
            "vzpa,vzay->vzpy", adjoint_ops[0], widened, preferred_element_type=jnp.float32
        ).astype(jnp.bfloat16)
        backs = pass_z_views(pass_y_views(after_x, adjoint_ops[1]), adjoint_ops[2], reach)
        estimate = estimate * (0.5 * (backs[0] + backs[1]))
    keep = lax.dynamic_slice_in_dim(estimate, view_bit * half_rows, half_rows, 0)
    give = lax.dynamic_slice_in_dim(estimate, (1 - view_bit) * half_rows, half_rows, 0)
    got = from_partner(give, "view", 0)
    first_half = jnp.where(view_bit == 0, keep, got)
    second_half = jnp.where(view_bit == 0, got, keep)
    return jnp.concatenate([first_half, second_half], axis=1)


def solution(mesh):
    in_specs = (P(("timepoin", "view"), "tile", None), P(), P(("timepoin", "view"), None))
    out_specs = P(("timepoin", "view"), "tile", None)
    return jax.shard_map(local, mesh=mesh, in_specs=in_specs, out_specs=out_specs, check_vma=False)
```

```python
import jax
import jax.numpy as jnp
from jax import lax
from jax.sharding import PartitionSpec as P

BX = 4
ITERS = 2


def shifted(block, axis, distance):
    devices = range(lax.axis_size(axis))
    route = [(i - distance, i) for i in devices if i - distance in devices]
    return lax.ppermute(block, axis, route)


def from_partner(block, axis, distance):
    count = lax.axis_size(axis)
    route = []
    for low in range(count):
        high = low | 1 << distance
        if high != low and high < count:
            route += [(low, high), (high, low)]
    return lax.ppermute(block, axis, route)


def extended_2(block, sides, width):
    for axis, dim in sides:
        count = lax.axis_size(axis)
        forward = [(i, i + 1) for i in range(count - 1)]
        backward = [(target, source) for source, target in forward]
        low = lax.ppermute(
            lax.slice_in_dim(block, block.shape[dim] - width, None, axis=dim), axis, forward
        )
        high = lax.ppermute(lax.slice_in_dim(block, 0, width, axis=dim), axis, backward)
        block = jnp.concatenate([low, block, high], axis=dim)
    return block


def band_matrix(kernel, row_count, col_count, base_shift):
    row_ids = lax.broadcasted_iota(jnp.int32, (row_count, col_count, 1), 0)
    col_ids = lax.broadcasted_iota(jnp.int32, (row_count, col_count, 1), 1)
    tap_ids = lax.broadcasted_iota(jnp.int32, (1, 1, kernel.shape[0]), 2)
    hit = row_ids - col_ids + base_shift == tap_ids
    taps = kernel.astype(jnp.float32)[None, None, :]
    matrix = jnp.sum(jnp.where(hit, taps, jnp.float32(0.0)), axis=2)
    return matrix.astype(jnp.bfloat16)


def operators(kernels, plane_count, width_x, width_y):
    reach = kernels.shape[1] // 2
    along_x = band_matrix(kernels[0], width_x + 2 * reach, width_x, 0).T
    along_x = jnp.broadcast_to(along_x[None], (plane_count,) + along_x.shape)
    return lax.optimization_barrier((
        along_x,
        band_matrix(kernels[1], width_y, width_y, reach),
        band_matrix(kernels[2], plane_count + 2 * reach, plane_count, 0).T,
    ))


def pass_xy(extended, matrices):
    width_y = extended.shape[2]
    after_x = jnp.einsum(
        "zpa,zay->zpy", matrices[0], extended, preferred_element_type=jnp.float32
    ).astype(jnp.bfloat16)
    after_y = jnp.dot(after_x.reshape(-1, width_y), matrices[1], preferred_element_type=jnp.float32)
    return after_y.reshape(after_x.shape).astype(jnp.bfloat16)


def pass_z(extended, matrix):
    planes = extended.shape[0]
    out = jnp.dot(matrix, extended.reshape(planes, -1), preferred_element_type=jnp.float32)
    return out.reshape((matrix.shape[0],) + extended.shape[1:])


def stacked_operators(kernels, plane_count, width_x, width_y):
    reach = kernels.shape[2] // 2
    views = range(kernels.shape[0])
    along_x = jnp.stack([band_matrix(kernels[v, 0], width_x + 2 * reach, width_x, 0).T for v in views])
    along_x = jnp.broadcast_to(along_x[:, None], (along_x.shape[0], plane_count) + along_x.shape[1:])
    return lax.optimization_barrier((
        along_x,
        jnp.stack([band_matrix(kernels[v, 1], width_y, width_y, reach) for v in views]),
        jnp.stack([band_matrix(kernels[v, 2], plane_count + 2 * reach, plane_count, 0).T for v in views]),
    ))


def pass_y_views(after_x, matrices):
    shape = after_x.shape
    flat = after_x.reshape(shape[0], -1, shape[-1])
    after_y = jnp.einsum("vmy,vyq->vmq", flat, matrices, preferred_element_type=jnp.float32)
    return after_y.reshape(shape).astype(jnp.bfloat16)


def pass_z_views(after_y, matrices, reach):
    below, above = z_rims(after_y, reach, 1)
    widened = jnp.concatenate([below, after_y, above], axis=1)
    return jnp.einsum("vpa,vaxy->vpxy", matrices, widened, preferred_element_type=jnp.float32)


def z_rims(volume, reach, axis):
    slabs = lax.axis_size("view") // 2
    slab = lax.axis_index("view") // 2
    planes = volume.shape[axis]
    shape = list(volume.shape)
    shape[axis] = reach
    below = jnp.zeros(shape, volume.dtype)
    above = below
    for phase in (0, 1):
        route = []
        for low in range(phase, slabs - 1, 2):
            for bit in (0, 1):
                route += [(2 * low + bit, 2 * low + 2 + bit), (2 * low + 2 + bit, 2 * low + bit)]
        if not route:
            continue
        is_lower = slab % 2 == phase
        start = jnp.where(is_lower, planes - reach, 0)
        payload = lax.dynamic_slice_in_dim(volume, start, reach, axis)
        got = lax.ppermute(payload, "view", route)
        below = jnp.where(is_lower, below, got)
        above = jnp.where(is_lower, got, above)
    return below, above


def x_rims(block, reach, axis):
    tiles = lax.axis_size("tile")
    views = lax.axis_size("view")
    route = []
    for tile in range(tiles - 1):
        for slab in range(views // 2):
            right_core = tile * views + 2 * slab + 1
            left_core = (tile + 1) * views + 2 * slab
            route += [(right_core, left_core), (left_core, right_core)]
    first = lax.axis_index("view") % 2 == 0
    width = block.shape[axis]
    across = lax.ppermute(block, ("tile", "view"), route)
    beside = from_partner(block, "view", 0)
    low = lax.slice_in_dim(jnp.where(first, across, beside), width - reach, width, axis=axis)
    high = lax.slice_in_dim(jnp.where(first, beside, across), 0, reach, axis=axis)
    return low, high


def local(acquired, psf_taps, block_source):
    planes, width_x, width_y = acquired.shape
    block_count = width_x // BX
    capacity = block_count // 2
    reach = psf_taps.shape[2] // 2
    tile_index = lax.axis_index("tile")
    tile_total = lax.axis_size("tile")
    view_bit = lax.axis_index("view") % 2
    sources = block_source[0]
    blocks = acquired.reshape(planes, block_count, BX, width_y)
    half_x = width_x // 2
    half_rows = planes // 2
    half_blocks = block_count // 2
    first = view_bit == 0
    starts = []
    for target, half in ((tile_index, 0), (tile_index, 1), (tile_index + 1, 0), (tile_index - 1, 1)):
        target = jnp.clip(target, 0, tile_total - 1)
        starts.append(target * block_count + half * half_blocks)
    slots = jnp.concatenate([lax.dynamic_slice_in_dim(sources, st, half_blocks) for st in starts])
    row_ids = jnp.arange(slots.shape[0] * BX, dtype=jnp.int32)
    row_slots = slots[row_ids // BX]
    source_x = (row_slots % block_count) * BX + row_ids % BX
    chosen_rows = (row_slots // block_count == tile_index)[:, None] & (
        source_x[:, None] == jnp.arange(width_x, dtype=jnp.int32)[None, :]
    )
    selection = jnp.broadcast_to(chosen_rows.astype(acquired.dtype)[None], (planes,) + chosen_rows.shape)
    partials = jnp.einsum(
        "zrx,zxy->zry", selection, acquired, preferred_element_type=jnp.float32
    ).astype(acquired.dtype)
    partials = partials.reshape(planes, 4, half_x, width_y)
    own_keep = jnp.where(first, partials[:, 0], partials[:, 1])
    own_give = jnp.where(first, partials[:, 1], partials[:, 0])
    cross_keep = jnp.where(first, partials[:, 3], partials[:, 2])
    cross_pass = jnp.where(first, partials[:, 2], partials[:, 3])
    got = from_partner(jnp.stack([own_give, cross_pass]), "view", 0)
    tiles = lax.axis_size("tile")
    views = lax.axis_size("view")
    route = []
    for tile in range(tiles - 1):
        for slab in range(views // 2):
            right_core = tile * views + 2 * slab + 1
            left_core = (tile + 1) * views + 2 * slab
            route += [(right_core, left_core), (left_core, right_core)]
    outgoing = jnp.where(first, jnp.stack([cross_keep, got[1]]), jnp.stack([got[1], cross_keep]))
    outgoing, psf_taps = lax.optimization_barrier((outgoing, psf_taps))
    incoming = lax.ppermute(outgoing, ("tile", "view"), route)
    own_parts = jnp.where(first, jnp.stack([own_keep, got[0]]), jnp.stack([got[0], own_keep]))
    views_measured = own_parts + incoming
    observed = views_measured.astype(jnp.float32)
    estimate = 0.5 * (observed[0] + observed[1])
    kernels = (psf_taps / jnp.sum(psf_taps, axis=2, keepdims=True)).astype(jnp.bfloat16)
    view_count = kernels.shape[0]
    forward_ops = stacked_operators(kernels, planes, half_x, width_y)
    adjoint_ops = stacked_operators(kernels[:, :, ::-1], planes, half_x, width_y)
    for iteration in range(ITERS):
        estimate_low = estimate.astype(jnp.bfloat16)
        low, high = x_rims(estimate_low, reach, 1)
        extended = jnp.concatenate([low, estimate_low, high], axis=1)
        after_x = jnp.einsum(
            "vzpa,zay->vzpy", forward_ops[0], extended, preferred_element_type=jnp.float32
        ).astype(jnp.bfloat16)
        blurred = pass_z_views(pass_y_views(after_x, forward_ops[1]), forward_ops[2], reach)
        quotients = (observed / blurred).astype(jnp.bfloat16)
        low, high = x_rims(quotients, reach, 2)
        widened = jnp.concatenate([low, quotients, high], axis=2)
        after_x = jnp.einsum(
            "vzpa,vzay->vzpy", adjoint_ops[0], widened, preferred_element_type=jnp.float32
        ).astype(jnp.bfloat16)
        backs = pass_z_views(pass_y_views(after_x, adjoint_ops[1]), adjoint_ops[2], reach)
        estimate = estimate * (0.5 * (backs[0] + backs[1]))
    keep = lax.dynamic_slice_in_dim(estimate, view_bit * half_rows, half_rows, 0)
    give = lax.dynamic_slice_in_dim(estimate, (1 - view_bit) * half_rows, half_rows, 0)
    got = from_partner(give, "view", 0)
    first_half = jnp.where(view_bit == 0, keep, got)
    second_half = jnp.where(view_bit == 0, got, keep)
    return jnp.concatenate([first_half, second_half], axis=1)


def solution(mesh):
    in_specs = (P(("timepoin", "view"), "tile", None), P(), P(("timepoin", "view"), None))
    out_specs = P(("timepoin", "view"), "tile", None)
    return jax.shard_map(local, mesh=mesh, in_specs=in_specs, out_specs=out_specs, check_vma=False)
```

```python
import jax
import jax.numpy as jnp
from jax import lax
from jax.sharding import PartitionSpec as P

BX = 4
ITERS = 2


def shifted(block, axis, distance):
    devices = range(lax.axis_size(axis))
    route = [(i - distance, i) for i in devices if i - distance in devices]
    return lax.ppermute(block, axis, route)


def from_partner(block, axis, distance):
    count = lax.axis_size(axis)
    route = []
    for low in range(count):
        high = low | 1 << distance
        if high != low and high < count:
            route += [(low, high), (high, low)]
    return lax.ppermute(block, axis, route)


def extended_2(block, sides, width):
    for axis, dim in sides:
        count = lax.axis_size(axis)
        forward = [(i, i + 1) for i in range(count - 1)]
        backward = [(target, source) for source, target in forward]
        low = lax.ppermute(
            lax.slice_in_dim(block, block.shape[dim] - width, None, axis=dim), axis, forward
        )
        high = lax.ppermute(lax.slice_in_dim(block, 0, width, axis=dim), axis, backward)
        block = jnp.concatenate([low, block, high], axis=dim)
    return block


def band_matrix(kernel, row_count, col_count, base_shift):
    row_ids = lax.broadcasted_iota(jnp.int32, (row_count, col_count, 1), 0)
    col_ids = lax.broadcasted_iota(jnp.int32, (row_count, col_count, 1), 1)
    tap_ids = lax.broadcasted_iota(jnp.int32, (1, 1, kernel.shape[0]), 2)
    hit = row_ids - col_ids + base_shift == tap_ids
    taps = kernel.astype(jnp.float32)[None, None, :]
    matrix = jnp.sum(jnp.where(hit, taps, jnp.float32(0.0)), axis=2)
    return matrix.astype(jnp.bfloat16)


def operators(kernels, plane_count, width_x, width_y):
    reach = kernels.shape[1] // 2
    along_x = band_matrix(kernels[0], width_x + 2 * reach, width_x, 0).T
    along_x = jnp.broadcast_to(along_x[None], (plane_count,) + along_x.shape)
    return lax.optimization_barrier((
        along_x,
        band_matrix(kernels[1], width_y, width_y, reach),
        band_matrix(kernels[2], plane_count + 2 * reach, plane_count, 0).T,
    ))


def pass_xy(extended, matrices):
    width_y = extended.shape[2]
    after_x = jnp.einsum(
        "zpa,zay->zpy", matrices[0], extended, preferred_element_type=jnp.float32
    ).astype(jnp.bfloat16)
    after_y = jnp.dot(after_x.reshape(-1, width_y), matrices[1], preferred_element_type=jnp.float32)
    return after_y.reshape(after_x.shape).astype(jnp.bfloat16)


def pass_z(extended, matrix):
    planes = extended.shape[0]
    out = jnp.dot(matrix, extended.reshape(planes, -1), preferred_element_type=jnp.float32)
    return out.reshape((matrix.shape[0],) + extended.shape[1:])


def stacked_operators(kernels, plane_count, width_x, width_y):
    reach = kernels.shape[2] // 2
    views = range(kernels.shape[0])
    along_x = jnp.stack([band_matrix(kernels[v, 0], width_x + 2 * reach, width_x, 0).T for v in views])
    along_x = jnp.broadcast_to(along_x[:, None], (along_x.shape[0], plane_count) + along_x.shape[1:])
    return lax.optimization_barrier((
        along_x,
        jnp.stack([band_matrix(kernels[v, 1], width_y, width_y, reach) for v in views]),
        jnp.stack([band_matrix(kernels[v, 2], plane_count + 2 * reach, plane_count, 0).T for v in views]),
    ))


def pass_y_views(after_x, matrices):
    shape = after_x.shape
    flat = after_x.reshape(shape[0], -1, shape[-1])
    after_y = jnp.einsum("vmy,vyq->vmq", flat, matrices, preferred_element_type=jnp.float32)
    return after_y.reshape(shape).astype(jnp.bfloat16)


def pass_z_views(after_y, matrices, reach):
    below, above = z_rims(after_y, reach, 1)
    widened = jnp.concatenate([below, after_y, above], axis=1)
    return jnp.einsum("vpa,vaxy->vpxy", matrices, widened, preferred_element_type=jnp.float32)


def z_rims(volume, reach, axis):
    slabs = lax.axis_size("view") // 2
    slab = lax.axis_index("view") // 2
    planes = volume.shape[axis]
    shape = list(volume.shape)
    shape[axis] = reach
    below = jnp.zeros(shape, volume.dtype)
    above = below
    for phase in (0, 1):
        route = []
        for low in range(phase, slabs - 1, 2):
            for bit in (0, 1):
                route += [(2 * low + bit, 2 * low + 2 + bit), (2 * low + 2 + bit, 2 * low + bit)]
        if not route:
            continue
        is_lower = slab % 2 == phase
        start = jnp.where(is_lower, planes - reach, 0)
        payload = lax.dynamic_slice_in_dim(volume, start, reach, axis)
        got = lax.ppermute(payload, "view", route)
        below = jnp.where(is_lower, below, got)
        above = jnp.where(is_lower, got, above)
    return below, above


def x_rims(block, reach, axis):
    tiles = lax.axis_size("tile")
    views = lax.axis_size("view")
    route = []
    for tile in range(tiles - 1):
        for slab in range(views // 2):
            right_core = tile * views + 2 * slab + 1
            left_core = (tile + 1) * views + 2 * slab
            route += [(right_core, left_core), (left_core, right_core)]
    first = lax.axis_index("view") % 2 == 0
    width = block.shape[axis]
    front = lax.slice_in_dim(block, 0, reach, axis=axis)
    back = lax.slice_in_dim(block, width - reach, width, axis=axis)
    outward = jnp.where(first, front, back)
    inward = jnp.where(first, back, front)
    if outward.ndim == 4:
        across = jnp.stack([lax.ppermute(outward[v], ("tile", "view"), route) for v in range(outward.shape[0])])
    else:
        across = lax.ppermute(outward, ("tile", "view"), route)
    beside = from_partner(inward, "view", 0)
    low = jnp.where(first, across, beside)
    high = jnp.where(first, beside, across)
    return low, high


def local(acquired, psf_taps, block_source):
    planes, width_x, width_y = acquired.shape
    block_count = width_x // BX
    capacity = block_count // 2
    reach = psf_taps.shape[2] // 2
    tile_index = lax.axis_index("tile")
    tile_total = lax.axis_size("tile")
    view_bit = lax.axis_index("view") % 2
    sources = block_source[0]
    blocks = acquired.reshape(planes, block_count, BX, width_y)
    half_x = width_x // 2
    half_rows = planes // 2
    half_blocks = block_count // 2
    first = view_bit == 0
    starts = []
    for target, half in ((tile_index, 0), (tile_index, 1), (tile_index + 1, 0), (tile_index - 1, 1)):
        target = jnp.clip(target, 0, tile_total - 1)
        starts.append(target * block_count + half * half_blocks)
    slots = jnp.concatenate([lax.dynamic_slice_in_dim(sources, st, half_blocks) for st in starts])
    row_ids = jnp.arange(slots.shape[0] * BX, dtype=jnp.int32)
    row_slots = slots[row_ids // BX]
    source_x = (row_slots % block_count) * BX + row_ids % BX
    chosen_rows = (row_slots // block_count == tile_index)[:, None] & (
        source_x[:, None] == jnp.arange(width_x, dtype=jnp.int32)[None, :]
    )
    selection = jnp.broadcast_to(chosen_rows.astype(acquired.dtype)[None], (planes,) + chosen_rows.shape)
    partials = jnp.einsum(
        "zrx,zxy->zry", selection, acquired, preferred_element_type=jnp.float32
    ).astype(acquired.dtype)
    partials = partials.reshape(planes, 4, half_x, width_y)
    own_keep = jnp.where(first, partials[:, 0], partials[:, 1])
    own_give = jnp.where(first, partials[:, 1], partials[:, 0])
    cross_keep = jnp.where(first, partials[:, 3], partials[:, 2])
    cross_pass = jnp.where(first, partials[:, 2], partials[:, 3])
    got = from_partner(jnp.stack([own_give, cross_pass]), "view", 0)
    tiles = lax.axis_size("tile")
    views = lax.axis_size("view")
    route = []
    for tile in range(tiles - 1):
        for slab in range(views // 2):
            right_core = tile * views + 2 * slab + 1
            left_core = (tile + 1) * views + 2 * slab
            route += [(right_core, left_core), (left_core, right_core)]
    outgoing = jnp.where(first, jnp.stack([cross_keep, got[1]]), jnp.stack([got[1], cross_keep]))
    outgoing, psf_taps = lax.optimization_barrier((outgoing, psf_taps))
    incoming = jnp.stack([lax.ppermute(outgoing[v], ("tile", "view"), route) for v in range(outgoing.shape[0])])
    own_parts = jnp.where(first, jnp.stack([own_keep, got[0]]), jnp.stack([got[0], own_keep]))
    views_measured = own_parts + incoming
    observed = views_measured.astype(jnp.float32)
    estimate = 0.5 * (observed[0] + observed[1])
    kernels = (psf_taps / jnp.sum(psf_taps, axis=2, keepdims=True)).astype(jnp.bfloat16)
    view_count = kernels.shape[0]
    forward_ops = stacked_operators(kernels, planes, half_x, width_y)
    adjoint_ops = stacked_operators(kernels[:, :, ::-1], planes, half_x, width_y)
    for iteration in range(ITERS):
        estimate_low = estimate.astype(jnp.bfloat16)
        low, high = x_rims(estimate_low, reach, 1)
        extended = jnp.concatenate([low, estimate_low, high], axis=1)
        after_x = jnp.einsum(
            "vzpa,zay->vzpy", forward_ops[0], extended, preferred_element_type=jnp.float32
        ).astype(jnp.bfloat16)
        blurred = pass_z_views(pass_y_views(after_x, forward_ops[1]), forward_ops[2], reach)
        quotients = (observed / blurred).astype(jnp.bfloat16)
        low, high = x_rims(quotients, reach, 2)
        widened = jnp.concatenate([low, quotients, high], axis=2)
        after_x = jnp.einsum(
            "vzpa,vzay->vzpy", adjoint_ops[0], widened, preferred_element_type=jnp.float32
        ).astype(jnp.bfloat16)
        backs = pass_z_views(pass_y_views(after_x, adjoint_ops[1]), adjoint_ops[2], reach)
        estimate = estimate * (0.5 * (backs[0] + backs[1]))
    keep = lax.dynamic_slice_in_dim(estimate, view_bit * half_rows, half_rows, 0)
    give = lax.dynamic_slice_in_dim(estimate, (1 - view_bit) * half_rows, half_rows, 0)
    got = from_partner(give, "view", 0)
    first_half = jnp.where(view_bit == 0, keep, got)
    second_half = jnp.where(view_bit == 0, got, keep)
    return jnp.concatenate([first_half, second_half], axis=1)


def solution(mesh):
    in_specs = (P(("timepoin", "view"), "tile", None), P(), P(("timepoin", "view"), None))
    out_specs = P(("timepoin", "view"), "tile", None)
    return jax.shard_map(local, mesh=mesh, in_specs=in_specs, out_specs=out_specs, check_vma=False)
```

```python
import jax
import jax.numpy as jnp
from jax import lax
from jax.sharding import PartitionSpec as P

BX = 4
ITERS = 2


def shifted(block, axis, distance):
    devices = range(lax.axis_size(axis))
    route = [(i - distance, i) for i in devices if i - distance in devices]
    return lax.ppermute(block, axis, route)


def from_partner(block, axis, distance):
    count = lax.axis_size(axis)
    route = []
    for low in range(count):
        high = low | 1 << distance
        if high != low and high < count:
            route += [(low, high), (high, low)]
    return lax.ppermute(block, axis, route)


def extended_2(block, sides, width):
    for axis, dim in sides:
        count = lax.axis_size(axis)
        forward = [(i, i + 1) for i in range(count - 1)]
        backward = [(target, source) for source, target in forward]
        low = lax.ppermute(
            lax.slice_in_dim(block, block.shape[dim] - width, None, axis=dim), axis, forward
        )
        high = lax.ppermute(lax.slice_in_dim(block, 0, width, axis=dim), axis, backward)
        block = jnp.concatenate([low, block, high], axis=dim)
    return block


def band_matrix(kernel, row_count, col_count, base_shift):
    row_ids = lax.broadcasted_iota(jnp.int32, (row_count, col_count, 1), 0)
    col_ids = lax.broadcasted_iota(jnp.int32, (row_count, col_count, 1), 1)
    tap_ids = lax.broadcasted_iota(jnp.int32, (1, 1, kernel.shape[0]), 2)
    hit = row_ids - col_ids + base_shift == tap_ids
    taps = kernel.astype(jnp.float32)[None, None, :]
    matrix = jnp.sum(jnp.where(hit, taps, jnp.float32(0.0)), axis=2)
    return matrix.astype(jnp.bfloat16)


def operators(kernels, plane_count, width_x, width_y):
    reach = kernels.shape[1] // 2
    along_x = band_matrix(kernels[0], width_x + 2 * reach, width_x, 0).T
    along_x = jnp.broadcast_to(along_x[None], (plane_count,) + along_x.shape)
    return lax.optimization_barrier((
        along_x,
        band_matrix(kernels[1], width_y, width_y, reach),
        band_matrix(kernels[2], plane_count + 2 * reach, plane_count, 0).T,
    ))


def pass_xy(extended, matrices):
    width_y = extended.shape[2]
    after_x = jnp.einsum(
        "zpa,zay->zpy", matrices[0], extended, preferred_element_type=jnp.float32
    ).astype(jnp.bfloat16)
    after_y = jnp.dot(after_x.reshape(-1, width_y), matrices[1], preferred_element_type=jnp.float32)
    return after_y.reshape(after_x.shape).astype(jnp.bfloat16)


def pass_z(extended, matrix):
    planes = extended.shape[0]
    out = jnp.dot(matrix, extended.reshape(planes, -1), preferred_element_type=jnp.float32)
    return out.reshape((matrix.shape[0],) + extended.shape[1:])


def stacked_operators(kernels, plane_count, width_x, width_y):
    reach = kernels.shape[2] // 2
    views = range(kernels.shape[0])
    along_x = jnp.stack([band_matrix(kernels[v, 0], width_x + 2 * reach, width_x, 0).T for v in views])
    along_x = jnp.broadcast_to(along_x[:, None], (along_x.shape[0], plane_count) + along_x.shape[1:])
    return lax.optimization_barrier((
        along_x,
        jnp.stack([band_matrix(kernels[v, 1], width_y, width_y, reach) for v in views]),
        jnp.stack([band_matrix(kernels[v, 2], plane_count + 2 * reach, plane_count, 0).T for v in views]),
    ))


def pass_y_views(after_x, matrices):
    shape = after_x.shape
    flat = after_x.reshape(shape[0], -1, shape[-1])
    after_y = jnp.einsum("vmy,vyq->vmq", flat, matrices, preferred_element_type=jnp.float32)
    return after_y.reshape(shape).astype(jnp.bfloat16)


def pass_z_views(after_y, matrices, reach):
    below, above = z_rims(after_y, reach, 1)
    widened = jnp.concatenate([below, after_y, above], axis=1)
    return jnp.einsum("vpa,vaxy->vpxy", matrices, widened, preferred_element_type=jnp.float32)


def z_rims(volume, reach, axis):
    slabs = lax.axis_size("view") // 2
    slab = lax.axis_index("view") // 2
    planes = volume.shape[axis]
    shape = list(volume.shape)
    shape[axis] = reach
    below = jnp.zeros(shape, volume.dtype)
    above = below
    for phase in (0, 1):
        route = []
        for low in range(phase, slabs - 1, 2):
            for bit in (0, 1):
                route += [(2 * low + bit, 2 * low + 2 + bit), (2 * low + 2 + bit, 2 * low + bit)]
        if not route:
            continue
        is_lower = slab % 2 == phase
        top = lax.slice_in_dim(volume, planes - reach, planes, axis=axis)
        bottom = lax.slice_in_dim(volume, 0, reach, axis=axis)
        payload = jnp.where(is_lower, top, bottom)
        got = lax.ppermute(payload, "view", route)
        below = jnp.where(is_lower, below, got)
        above = jnp.where(is_lower, got, above)
    return below, above


def x_rims(block, reach, axis):
    tiles = lax.axis_size("tile")
    views = lax.axis_size("view")
    route = []
    for tile in range(tiles - 1):
        for slab in range(views // 2):
            right_core = tile * views + 2 * slab + 1
            left_core = (tile + 1) * views + 2 * slab
            route += [(right_core, left_core), (left_core, right_core)]
    first = lax.axis_index("view") % 2 == 0
    width = block.shape[axis]
    front = lax.slice_in_dim(block, 0, reach, axis=axis)
    back = lax.slice_in_dim(block, width - reach, width, axis=axis)
    outward = jnp.where(first, front, back)
    inward = jnp.where(first, back, front)
    across = lax.ppermute(outward, ("tile", "view"), route)
    beside = from_partner(inward, "view", 0)
    low = jnp.where(first, across, beside)
    high = jnp.where(first, beside, across)
    return low, high


def local(acquired, psf_taps, block_source):
    planes, width_x, width_y = acquired.shape
    block_count = width_x // BX
    capacity = block_count // 2
    reach = psf_taps.shape[2] // 2
    tile_index = lax.axis_index("tile")
    tile_total = lax.axis_size("tile")
    view_bit = lax.axis_index("view") % 2
    sources = block_source[0]
    blocks = acquired.reshape(planes, block_count, BX, width_y)
    half_x = width_x // 2
    half_rows = planes // 2
    half_blocks = block_count // 2
    first = view_bit == 0
    starts = []
    for target, half in ((tile_index, 0), (tile_index, 1), (tile_index + 1, 0), (tile_index - 1, 1)):
        target = jnp.clip(target, 0, tile_total - 1)
        starts.append(target * block_count + half * half_blocks)
    slots = jnp.concatenate([lax.dynamic_slice_in_dim(sources, st, half_blocks) for st in starts])
    row_ids = jnp.arange(slots.shape[0] * BX, dtype=jnp.int32)
    row_slots = slots[row_ids // BX]
    source_x = (row_slots % block_count) * BX + row_ids % BX
    chosen_rows = (row_slots // block_count == tile_index)[:, None] & (
        source_x[:, None] == jnp.arange(width_x, dtype=jnp.int32)[None, :]
    )
    selection = jnp.broadcast_to(chosen_rows.astype(acquired.dtype)[None], (planes,) + chosen_rows.shape)
    partials = jnp.einsum(
        "zrx,zxy->zry", selection, acquired, preferred_element_type=jnp.float32
    ).astype(acquired.dtype)
    partials = partials.reshape(planes, 4, half_x, width_y)
    own_keep = jnp.where(first, partials[:, 0], partials[:, 1])
    own_give = jnp.where(first, partials[:, 1], partials[:, 0])
    cross_keep = jnp.where(first, partials[:, 3], partials[:, 2])
    cross_pass = jnp.where(first, partials[:, 2], partials[:, 3])
    got = from_partner(jnp.stack([own_give, cross_pass]), "view", 0)
    tiles = lax.axis_size("tile")
    views = lax.axis_size("view")
    route = []
    for tile in range(tiles - 1):
        for slab in range(views // 2):
            right_core = tile * views + 2 * slab + 1
            left_core = (tile + 1) * views + 2 * slab
            route += [(right_core, left_core), (left_core, right_core)]
    outgoing = jnp.where(first, jnp.stack([cross_keep, got[1]]), jnp.stack([got[1], cross_keep]))
    outgoing, psf_taps = lax.optimization_barrier((outgoing, psf_taps))
    incoming = lax.ppermute(outgoing, ("tile", "view"), route)
    own_parts = jnp.where(first, jnp.stack([own_keep, got[0]]), jnp.stack([got[0], own_keep]))
    views_measured = own_parts + incoming
    observed = views_measured.astype(jnp.float32)
    estimate = 0.5 * (observed[0] + observed[1])
    kernels = (psf_taps / jnp.sum(psf_taps, axis=2, keepdims=True)).astype(jnp.bfloat16)
    view_count = kernels.shape[0]
    forward_ops = stacked_operators(kernels, planes, half_x, width_y)
    adjoint_ops = stacked_operators(kernels[:, :, ::-1], planes, half_x, width_y)
    for iteration in range(ITERS):
        estimate_low = estimate.astype(jnp.bfloat16)
        low, high = x_rims(estimate_low, reach, 1)
        extended = jnp.concatenate([low, estimate_low, high], axis=1)
        after_x = jnp.einsum(
            "vzpa,zay->vzpy", forward_ops[0], extended, preferred_element_type=jnp.float32
        ).astype(jnp.bfloat16)
        blurred = pass_z_views(pass_y_views(after_x, forward_ops[1]), forward_ops[2], reach)
        quotients = (observed / blurred).astype(jnp.bfloat16)
        low, high = x_rims(quotients, reach, 2)
        widened = jnp.concatenate([low, quotients, high], axis=2)
        after_x = jnp.einsum(
            "vzpa,vzay->vzpy", adjoint_ops[0], widened, preferred_element_type=jnp.float32
        ).astype(jnp.bfloat16)
        backs = pass_z_views(pass_y_views(after_x, adjoint_ops[1]), adjoint_ops[2], reach)
        estimate = estimate * (0.5 * (backs[0] + backs[1]))
    keep = lax.dynamic_slice_in_dim(estimate, view_bit * half_rows, half_rows, 0)
    give = lax.dynamic_slice_in_dim(estimate, (1 - view_bit) * half_rows, half_rows, 0)
    got = from_partner(give, "view", 0)
    first_half = jnp.where(view_bit == 0, keep, got)
    second_half = jnp.where(view_bit == 0, got, keep)
    return jnp.concatenate([first_half, second_half], axis=1)


def solution(mesh):
    in_specs = (P(("timepoin", "view"), "tile", None), P(), P(("timepoin", "view"), None))
    out_specs = P(("timepoin", "view"), "tile", None)
    return jax.shard_map(local, mesh=mesh, in_specs=in_specs, out_specs=out_specs, check_vma=False)
```

```python
import jax
import jax.numpy as jnp
from jax import lax
from jax.sharding import PartitionSpec as P

BX = 4
ITERS = 2


def shifted(block, axis, distance):
    devices = range(lax.axis_size(axis))
    route = [(i - distance, i) for i in devices if i - distance in devices]
    return lax.ppermute(block, axis, route)


def from_partner(block, axis, distance):
    count = lax.axis_size(axis)
    route = []
    for low in range(count):
        high = low | 1 << distance
        if high != low and high < count:
            route += [(low, high), (high, low)]
    return lax.ppermute(block, axis, route)


def extended_2(block, sides, width):
    for axis, dim in sides:
        count = lax.axis_size(axis)
        forward = [(i, i + 1) for i in range(count - 1)]
        backward = [(target, source) for source, target in forward]
        low = lax.ppermute(
            lax.slice_in_dim(block, block.shape[dim] - width, None, axis=dim), axis, forward
        )
        high = lax.ppermute(lax.slice_in_dim(block, 0, width, axis=dim), axis, backward)
        block = jnp.concatenate([low, block, high], axis=dim)
    return block


def band_matrix(kernel, row_count, col_count, base_shift):
    row_ids = lax.broadcasted_iota(jnp.int32, (row_count, col_count, 1), 0)
    col_ids = lax.broadcasted_iota(jnp.int32, (row_count, col_count, 1), 1)
    tap_ids = lax.broadcasted_iota(jnp.int32, (1, 1, kernel.shape[0]), 2)
    hit = row_ids - col_ids + base_shift == tap_ids
    taps = kernel.astype(jnp.float32)[None, None, :]
    matrix = jnp.sum(jnp.where(hit, taps, jnp.float32(0.0)), axis=2)
    return matrix.astype(jnp.bfloat16)


def operators(kernels, plane_count, width_x, width_y):
    reach = kernels.shape[1] // 2
    along_x = band_matrix(kernels[0], width_x + 2 * reach, width_x, 0).T
    along_x = jnp.broadcast_to(along_x[None], (plane_count,) + along_x.shape)
    return lax.optimization_barrier((
        along_x,
        band_matrix(kernels[1], width_y, width_y, reach),
        band_matrix(kernels[2], plane_count + 2 * reach, plane_count, 0).T,
    ))


def pass_xy(extended, matrices):
    width_y = extended.shape[2]
    after_x = jnp.einsum(
        "zpa,zay->zpy", matrices[0], extended, preferred_element_type=jnp.float32
    ).astype(jnp.bfloat16)
    after_y = jnp.dot(after_x.reshape(-1, width_y), matrices[1], preferred_element_type=jnp.float32)
    return after_y.reshape(after_x.shape).astype(jnp.bfloat16)


def pass_z(extended, matrix):
    planes = extended.shape[0]
    out = jnp.dot(matrix, extended.reshape(planes, -1), preferred_element_type=jnp.float32)
    return out.reshape((matrix.shape[0],) + extended.shape[1:])


def stacked_operators(kernels, plane_count, width_x, width_y):
    reach = kernels.shape[2] // 2
    views = range(kernels.shape[0])
    along_x = jnp.stack([band_matrix(kernels[v, 0], width_x + 2 * reach, width_x, 0).T for v in views])
    along_x = jnp.broadcast_to(along_x[:, None], (along_x.shape[0], plane_count) + along_x.shape[1:])
    return lax.optimization_barrier((
        along_x,
        jnp.stack([band_matrix(kernels[v, 1], width_y, width_y, reach) for v in views]),
        jnp.stack([band_matrix(kernels[v, 2], plane_count + 2 * reach, plane_count, 0).T for v in views]),
    ))


def pass_y_views(after_x, matrices):
    shape = after_x.shape
    flat = after_x.reshape(shape[0], -1, shape[-1])
    after_y = jnp.einsum("vmy,vyq->vmq", flat, matrices, preferred_element_type=jnp.float32)
    return after_y.reshape(shape).astype(jnp.bfloat16)


def pass_z_views(after_y, matrices, reach):
    below, above = z_rims(after_y, reach, 1)
    widened = jnp.concatenate([below, after_y, above], axis=1)
    return jnp.einsum("vpa,vaxy->vpxy", matrices, widened, preferred_element_type=jnp.float32)


def z_rims(volume, reach, axis):
    slabs = lax.axis_size("view") // 2
    slab = lax.axis_index("view") // 2
    planes = volume.shape[axis]
    shape = list(volume.shape)
    shape[axis] = reach
    below = jnp.zeros(shape, volume.dtype)
    above = below
    for phase in (0, 1):
        route = []
        for low in range(phase, slabs - 1, 2):
            for bit in (0, 1):
                route += [(2 * low + bit, 2 * low + 2 + bit), (2 * low + 2 + bit, 2 * low + bit)]
        if not route:
            continue
        is_lower = slab % 2 == phase
        top = lax.slice_in_dim(volume, planes - reach, planes, axis=axis)
        bottom = lax.slice_in_dim(volume, 0, reach, axis=axis)
        payload = jnp.where(is_lower, top, bottom)
        got = lax.ppermute(payload, "view", route)
        below = jnp.where(is_lower, below, got)
        above = jnp.where(is_lower, got, above)
    return below, above


def x_rims(block, reach, axis):
    tiles = lax.axis_size("tile")
    views = lax.axis_size("view")
    route = []
    for tile in range(tiles - 1):
        for slab in range(views // 2):
            right_core = tile * views + 2 * slab + 1
            left_core = (tile + 1) * views + 2 * slab
            route += [(right_core, left_core), (left_core, right_core)]
    first = lax.axis_index("view") % 2 == 0
    width = block.shape[axis]
    front = lax.slice_in_dim(block, 0, reach, axis=axis)
    back = lax.slice_in_dim(block, width - reach, width, axis=axis)
    outward = jnp.where(first, front, back)
    inward = jnp.where(first, back, front)
    across = lax.ppermute(outward, ("tile", "view"), route)
    beside = from_partner(inward, "view", 0)
    low = jnp.where(first, across, beside)
    high = jnp.where(first, beside, across)
    return low, high


def local(acquired, psf_taps, block_source):
    planes, width_x, width_y = acquired.shape
    block_count = width_x // BX
    capacity = block_count // 2
    reach = psf_taps.shape[2] // 2
    tile_index = lax.axis_index("tile")
    tile_total = lax.axis_size("tile")
    view_bit = lax.axis_index("view") % 2
    sources = block_source[0]
    blocks = acquired.reshape(planes, block_count, BX, width_y)
    half_x = width_x // 2
    half_rows = planes // 2
    half_blocks = block_count // 2
    first = view_bit == 0
    table = jnp.pad(sources.reshape(tile_total, block_count), ((1, 1), (0, 0)))
    near = lax.dynamic_slice_in_dim(table, tile_index, 3, 0)
    slots = jnp.concatenate([near[1], near[2, :half_blocks], near[0, half_blocks:]])
    row_ids = jnp.arange(slots.shape[0] * BX, dtype=jnp.int32)
    row_slots = slots[row_ids // BX]
    source_x = (row_slots % block_count) * BX + row_ids % BX
    chosen_rows = (row_slots // block_count == tile_index)[:, None] & (
        source_x[:, None] == jnp.arange(width_x, dtype=jnp.int32)[None, :]
    )
    selection = jnp.broadcast_to(chosen_rows.astype(acquired.dtype)[None], (planes,) + chosen_rows.shape)
    partials = jnp.einsum(
        "zrx,zxy->zry", selection, acquired, preferred_element_type=jnp.float32
    ).astype(acquired.dtype)
    partials = partials.reshape(planes, 4, half_x, width_y)
    own_keep = jnp.where(first, partials[:, 0], partials[:, 1])
    own_give = jnp.where(first, partials[:, 1], partials[:, 0])
    cross_keep = jnp.where(first, partials[:, 3], partials[:, 2])
    cross_pass = jnp.where(first, partials[:, 2], partials[:, 3])
    got = from_partner(jnp.stack([own_give, cross_pass]), "view", 0)
    tiles = lax.axis_size("tile")
    views = lax.axis_size("view")
    route = []
    for tile in range(tiles - 1):
        for slab in range(views // 2):
            right_core = tile * views + 2 * slab + 1
            left_core = (tile + 1) * views + 2 * slab
            route += [(right_core, left_core), (left_core, right_core)]
    outgoing = jnp.where(first, jnp.stack([cross_keep, got[1]]), jnp.stack([got[1], cross_keep]))
    outgoing, psf_taps = lax.optimization_barrier((outgoing, psf_taps))
    incoming = lax.ppermute(outgoing, ("tile", "view"), route)
    own_parts = jnp.where(first, jnp.stack([own_keep, got[0]]), jnp.stack([got[0], own_keep]))
    views_measured = own_parts + incoming
    observed = views_measured.astype(jnp.float32)
    estimate = 0.5 * (observed[0] + observed[1])
    kernels = (psf_taps / jnp.sum(psf_taps, axis=2, keepdims=True)).astype(jnp.bfloat16)
    view_count = kernels.shape[0]
    forward_ops = stacked_operators(kernels, planes, half_x, width_y)
    adjoint_ops = stacked_operators(kernels[:, :, ::-1], planes, half_x, width_y)
    for iteration in range(ITERS):
        estimate_low = estimate.astype(jnp.bfloat16)
        low, high = x_rims(estimate_low, reach, 1)
        extended = jnp.concatenate([low, estimate_low, high], axis=1)
        after_x = jnp.einsum(
            "vzpa,zay->vzpy", forward_ops[0], extended, preferred_element_type=jnp.float32
        ).astype(jnp.bfloat16)
        blurred = pass_z_views(pass_y_views(after_x, forward_ops[1]), forward_ops[2], reach)
        quotients = (observed / blurred).astype(jnp.bfloat16)
        low, high = x_rims(quotients, reach, 2)
        widened = jnp.concatenate([low, quotients, high], axis=2)
        after_x = jnp.einsum(
            "vzpa,vzay->vzpy", adjoint_ops[0], widened, preferred_element_type=jnp.float32
        ).astype(jnp.bfloat16)
        backs = pass_z_views(pass_y_views(after_x, adjoint_ops[1]), adjoint_ops[2], reach)
        estimate = estimate * (0.5 * (backs[0] + backs[1]))
    keep = lax.dynamic_slice_in_dim(estimate, view_bit * half_rows, half_rows, 0)
    give = lax.dynamic_slice_in_dim(estimate, (1 - view_bit) * half_rows, half_rows, 0)
    got = from_partner(give, "view", 0)
    first_half = jnp.where(view_bit == 0, keep, got)
    second_half = jnp.where(view_bit == 0, got, keep)
    return jnp.concatenate([first_half, second_half], axis=1)


def solution(mesh):
    in_specs = (P(("timepoin", "view"), "tile", None), P(), P(("timepoin", "view"), None))
    out_specs = P(("timepoin", "view"), "tile", None)
    return jax.shard_map(local, mesh=mesh, in_specs=in_specs, out_specs=out_specs, check_vma=False)
```

```python
import jax
import jax.numpy as jnp
from jax import lax
from jax.sharding import PartitionSpec as P

BX = 4
ITERS = 2


def shifted(block, axis, distance):
    devices = range(lax.axis_size(axis))
    route = [(i - distance, i) for i in devices if i - distance in devices]
    return lax.ppermute(block, axis, route)


def from_partner(block, axis, distance):
    count = lax.axis_size(axis)
    route = []
    for low in range(count):
        high = low | 1 << distance
        if high != low and high < count:
            route += [(low, high), (high, low)]
    return lax.ppermute(block, axis, route)


def extended_2(block, sides, width):
    for axis, dim in sides:
        count = lax.axis_size(axis)
        forward = [(i, i + 1) for i in range(count - 1)]
        backward = [(target, source) for source, target in forward]
        low = lax.ppermute(
            lax.slice_in_dim(block, block.shape[dim] - width, None, axis=dim), axis, forward
        )
        high = lax.ppermute(lax.slice_in_dim(block, 0, width, axis=dim), axis, backward)
        block = jnp.concatenate([low, block, high], axis=dim)
    return block


def band_matrix(kernel, row_count, col_count, base_shift):
    row_ids = lax.broadcasted_iota(jnp.int32, (row_count, col_count, 1), 0)
    col_ids = lax.broadcasted_iota(jnp.int32, (row_count, col_count, 1), 1)
    tap_ids = lax.broadcasted_iota(jnp.int32, (1, 1, kernel.shape[0]), 2)
    hit = row_ids - col_ids + base_shift == tap_ids
    taps = kernel.astype(jnp.float32)[None, None, :]
    matrix = jnp.sum(jnp.where(hit, taps, jnp.float32(0.0)), axis=2)
    return matrix.astype(jnp.bfloat16)


def operators(kernels, plane_count, width_x, width_y):
    reach = kernels.shape[1] // 2
    along_x = band_matrix(kernels[0], width_x + 2 * reach, width_x, 0).T
    along_x = jnp.broadcast_to(along_x[None], (plane_count,) + along_x.shape)
    return lax.optimization_barrier((
        along_x,
        band_matrix(kernels[1], width_y, width_y, reach),
        band_matrix(kernels[2], plane_count + 2 * reach, plane_count, 0).T,
    ))


def pass_xy(extended, matrices):
    width_y = extended.shape[2]
    after_x = jnp.einsum(
        "zpa,zay->zpy", matrices[0], extended, preferred_element_type=jnp.float32
    ).astype(jnp.bfloat16)
    after_y = jnp.dot(after_x.reshape(-1, width_y), matrices[1], preferred_element_type=jnp.float32)
    return after_y.reshape(after_x.shape).astype(jnp.bfloat16)


def pass_z(extended, matrix):
    planes = extended.shape[0]
    out = jnp.dot(matrix, extended.reshape(planes, -1), preferred_element_type=jnp.float32)
    return out.reshape((matrix.shape[0],) + extended.shape[1:])


def stacked_operators(kernels, plane_count, width_x, width_y):
    reach = kernels.shape[2] // 2
    views = range(kernels.shape[0])
    along_x = jnp.stack([band_matrix(kernels[v, 0], width_x + 2 * reach, width_x, 0).T for v in views])
    along_x = jnp.broadcast_to(along_x[:, None], (along_x.shape[0], plane_count) + along_x.shape[1:])
    return lax.optimization_barrier((
        along_x,
        jnp.stack([band_matrix(kernels[v, 1], width_y, width_y, reach) for v in views]),
        jnp.stack([band_matrix(kernels[v, 2], plane_count + 2 * reach, plane_count, 0).T for v in views]),
    ))


def pass_y_views(after_x, matrices):
    shape = after_x.shape
    flat = after_x.reshape(shape[0], -1, shape[-1])
    after_y = jnp.einsum("vmy,vyq->vmq", flat, matrices, preferred_element_type=jnp.float32)
    return after_y.reshape(shape).astype(jnp.bfloat16)


def pass_z_views(after_y, matrices, reach):
    below, above = z_rims(after_y, reach, 1)
    widened = jnp.concatenate([below, after_y, above], axis=1)
    return jnp.einsum("vpa,vaxy->vpxy", matrices, widened, preferred_element_type=jnp.float32)


def z_rims(volume, reach, axis):
    slabs = lax.axis_size("view") // 2
    slab = lax.axis_index("view") // 2
    planes = volume.shape[axis]
    shape = list(volume.shape)
    shape[axis] = reach
    below = jnp.zeros(shape, volume.dtype)
    above = below
    for phase in (0, 1):
        route = []
        for low in range(phase, slabs - 1, 2):
            for bit in (0, 1):
                route += [(2 * low + bit, 2 * low + 2 + bit), (2 * low + 2 + bit, 2 * low + bit)]
        if not route:
            continue
        is_lower = slab % 2 == phase
        top = lax.slice_in_dim(volume, planes - reach, planes, axis=axis)
        bottom = lax.slice_in_dim(volume, 0, reach, axis=axis)
        payload = jnp.where(is_lower, top, bottom)
        got = lax.ppermute(payload, "view", route)
        below = jnp.where(is_lower, below, got)
        above = jnp.where(is_lower, got, above)
    return below, above


def x_rims(block, reach, axis):
    tiles = lax.axis_size("tile")
    views = lax.axis_size("view")
    route = []
    for tile in range(tiles - 1):
        for slab in range(views // 2):
            right_core = tile * views + 2 * slab + 1
            left_core = (tile + 1) * views + 2 * slab
            route += [(right_core, left_core), (left_core, right_core)]
    first = lax.axis_index("view") % 2 == 0
    width = block.shape[axis]
    front = lax.slice_in_dim(block, 0, reach, axis=axis)
    back = lax.slice_in_dim(block, width - reach, width, axis=axis)
    outward = jnp.where(first, front, back)
    inward = jnp.where(first, back, front)
    across = lax.ppermute(outward, ("tile", "view"), route)
    beside = from_partner(inward, "view", 0)
    low = jnp.where(first, across, beside)
    high = jnp.where(first, beside, across)
    return low, high


def local(acquired, psf_taps, block_source):
    planes, width_x, width_y = acquired.shape
    block_count = width_x // BX
    capacity = block_count // 2
    reach = psf_taps.shape[2] // 2
    tile_index = lax.axis_index("tile")
    tile_total = lax.axis_size("tile")
    view_bit = lax.axis_index("view") % 2
    sources = block_source[0]
    blocks = acquired.reshape(planes, block_count, BX, width_y)
    half_x = width_x // 2
    half_rows = planes // 2
    half_blocks = block_count // 2
    first = view_bit == 0
    starts = []
    for target, half in ((tile_index, 0), (tile_index, 1), (tile_index + 1, 0), (tile_index - 1, 1)):
        target = jnp.clip(target, 0, tile_total - 1)
        starts.append(target * block_count + half * half_blocks)
    slots = jnp.concatenate([lax.dynamic_slice_in_dim(sources, st, half_blocks) for st in starts])
    row_ids = jnp.arange(slots.shape[0] * BX, dtype=jnp.int32)
    row_slots = slots[row_ids // BX]
    source_x = (row_slots % block_count) * BX + row_ids % BX
    chosen_rows = (row_slots // block_count == tile_index)[:, None] & (
        source_x[:, None] == jnp.arange(width_x, dtype=jnp.int32)[None, :]
    )
    selection = jnp.broadcast_to(chosen_rows.astype(acquired.dtype)[None], (planes,) + chosen_rows.shape)
    partials = jnp.einsum(
        "zrx,zxy->zry", selection, acquired, preferred_element_type=jnp.float32
    ).astype(acquired.dtype)
    partials = partials.reshape(planes, 4, half_x, width_y)
    own_keep = jnp.where(first, partials[:, 0], partials[:, 1])
    own_give = jnp.where(first, partials[:, 1], partials[:, 0])
    cross_keep = jnp.where(first, partials[:, 3], partials[:, 2])
    cross_pass = jnp.where(first, partials[:, 2], partials[:, 3])
    got = from_partner(jnp.stack([own_give, cross_pass]), "view", 0)
    tiles = lax.axis_size("tile")
    views = lax.axis_size("view")
    route = []
    for tile in range(tiles - 1):
        for slab in range(views // 2):
            right_core = tile * views + 2 * slab + 1
            left_core = (tile + 1) * views + 2 * slab
            route += [(right_core, left_core), (left_core, right_core)]
    outgoing = jnp.where(first, jnp.stack([cross_keep, got[1]]), jnp.stack([got[1], cross_keep]))
    outgoing, psf_taps = lax.optimization_barrier((outgoing, psf_taps))
    incoming = lax.ppermute(outgoing, ("tile", "view"), route)
    own_parts = jnp.where(first, jnp.stack([own_keep, got[0]]), jnp.stack([got[0], own_keep]))
    views_measured = own_parts + incoming
    observed = views_measured.astype(jnp.float32)
    estimate = 0.5 * (observed[0] + observed[1])
    kernels = (psf_taps / jnp.sum(psf_taps, axis=2, keepdims=True)).astype(jnp.bfloat16)
    view_count = kernels.shape[0]
    forward_ops = stacked_operators(kernels, planes, half_x, width_y)
    adjoint_ops = stacked_operators(kernels[:, :, ::-1], planes, half_x, width_y)
    for iteration in range(ITERS):
        estimate_low = estimate.astype(jnp.bfloat16)
        low, high = x_rims(estimate_low, reach, 1)
        extended = jnp.concatenate([low, estimate_low, high], axis=1)
        after_x = jnp.einsum(
            "vzpa,zay->vzpy", forward_ops[0], extended, preferred_element_type=jnp.float32
        ).astype(jnp.bfloat16)
        blurred = pass_z_views(pass_y_views(after_x, forward_ops[1]), forward_ops[2], reach)
        quotients = (observed / blurred).astype(jnp.bfloat16)
        low, high = x_rims(quotients, reach, 2)
        widened = jnp.concatenate([low, quotients, high], axis=2)
        after_x = jnp.einsum(
            "vzpa,vzay->vzpy", adjoint_ops[0], widened, preferred_element_type=jnp.float32
        ).astype(jnp.bfloat16)
        backs = pass_z_views(pass_y_views(after_x, adjoint_ops[1]), adjoint_ops[2], reach)
        estimate = estimate * (0.5 * (backs[0] + backs[1]))
    keep = lax.dynamic_slice_in_dim(estimate, view_bit * half_rows, half_rows, 0)
    give = lax.dynamic_slice_in_dim(estimate, (1 - view_bit) * half_rows, half_rows, 0)
    got = from_partner(give, "view", 0)
    both = jnp.concatenate([keep, got, keep], axis=1)
    return lax.dynamic_slice_in_dim(both, view_bit * half_x, width_x, 1)


def solution(mesh):
    in_specs = (P(("timepoin", "view"), "tile", None), P(), P(("timepoin", "view"), None))
    out_specs = P(("timepoin", "view"), "tile", None)
    return jax.shard_map(local, mesh=mesh, in_specs=in_specs, out_specs=out_specs, check_vma=False)
```

```python
import jax
import jax.numpy as jnp
from jax import lax
from jax.sharding import PartitionSpec as P

BX = 4
ITERS = 2


def shifted(block, axis, distance):
    devices = range(lax.axis_size(axis))
    route = [(i - distance, i) for i in devices if i - distance in devices]
    return lax.ppermute(block, axis, route)


def from_partner(block, axis, distance):
    count = lax.axis_size(axis)
    route = []
    for low in range(count):
        high = low | 1 << distance
        if high != low and high < count:
            route += [(low, high), (high, low)]
    return lax.ppermute(block, axis, route)


def extended_2(block, sides, width):
    for axis, dim in sides:
        count = lax.axis_size(axis)
        forward = [(i, i + 1) for i in range(count - 1)]
        backward = [(target, source) for source, target in forward]
        low = lax.ppermute(
            lax.slice_in_dim(block, block.shape[dim] - width, None, axis=dim), axis, forward
        )
        high = lax.ppermute(lax.slice_in_dim(block, 0, width, axis=dim), axis, backward)
        block = jnp.concatenate([low, block, high], axis=dim)
    return block


def band_matrix(kernel, row_count, col_count, base_shift):
    row_ids = lax.broadcasted_iota(jnp.int32, (row_count, col_count, 1), 0)
    col_ids = lax.broadcasted_iota(jnp.int32, (row_count, col_count, 1), 1)
    tap_ids = lax.broadcasted_iota(jnp.int32, (1, 1, kernel.shape[0]), 2)
    hit = row_ids - col_ids + base_shift == tap_ids
    taps = kernel.astype(jnp.float32)[None, None, :]
    matrix = jnp.sum(jnp.where(hit, taps, jnp.float32(0.0)), axis=2)
    return matrix.astype(jnp.bfloat16)


def operators(kernels, plane_count, width_x, width_y):
    reach = kernels.shape[1] // 2
    along_x = band_matrix(kernels[0], width_x + 2 * reach, width_x, 0).T
    along_x = jnp.broadcast_to(along_x[None], (plane_count,) + along_x.shape)
    return lax.optimization_barrier((
        along_x,
        band_matrix(kernels[1], width_y, width_y, reach),
        band_matrix(kernels[2], plane_count + 2 * reach, plane_count, 0).T,
    ))


def pass_xy(extended, matrices):
    width_y = extended.shape[2]
    after_x = jnp.einsum(
        "zpa,zay->zpy", matrices[0], extended, preferred_element_type=jnp.float32
    ).astype(jnp.bfloat16)
    after_y = jnp.dot(after_x.reshape(-1, width_y), matrices[1], preferred_element_type=jnp.float32)
    return after_y.reshape(after_x.shape).astype(jnp.bfloat16)


def pass_z(extended, matrix):
    planes = extended.shape[0]
    out = jnp.dot(matrix, extended.reshape(planes, -1), preferred_element_type=jnp.float32)
    return out.reshape((matrix.shape[0],) + extended.shape[1:])


def stacked_operators(kernels, plane_count, width_x, width_y):
    reach = kernels.shape[2] // 2
    views = range(kernels.shape[0])
    along_x = jnp.stack([band_matrix(kernels[v, 0], width_x + 2 * reach, width_x, 0).T for v in views])
    along_x = jnp.broadcast_to(along_x[:, None], (along_x.shape[0], plane_count) + along_x.shape[1:])
    return lax.optimization_barrier((
        along_x,
        jnp.stack([band_matrix(kernels[v, 1], width_y, width_y, reach) for v in views]),
        jnp.stack([band_matrix(kernels[v, 2], plane_count + 2 * reach, plane_count, 0).T for v in views]),
    ))


def pass_y_views(after_x, matrices):
    shape = after_x.shape
    flat = after_x.reshape(shape[0], -1, shape[-1])
    after_y = jnp.einsum("vmy,vyq->vmq", flat, matrices, preferred_element_type=jnp.float32)
    return after_y.reshape(shape).astype(jnp.bfloat16)


def pass_z_views(after_y, matrices, reach):
    below, above = z_rims(after_y, reach, 1)
    planes = after_y.shape[1]
    inner = jnp.einsum(
        "vpa,vaxy->vpxy", matrices[:, :, reach : reach + planes], after_y, preferred_element_type=jnp.float32
    )
    lower = jnp.einsum("vpa,vaxy->vpxy", matrices[:, :, :reach], below, preferred_element_type=jnp.float32)
    upper = jnp.einsum(
        "vpa,vaxy->vpxy", matrices[:, :, reach + planes :], above, preferred_element_type=jnp.float32
    )
    return inner + lower + upper


def z_rims(volume, reach, axis):
    slabs = lax.axis_size("view") // 2
    slab = lax.axis_index("view") // 2
    planes = volume.shape[axis]
    shape = list(volume.shape)
    shape[axis] = reach
    below = jnp.zeros(shape, volume.dtype)
    above = below
    for phase in (0, 1):
        route = []
        for low in range(phase, slabs - 1, 2):
            for bit in (0, 1):
                route += [(2 * low + bit, 2 * low + 2 + bit), (2 * low + 2 + bit, 2 * low + bit)]
        if not route:
            continue
        is_lower = slab % 2 == phase
        top = lax.slice_in_dim(volume, planes - reach, planes, axis=axis)
        bottom = lax.slice_in_dim(volume, 0, reach, axis=axis)
        payload = jnp.where(is_lower, top, bottom)
        got = lax.ppermute(payload, "view", route)
        below = jnp.where(is_lower, below, got)
        above = jnp.where(is_lower, got, above)
    return below, above


def x_rims(block, reach, axis):
    tiles = lax.axis_size("tile")
    views = lax.axis_size("view")
    route = []
    for tile in range(tiles - 1):
        for slab in range(views // 2):
            right_core = tile * views + 2 * slab + 1
            left_core = (tile + 1) * views + 2 * slab
            route += [(right_core, left_core), (left_core, right_core)]
    first = lax.axis_index("view") % 2 == 0
    width = block.shape[axis]
    front = lax.slice_in_dim(block, 0, reach, axis=axis)
    back = lax.slice_in_dim(block, width - reach, width, axis=axis)
    outward = jnp.where(first, front, back)
    inward = jnp.where(first, back, front)
    across = lax.ppermute(outward, ("tile", "view"), route)
    beside = from_partner(inward, "view", 0)
    low = jnp.where(first, across, beside)
    high = jnp.where(first, beside, across)
    return low, high


def local(acquired, psf_taps, block_source):
    planes, width_x, width_y = acquired.shape
    block_count = width_x // BX
    capacity = block_count // 2
    reach = psf_taps.shape[2] // 2
    tile_index = lax.axis_index("tile")
    tile_total = lax.axis_size("tile")
    view_bit = lax.axis_index("view") % 2
    sources = block_source[0]
    blocks = acquired.reshape(planes, block_count, BX, width_y)
    half_x = width_x // 2
    half_rows = planes // 2
    half_blocks = block_count // 2
    first = view_bit == 0
    starts = []
    for target, half in ((tile_index, 0), (tile_index, 1), (tile_index + 1, 0), (tile_index - 1, 1)):
        target = jnp.clip(target, 0, tile_total - 1)
        starts.append(target * block_count + half * half_blocks)
    slots = jnp.concatenate([lax.dynamic_slice_in_dim(sources, st, half_blocks) for st in starts])
    row_ids = jnp.arange(slots.shape[0] * BX, dtype=jnp.int32)
    row_slots = slots[row_ids // BX]
    source_x = (row_slots % block_count) * BX + row_ids % BX
    chosen_rows = (row_slots // block_count == tile_index)[:, None] & (
        source_x[:, None] == jnp.arange(width_x, dtype=jnp.int32)[None, :]
    )
    selection = jnp.broadcast_to(chosen_rows.astype(acquired.dtype)[None], (planes,) + chosen_rows.shape)
    partials = jnp.einsum(
        "zrx,zxy->zry", selection, acquired, preferred_element_type=jnp.float32
    ).astype(acquired.dtype)
    partials = partials.reshape(planes, 4, half_x, width_y)
    own_keep = jnp.where(first, partials[:, 0], partials[:, 1])
    own_give = jnp.where(first, partials[:, 1], partials[:, 0])
    cross_keep = jnp.where(first, partials[:, 3], partials[:, 2])
    cross_pass = jnp.where(first, partials[:, 2], partials[:, 3])
    got = from_partner(jnp.stack([own_give, cross_pass]), "view", 0)
    tiles = lax.axis_size("tile")
    views = lax.axis_size("view")
    route = []
    for tile in range(tiles - 1):
        for slab in range(views // 2):
            right_core = tile * views + 2 * slab + 1
            left_core = (tile + 1) * views + 2 * slab
            route += [(right_core, left_core), (left_core, right_core)]
    outgoing = jnp.where(first, jnp.stack([cross_keep, got[1]]), jnp.stack([got[1], cross_keep]))
    outgoing, psf_taps = lax.optimization_barrier((outgoing, psf_taps))
    incoming = lax.ppermute(outgoing, ("tile", "view"), route)
    own_parts = jnp.where(first, jnp.stack([own_keep, got[0]]), jnp.stack([got[0], own_keep]))
    views_measured = own_parts + incoming
    observed = views_measured.astype(jnp.float32)
    estimate = 0.5 * (observed[0] + observed[1])
    kernels = (psf_taps / jnp.sum(psf_taps, axis=2, keepdims=True)).astype(jnp.bfloat16)
    view_count = kernels.shape[0]
    forward_ops = stacked_operators(kernels, planes, half_x, width_y)
    adjoint_ops = stacked_operators(kernels[:, :, ::-1], planes, half_x, width_y)
    for iteration in range(ITERS):
        estimate_low = estimate.astype(jnp.bfloat16)
        low, high = x_rims(estimate_low, reach, 1)
        extended = jnp.concatenate([low, estimate_low, high], axis=1)
        after_x = jnp.einsum(
            "vzpa,zay->vzpy", forward_ops[0], extended, preferred_element_type=jnp.float32
        ).astype(jnp.bfloat16)
        blurred = pass_z_views(pass_y_views(after_x, forward_ops[1]), forward_ops[2], reach)
        quotients = (observed / blurred).astype(jnp.bfloat16)
        low, high = x_rims(quotients, reach, 2)
        widened = jnp.concatenate([low, quotients, high], axis=2)
        after_x = jnp.einsum(
            "vzpa,vzay->vzpy", adjoint_ops[0], widened, preferred_element_type=jnp.float32
        ).astype(jnp.bfloat16)
        backs = pass_z_views(pass_y_views(after_x, adjoint_ops[1]), adjoint_ops[2], reach)
        estimate = estimate * (0.5 * (backs[0] + backs[1]))
    keep = lax.dynamic_slice_in_dim(estimate, view_bit * half_rows, half_rows, 0)
    give = lax.dynamic_slice_in_dim(estimate, (1 - view_bit) * half_rows, half_rows, 0)
    got = from_partner(give, "view", 0)
    first_half = jnp.where(view_bit == 0, keep, got)
    second_half = jnp.where(view_bit == 0, got, keep)
    return jnp.concatenate([first_half, second_half], axis=1)


def solution(mesh):
    in_specs = (P(("timepoin", "view"), "tile", None), P(), P(("timepoin", "view"), None))
    out_specs = P(("timepoin", "view"), "tile", None)
    return jax.shard_map(local, mesh=mesh, in_specs=in_specs, out_specs=out_specs, check_vma=False)
```

```python
import jax
import jax.numpy as jnp
from jax import lax
from jax.sharding import PartitionSpec as P

BX = 4
ITERS = 2


def shifted(block, axis, distance):
    devices = range(lax.axis_size(axis))
    route = [(i - distance, i) for i in devices if i - distance in devices]
    return lax.ppermute(block, axis, route)


def from_partner(block, axis, distance):
    count = lax.axis_size(axis)
    route = []
    for low in range(count):
        high = low | 1 << distance
        if high != low and high < count:
            route += [(low, high), (high, low)]
    return lax.ppermute(block, axis, route)


def extended_2(block, sides, width):
    for axis, dim in sides:
        count = lax.axis_size(axis)
        forward = [(i, i + 1) for i in range(count - 1)]
        backward = [(target, source) for source, target in forward]
        low = lax.ppermute(
            lax.slice_in_dim(block, block.shape[dim] - width, None, axis=dim), axis, forward
        )
        high = lax.ppermute(lax.slice_in_dim(block, 0, width, axis=dim), axis, backward)
        block = jnp.concatenate([low, block, high], axis=dim)
    return block


def band_matrix(kernel, row_count, col_count, base_shift):
    row_ids = lax.broadcasted_iota(jnp.int32, (row_count, col_count, 1), 0)
    col_ids = lax.broadcasted_iota(jnp.int32, (row_count, col_count, 1), 1)
    tap_ids = lax.broadcasted_iota(jnp.int32, (1, 1, kernel.shape[0]), 2)
    hit = row_ids - col_ids + base_shift == tap_ids
    taps = kernel.astype(jnp.float32)[None, None, :]
    matrix = jnp.sum(jnp.where(hit, taps, jnp.float32(0.0)), axis=2)
    return matrix.astype(jnp.bfloat16)


def operators(kernels, plane_count, width_x, width_y):
    reach = kernels.shape[1] // 2
    along_x = band_matrix(kernels[0], width_x + 2 * reach, width_x, 0).T
    along_x = jnp.broadcast_to(along_x[None], (plane_count,) + along_x.shape)
    return lax.optimization_barrier((
        along_x,
        band_matrix(kernels[1], width_y, width_y, reach),
        band_matrix(kernels[2], plane_count + 2 * reach, plane_count, 0).T,
    ))


def pass_xy(extended, matrices):
    width_y = extended.shape[2]
    after_x = jnp.einsum(
        "zpa,zay->zpy", matrices[0], extended, preferred_element_type=jnp.float32
    ).astype(jnp.bfloat16)
    after_y = jnp.dot(after_x.reshape(-1, width_y), matrices[1], preferred_element_type=jnp.float32)
    return after_y.reshape(after_x.shape).astype(jnp.bfloat16)


def pass_z(extended, matrix):
    planes = extended.shape[0]
    out = jnp.dot(matrix, extended.reshape(planes, -1), preferred_element_type=jnp.float32)
    return out.reshape((matrix.shape[0],) + extended.shape[1:])


def stacked_operators(kernels, plane_count, width_x, width_y):
    reach = kernels.shape[2] // 2
    views = range(kernels.shape[0])
    along_x = jnp.stack([band_matrix(kernels[v, 0], width_x + 2 * reach, width_x, 0).T for v in views])
    along_x = jnp.broadcast_to(along_x[:, None], (along_x.shape[0], plane_count) + along_x.shape[1:])
    return lax.optimization_barrier((
        along_x,
        jnp.stack([band_matrix(kernels[v, 1], width_y, width_y, reach) for v in views]),
        jnp.stack([band_matrix(kernels[v, 2], plane_count + 2 * reach, plane_count, 0).T for v in views]),
    ))


def pass_y_views(after_x, matrices):
    shape = after_x.shape
    flat = after_x.reshape(shape[0], -1, shape[-1])
    after_y = jnp.einsum("vmy,vyq->vmq", flat, matrices, preferred_element_type=jnp.float32)
    return after_y.reshape(shape).astype(jnp.bfloat16)


def pass_z_views(after_y, matrices, reach):
    below, above = z_rims(after_y, reach, 1)
    widened = jnp.concatenate([below, after_y, above], axis=1)
    return jnp.einsum("vpa,vaxy->vpxy", matrices, widened, preferred_element_type=jnp.float32)


def z_rims(volume, reach, axis):
    slabs = lax.axis_size("view") // 2
    slab = lax.axis_index("view") // 2
    planes = volume.shape[axis]
    shape = list(volume.shape)
    shape[axis] = reach
    below = jnp.zeros(shape, volume.dtype)
    above = below
    for phase in (0, 1):
        route = []
        for low in range(phase, slabs - 1, 2):
            for bit in (0, 1):
                route += [(2 * low + bit, 2 * low + 2 + bit), (2 * low + 2 + bit, 2 * low + bit)]
        if not route:
            continue
        is_lower = slab % 2 == phase
        top = lax.slice_in_dim(volume, planes - reach, planes, axis=axis)
        bottom = lax.slice_in_dim(volume, 0, reach, axis=axis)
        payload = jnp.where(is_lower, top, bottom)
        got = lax.ppermute(payload, "view", route)
        below = jnp.where(is_lower, below, got)
        above = jnp.where(is_lower, got, above)
    return below, above


def x_rims(block, reach, axis):
    tiles = lax.axis_size("tile")
    views = lax.axis_size("view")
    route = []
    for tile in range(tiles - 1):
        for slab in range(views // 2):
            right_core = tile * views + 2 * slab + 1
            left_core = (tile + 1) * views + 2 * slab
            route += [(right_core, left_core), (left_core, right_core)]
    first = lax.axis_index("view") % 2 == 0
    width = block.shape[axis]
    front = lax.slice_in_dim(block, 0, reach, axis=axis)
    back = lax.slice_in_dim(block, width - reach, width, axis=axis)
    outward = jnp.where(first, front, back)
    across = lax.ppermute(outward, ("tile", "view"), route)
    whole = from_partner(block, "view", 0)
    beside_low = lax.slice_in_dim(whole, width - reach, width, axis=axis)
    beside_high = lax.slice_in_dim(whole, 0, reach, axis=axis)
    low = jnp.where(first, across, beside_low)
    high = jnp.where(first, beside_high, across)
    return low, high


def local(acquired, psf_taps, block_source):
    planes, width_x, width_y = acquired.shape
    block_count = width_x // BX
    capacity = block_count // 2
    reach = psf_taps.shape[2] // 2
    tile_index = lax.axis_index("tile")
    tile_total = lax.axis_size("tile")
    view_bit = lax.axis_index("view") % 2
    sources = block_source[0]
    blocks = acquired.reshape(planes, block_count, BX, width_y)
    half_x = width_x // 2
    half_rows = planes // 2
    half_blocks = block_count // 2
    first = view_bit == 0
    starts = []
    for target, half in ((tile_index, 0), (tile_index, 1), (tile_index + 1, 0), (tile_index - 1, 1)):
        target = jnp.clip(target, 0, tile_total - 1)
        starts.append(target * block_count + half * half_blocks)
    slots = jnp.concatenate([lax.dynamic_slice_in_dim(sources, st, half_blocks) for st in starts])
    row_ids = jnp.arange(slots.shape[0] * BX, dtype=jnp.int32)
    row_slots = slots[row_ids // BX]
    source_x = (row_slots % block_count) * BX + row_ids % BX
    chosen_rows = (row_slots // block_count == tile_index)[:, None] & (
        source_x[:, None] == jnp.arange(width_x, dtype=jnp.int32)[None, :]
    )
    selection = jnp.broadcast_to(chosen_rows.astype(acquired.dtype)[None], (planes,) + chosen_rows.shape)
    partials = jnp.einsum(
        "zrx,zxy->zry", selection, acquired, preferred_element_type=jnp.float32
    ).astype(acquired.dtype)
    partials = partials.reshape(planes, 4, half_x, width_y)
    own_keep = jnp.where(first, partials[:, 0], partials[:, 1])
    own_give = jnp.where(first, partials[:, 1], partials[:, 0])
    cross_keep = jnp.where(first, partials[:, 3], partials[:, 2])
    cross_pass = jnp.where(first, partials[:, 2], partials[:, 3])
    got = from_partner(jnp.stack([own_give, cross_pass]), "view", 0)
    tiles = lax.axis_size("tile")
    views = lax.axis_size("view")
    route = []
    for tile in range(tiles - 1):
        for slab in range(views // 2):
            right_core = tile * views + 2 * slab + 1
            left_core = (tile + 1) * views + 2 * slab
            route += [(right_core, left_core), (left_core, right_core)]
    outgoing = jnp.where(first, jnp.stack([cross_keep, got[1]]), jnp.stack([got[1], cross_keep]))
    outgoing, psf_taps = lax.optimization_barrier((outgoing, psf_taps))
    incoming = lax.ppermute(outgoing, ("tile", "view"), route)
    own_parts = jnp.where(first, jnp.stack([own_keep, got[0]]), jnp.stack([got[0], own_keep]))
    views_measured = own_parts + incoming
    observed = views_measured.astype(jnp.float32)
    estimate = 0.5 * (observed[0] + observed[1])
    kernels = (psf_taps / jnp.sum(psf_taps, axis=2, keepdims=True)).astype(jnp.bfloat16)
    view_count = kernels.shape[0]
    forward_ops = stacked_operators(kernels, planes, half_x, width_y)
    adjoint_ops = stacked_operators(kernels[:, :, ::-1], planes, half_x, width_y)
    for iteration in range(ITERS):
        estimate_low = estimate.astype(jnp.bfloat16)
        low, high = x_rims(estimate_low, reach, 1)
        extended = jnp.concatenate([low, estimate_low, high], axis=1)
        after_x = jnp.einsum(
            "vzpa,zay->vzpy", forward_ops[0], extended, preferred_element_type=jnp.float32
        ).astype(jnp.bfloat16)
        blurred = pass_z_views(pass_y_views(after_x, forward_ops[1]), forward_ops[2], reach)
        quotients = (observed / blurred).astype(jnp.bfloat16)
        low, high = x_rims(quotients, reach, 2)
        widened = jnp.concatenate([low, quotients, high], axis=2)
        after_x = jnp.einsum(
            "vzpa,vzay->vzpy", adjoint_ops[0], widened, preferred_element_type=jnp.float32
        ).astype(jnp.bfloat16)
        backs = pass_z_views(pass_y_views(after_x, adjoint_ops[1]), adjoint_ops[2], reach)
        estimate = estimate * (0.5 * (backs[0] + backs[1]))
    keep = lax.dynamic_slice_in_dim(estimate, view_bit * half_rows, half_rows, 0)
    give = lax.dynamic_slice_in_dim(estimate, (1 - view_bit) * half_rows, half_rows, 0)
    got = from_partner(give, "view", 0)
    first_half = jnp.where(view_bit == 0, keep, got)
    second_half = jnp.where(view_bit == 0, got, keep)
    return jnp.concatenate([first_half, second_half], axis=1)


def solution(mesh):
    in_specs = (P(("timepoin", "view"), "tile", None), P(), P(("timepoin", "view"), None))
    out_specs = P(("timepoin", "view"), "tile", None)
    return jax.shard_map(local, mesh=mesh, in_specs=in_specs, out_specs=out_specs, check_vma=False)
```

```python
import jax
import jax.numpy as jnp
from jax import lax
from jax.sharding import PartitionSpec as P

BX = 4
ITERS = 2


def shifted(block, axis, distance):
    devices = range(lax.axis_size(axis))
    route = [(i - distance, i) for i in devices if i - distance in devices]
    return lax.ppermute(block, axis, route)


def from_partner(block, axis, distance):
    count = lax.axis_size(axis)
    route = []
    for low in range(count):
        high = low | 1 << distance
        if high != low and high < count:
            route += [(low, high), (high, low)]
    return lax.ppermute(block, axis, route)


def extended_2(block, sides, width):
    for axis, dim in sides:
        count = lax.axis_size(axis)
        forward = [(i, i + 1) for i in range(count - 1)]
        backward = [(target, source) for source, target in forward]
        low = lax.ppermute(
            lax.slice_in_dim(block, block.shape[dim] - width, None, axis=dim), axis, forward
        )
        high = lax.ppermute(lax.slice_in_dim(block, 0, width, axis=dim), axis, backward)
        block = jnp.concatenate([low, block, high], axis=dim)
    return block


def band_matrix(kernel, row_count, col_count, base_shift):
    row_ids = lax.broadcasted_iota(jnp.int32, (row_count, col_count, 1), 0)
    col_ids = lax.broadcasted_iota(jnp.int32, (row_count, col_count, 1), 1)
    tap_ids = lax.broadcasted_iota(jnp.int32, (1, 1, kernel.shape[0]), 2)
    hit = row_ids - col_ids + base_shift == tap_ids
    taps = kernel.astype(jnp.float32)[None, None, :]
    matrix = jnp.sum(jnp.where(hit, taps, jnp.float32(0.0)), axis=2)
    return matrix.astype(jnp.bfloat16)


def operators(kernels, plane_count, width_x, width_y):
    reach = kernels.shape[1] // 2
    along_x = band_matrix(kernels[0], width_x + 2 * reach, width_x, 0).T
    along_x = jnp.broadcast_to(along_x[None], (plane_count,) + along_x.shape)
    return lax.optimization_barrier((
        along_x,
        band_matrix(kernels[1], width_y, width_y, reach),
        band_matrix(kernels[2], plane_count + 2 * reach, plane_count, 0).T,
    ))


def pass_xy(extended, matrices):
    width_y = extended.shape[2]
    after_x = jnp.einsum(
        "zpa,zay->zpy", matrices[0], extended, preferred_element_type=jnp.float32
    ).astype(jnp.bfloat16)
    after_y = jnp.dot(after_x.reshape(-1, width_y), matrices[1], preferred_element_type=jnp.float32)
    return after_y.reshape(after_x.shape).astype(jnp.bfloat16)


def pass_z(extended, matrix):
    planes = extended.shape[0]
    out = jnp.dot(matrix, extended.reshape(planes, -1), preferred_element_type=jnp.float32)
    return out.reshape((matrix.shape[0],) + extended.shape[1:])


def stacked_operators(kernels, plane_count, width_x, width_y):
    reach = kernels.shape[2] // 2
    views = range(kernels.shape[0])
    along_x = jnp.stack([band_matrix(kernels[v, 0], width_x + 2 * reach, width_x, 0).T for v in views])
    along_x = jnp.broadcast_to(along_x[:, None], (along_x.shape[0], plane_count) + along_x.shape[1:])
    return lax.optimization_barrier((
        along_x,
        jnp.stack([band_matrix(kernels[v, 1], width_y, width_y, reach) for v in views]),
        jnp.stack([band_matrix(kernels[v, 2], plane_count + 2 * reach, plane_count, 0).T for v in views]),
    ))


def pass_y_views(after_x, matrices):
    shape = after_x.shape
    flat = after_x.reshape(shape[0], -1, shape[-1])
    after_y = jnp.einsum("vmy,vyq->vmq", flat, matrices, preferred_element_type=jnp.float32)
    return after_y.reshape(shape).astype(jnp.bfloat16)


def pass_z_views(after_y, matrices, reach):
    below, above = z_rims(after_y, reach, 1)
    widened = jnp.concatenate([below, after_y, above], axis=1)
    return jnp.einsum("vpa,vaxy->vpxy", matrices, widened, preferred_element_type=jnp.float32)


def z_rims(volume, reach, axis):
    slabs = lax.axis_size("view") // 2
    slab = lax.axis_index("view") // 2
    planes = volume.shape[axis]
    shape = list(volume.shape)
    shape[axis] = reach
    below = jnp.zeros(shape, volume.dtype)
    above = below
    for phase in (0, 1):
        route = []
        for low in range(phase, slabs - 1, 2):
            for bit in (0, 1):
                route += [(2 * low + bit, 2 * low + 2 + bit), (2 * low + 2 + bit, 2 * low + bit)]
        if not route:
            continue
        is_lower = slab % 2 == phase
        top = lax.slice_in_dim(volume, planes - reach, planes, axis=axis)
        bottom = lax.slice_in_dim(volume, 0, reach, axis=axis)
        payload = jnp.where(is_lower, top, bottom)
        got = lax.ppermute(payload, "view", route)
        below = jnp.where(is_lower, below, got)
        above = jnp.where(is_lower, got, above)
    return below, above


def x_rims(block, reach, axis):
    tiles = lax.axis_size("tile")
    views = lax.axis_size("view")
    route = []
    for tile in range(tiles - 1):
        for slab in range(views // 2):
            right_core = tile * views + 2 * slab + 1
            left_core = (tile + 1) * views + 2 * slab
            route += [(right_core, left_core), (left_core, right_core)]
    first = lax.axis_index("view") % 2 == 0
    width = block.shape[axis]
    front = lax.slice_in_dim(block, 0, reach, axis=axis)
    back = lax.slice_in_dim(block, width - reach, width, axis=axis)
    outward = jnp.where(first, front, back)
    inward = jnp.where(first, back, front)
    across = lax.ppermute(outward, ("tile", "view"), route)
    beside = from_partner(inward, "view", 0)
    low = jnp.where(first, across, beside)
    high = jnp.where(first, beside, across)
    return low, high


def local(acquired, psf_taps, block_source):
    planes, width_x, width_y = acquired.shape
    block_count = width_x // BX
    capacity = block_count // 2
    reach = psf_taps.shape[2] // 2
    tile_index = lax.axis_index("tile")
    tile_total = lax.axis_size("tile")
    view_bit = lax.axis_index("view") % 2
    sources = block_source[0]
    blocks = acquired.reshape(planes, block_count, BX, width_y)
    half_x = width_x // 2
    half_rows = planes // 2
    half_blocks = block_count // 2
    first = view_bit == 0
    starts = []
    for target, half in ((tile_index, 0), (tile_index, 1), (tile_index + 1, 0), (tile_index - 1, 1)):
        target = jnp.clip(target, 0, tile_total - 1)
        starts.append(target * block_count + half * half_blocks)
    slots = jnp.concatenate([lax.dynamic_slice_in_dim(sources, st, half_blocks) for st in starts])
    row_ids = jnp.arange(slots.shape[0] * BX, dtype=jnp.int32)
    row_slots = slots[row_ids // BX]
    source_x = (row_slots % block_count) * BX + row_ids % BX
    chosen_rows = (row_slots // block_count == tile_index)[:, None] & (
        source_x[:, None] == jnp.arange(width_x, dtype=jnp.int32)[None, :]
    )
    selection = jnp.broadcast_to(chosen_rows.astype(acquired.dtype)[None], (planes,) + chosen_rows.shape)
    partials = jnp.einsum(
        "zrx,zxy->zry", selection, acquired, preferred_element_type=jnp.float32
    ).astype(acquired.dtype)
    partials = partials.reshape(planes, 4, half_x, width_y)
    own_keep = jnp.where(first, partials[:, 0], partials[:, 1])
    own_give = jnp.where(first, partials[:, 1], partials[:, 0])
    cross_keep = jnp.where(first, partials[:, 3], partials[:, 2])
    cross_pass = jnp.where(first, partials[:, 2], partials[:, 3])
    got = from_partner(jnp.stack([own_give, cross_pass]), "view", 0)
    tiles = lax.axis_size("tile")
    views = lax.axis_size("view")
    route = []
    for tile in range(tiles - 1):
        for slab in range(views // 2):
            right_core = tile * views + 2 * slab + 1
            left_core = (tile + 1) * views + 2 * slab
            route += [(right_core, left_core), (left_core, right_core)]
    outgoing = jnp.stack([cross_keep, got[1]])
    outgoing, psf_taps = lax.optimization_barrier((outgoing, psf_taps))
    arrived = lax.ppermute(outgoing, ("tile", "view"), route)
    local = jnp.stack([own_keep, got[0]]) + arrived[::-1]
    views_measured = jnp.where(first, local, local[::-1])
    observed = views_measured.astype(jnp.float32)
    estimate = 0.5 * (observed[0] + observed[1])
    kernels = (psf_taps / jnp.sum(psf_taps, axis=2, keepdims=True)).astype(jnp.bfloat16)
    view_count = kernels.shape[0]
    forward_ops = stacked_operators(kernels, planes, half_x, width_y)
    adjoint_ops = stacked_operators(kernels[:, :, ::-1], planes, half_x, width_y)
    for iteration in range(ITERS):
        estimate_low = estimate.astype(jnp.bfloat16)
        low, high = x_rims(estimate_low, reach, 1)
        extended = jnp.concatenate([low, estimate_low, high], axis=1)
        after_x = jnp.einsum(
            "vzpa,zay->vzpy", forward_ops[0], extended, preferred_element_type=jnp.float32
        ).astype(jnp.bfloat16)
        blurred = pass_z_views(pass_y_views(after_x, forward_ops[1]), forward_ops[2], reach)
        quotients = (observed / blurred).astype(jnp.bfloat16)
        low, high = x_rims(quotients, reach, 2)
        widened = jnp.concatenate([low, quotients, high], axis=2)
        after_x = jnp.einsum(
            "vzpa,vzay->vzpy", adjoint_ops[0], widened, preferred_element_type=jnp.float32
        ).astype(jnp.bfloat16)
        backs = pass_z_views(pass_y_views(after_x, adjoint_ops[1]), adjoint_ops[2], reach)
        estimate = estimate * (0.5 * (backs[0] + backs[1]))
    keep = lax.dynamic_slice_in_dim(estimate, view_bit * half_rows, half_rows, 0)
    give = lax.dynamic_slice_in_dim(estimate, (1 - view_bit) * half_rows, half_rows, 0)
    got = from_partner(give, "view", 0)
    first_half = jnp.where(view_bit == 0, keep, got)
    second_half = jnp.where(view_bit == 0, got, keep)
    return jnp.concatenate([first_half, second_half], axis=1)


def solution(mesh):
    in_specs = (P(("timepoin", "view"), "tile", None), P(), P(("timepoin", "view"), None))
    out_specs = P(("timepoin", "view"), "tile", None)
    return jax.shard_map(local, mesh=mesh, in_specs=in_specs, out_specs=out_specs, check_vma=False)
```

```python
import jax
import jax.numpy as jnp
from jax import lax
from jax.sharding import PartitionSpec as P

BX = 4
ITERS = 2


def shifted(block, axis, distance):
    devices = range(lax.axis_size(axis))
    route = [(i - distance, i) for i in devices if i - distance in devices]
    return lax.ppermute(block, axis, route)


def from_partner(block, axis, distance):
    count = lax.axis_size(axis)
    route = []
    for low in range(count):
        high = low | 1 << distance
        if high != low and high < count:
            route += [(low, high), (high, low)]
    return lax.ppermute(block, axis, route)


def extended_2(block, sides, width):
    for axis, dim in sides:
        count = lax.axis_size(axis)
        forward = [(i, i + 1) for i in range(count - 1)]
        backward = [(target, source) for source, target in forward]
        low = lax.ppermute(
            lax.slice_in_dim(block, block.shape[dim] - width, None, axis=dim), axis, forward
        )
        high = lax.ppermute(lax.slice_in_dim(block, 0, width, axis=dim), axis, backward)
        block = jnp.concatenate([low, block, high], axis=dim)
    return block


def band_matrix(kernel, row_count, col_count, base_shift):
    row_ids = lax.broadcasted_iota(jnp.int32, (row_count, col_count, 1), 0)
    col_ids = lax.broadcasted_iota(jnp.int32, (row_count, col_count, 1), 1)
    tap_ids = lax.broadcasted_iota(jnp.int32, (1, 1, kernel.shape[0]), 2)
    hit = row_ids - col_ids + base_shift == tap_ids
    taps = kernel.astype(jnp.float32)[None, None, :]
    matrix = jnp.sum(jnp.where(hit, taps, jnp.float32(0.0)), axis=2)
    return matrix.astype(jnp.bfloat16)


def operators(kernels, plane_count, width_x, width_y):
    reach = kernels.shape[1] // 2
    along_x = band_matrix(kernels[0], width_x + 2 * reach, width_x, 0).T
    along_x = jnp.broadcast_to(along_x[None], (plane_count,) + along_x.shape)
    return lax.optimization_barrier((
        along_x,
        band_matrix(kernels[1], width_y, width_y, reach),
        band_matrix(kernels[2], plane_count + 2 * reach, plane_count, 0).T,
    ))


def pass_xy(extended, matrices):
    width_y = extended.shape[2]
    after_x = jnp.einsum(
        "zpa,zay->zpy", matrices[0], extended, preferred_element_type=jnp.float32
    ).astype(jnp.bfloat16)
    after_y = jnp.dot(after_x.reshape(-1, width_y), matrices[1], preferred_element_type=jnp.float32)
    return after_y.reshape(after_x.shape).astype(jnp.bfloat16)


def pass_z(extended, matrix):
    planes = extended.shape[0]
    out = jnp.dot(matrix, extended.reshape(planes, -1), preferred_element_type=jnp.float32)
    return out.reshape((matrix.shape[0],) + extended.shape[1:])


def stacked_operators(kernels, plane_count, width_x, width_y):
    reach = kernels.shape[2] // 2
    views = range(kernels.shape[0])
    along_x = jnp.stack([band_matrix(kernels[v, 0], width_x + 2 * reach, width_x, 0).T for v in views])
    along_x = jnp.broadcast_to(along_x[:, None], (along_x.shape[0], plane_count) + along_x.shape[1:])
    return lax.optimization_barrier((
        along_x,
        jnp.stack([band_matrix(kernels[v, 1], width_y, width_y, reach) for v in views]),
        jnp.stack([band_matrix(kernels[v, 2], plane_count + 2 * reach, plane_count, 0).T for v in views]),
    ))


def pass_y_views(after_x, matrices):
    shape = after_x.shape
    flat = after_x.reshape(shape[0], -1, shape[-1])
    after_y = jnp.einsum("vmy,vyq->vmq", flat, matrices, preferred_element_type=jnp.float32)
    return after_y.reshape(shape).astype(jnp.bfloat16)


def pass_z_views(after_y, matrices, reach):
    below, above = z_rims(after_y, reach, 1)
    widened = jnp.concatenate([below, after_y, above], axis=1)
    return jnp.einsum("vpa,vaxy->vpxy", matrices, widened, preferred_element_type=jnp.float32)


def z_rims(volume, reach, axis):
    slabs = lax.axis_size("view") // 2
    slab = lax.axis_index("view") // 2
    planes = volume.shape[axis]
    shape = list(volume.shape)
    shape[axis] = reach
    below = jnp.zeros(shape, volume.dtype)
    above = below
    for phase in (0, 1):
        route = []
        for low in range(phase, slabs - 1, 2):
            for bit in (0, 1):
                route += [(2 * low + bit, 2 * low + 2 + bit), (2 * low + 2 + bit, 2 * low + bit)]
        if not route:
            continue
        is_lower = slab % 2 == phase
        top = lax.slice_in_dim(volume, planes - reach, planes, axis=axis)
        bottom = lax.slice_in_dim(volume, 0, reach, axis=axis)
        payload = jnp.where(is_lower, top, bottom)
        got = lax.ppermute(payload, "view", route)
        below = jnp.where(is_lower, below, got)
        above = jnp.where(is_lower, got, above)
    return below, above


def x_rims(block, reach, axis):
    tiles = lax.axis_size("tile")
    views = lax.axis_size("view")
    route = []
    for tile in range(tiles - 1):
        for slab in range(views // 2):
            right_core = tile * views + 2 * slab + 1
            left_core = (tile + 1) * views + 2 * slab
            route += [(right_core, left_core), (left_core, right_core)]
    first = lax.axis_index("view") % 2 == 0
    width = block.shape[axis]
    front = lax.slice_in_dim(block, 0, reach, axis=axis)
    back = lax.slice_in_dim(block, width - reach, width, axis=axis)
    outward = jnp.where(first, front, back)
    inward = jnp.where(first, back, front)
    across = lax.ppermute(outward, ("tile", "view"), route)
    beside = from_partner(inward, "view", 0)
    low = jnp.where(first, across, beside)
    high = jnp.where(first, beside, across)
    return low, high


def local(acquired, psf_taps, block_source):
    planes, width_x, width_y = acquired.shape
    block_count = width_x // BX
    capacity = block_count // 2
    reach = psf_taps.shape[2] // 2
    tile_index = lax.axis_index("tile")
    tile_total = lax.axis_size("tile")
    view_bit = lax.axis_index("view") % 2
    sources = block_source[0]
    blocks = acquired.reshape(planes, block_count, BX, width_y)
    half_x = width_x // 2
    half_rows = planes // 2
    half_blocks = block_count // 2
    first = view_bit == 0
    starts = []
    for target, half in ((tile_index, 0), (tile_index, 1), (tile_index + 1, 0), (tile_index - 1, 1)):
        target = jnp.clip(target, 0, tile_total - 1)
        starts.append(target * block_count + half * half_blocks)
    slots = jnp.concatenate([lax.dynamic_slice_in_dim(sources, st, half_blocks) for st in starts])
    row_ids = jnp.arange(slots.shape[0] * BX, dtype=jnp.int32)
    row_slots = slots[row_ids // BX]
    source_x = (row_slots % block_count) * BX + row_ids % BX
    chosen_rows = (row_slots // block_count == tile_index)[:, None] & (
        source_x[:, None] == jnp.arange(width_x, dtype=jnp.int32)[None, :]
    )
    selection = jnp.broadcast_to(chosen_rows.astype(acquired.dtype)[None], (planes,) + chosen_rows.shape)
    partials = jnp.einsum(
        "zrx,zxy->zry", selection, acquired, preferred_element_type=jnp.float32
    ).astype(acquired.dtype)
    partials = partials.reshape(planes, 4, half_x, width_y)
    own_keep = jnp.where(first, partials[:, 0], partials[:, 1])
    own_give = jnp.where(first, partials[:, 1], partials[:, 0])
    cross_keep = jnp.where(first, partials[:, 3], partials[:, 2])
    cross_pass = jnp.where(first, partials[:, 2], partials[:, 3])
    got = from_partner(jnp.stack([own_give, cross_pass]), "view", 0)
    tiles = lax.axis_size("tile")
    views = lax.axis_size("view")
    route = []
    for tile in range(tiles - 1):
        for slab in range(views // 2):
            right_core = tile * views + 2 * slab + 1
            left_core = (tile + 1) * views + 2 * slab
            route += [(right_core, left_core), (left_core, right_core)]
    outgoing = jnp.stack([cross_keep, got[1]])
    outgoing, psf_taps = lax.optimization_barrier((outgoing, psf_taps))
    arrived = lax.ppermute(outgoing, ("tile", "view"), route)
    local = jnp.stack([own_keep, got[0]]) + arrived[::-1]
    views_measured = jnp.where(first, local, local[::-1])
    observed = views_measured.astype(jnp.float32)
    estimate = 0.5 * (observed[0] + observed[1])
    kernels = (psf_taps / jnp.sum(psf_taps, axis=2, keepdims=True)).astype(jnp.bfloat16)
    view_count = kernels.shape[0]
    forward_ops = stacked_operators(kernels, planes, half_x, width_y)
    adjoint_ops = stacked_operators(kernels[:, :, ::-1], planes, half_x, width_y)
    for iteration in range(ITERS):
        estimate_low = estimate.astype(jnp.bfloat16)
        low, high = x_rims(estimate_low, reach, 1)
        extended = jnp.concatenate([low, estimate_low, high], axis=1)
        after_x = jnp.einsum(
            "vzpa,zay->vzpy", forward_ops[0], extended, preferred_element_type=jnp.float32
        ).astype(jnp.bfloat16)
        blurred = pass_z_views(pass_y_views(after_x, forward_ops[1]), forward_ops[2], reach)
        quotients = (observed / blurred).astype(jnp.bfloat16)
        low, high = x_rims(quotients, reach, 2)
        widened = jnp.concatenate([low, quotients, high], axis=2)
        after_x = jnp.einsum(
            "vzpa,vzay->vzpy", adjoint_ops[0], widened, preferred_element_type=jnp.float32
        ).astype(jnp.bfloat16)
        backs = pass_z_views(pass_y_views(after_x, adjoint_ops[1]), adjoint_ops[2], reach)
        estimate = estimate * (0.5 * (backs[0] + backs[1]))
    keep = lax.dynamic_slice_in_dim(estimate, view_bit * half_rows, half_rows, 0)
    give = lax.dynamic_slice_in_dim(estimate, (1 - view_bit) * half_rows, half_rows, 0)
    got = from_partner(give, "view", 0)
    both = jnp.concatenate([keep, got, keep], axis=1)
    return lax.dynamic_slice_in_dim(both, view_bit * half_x, width_x, 1)


def solution(mesh):
    in_specs = (P(("timepoin", "view"), "tile", None), P(), P(("timepoin", "view"), None))
    out_specs = P(("timepoin", "view"), "tile", None)
    return jax.shard_map(local, mesh=mesh, in_specs=in_specs, out_specs=out_specs, check_vma=False)
```

```python
import jax
import jax.numpy as jnp
from jax import lax
from jax.sharding import PartitionSpec as P

BX = 4
ITERS = 2


def shifted(block, axis, distance):
    devices = range(lax.axis_size(axis))
    route = [(i - distance, i) for i in devices if i - distance in devices]
    return lax.ppermute(block, axis, route)


def from_partner(block, axis, distance):
    count = lax.axis_size(axis)
    route = []
    for low in range(count):
        high = low | 1 << distance
        if high != low and high < count:
            route += [(low, high), (high, low)]
    return lax.ppermute(block, axis, route)


def extended_2(block, sides, width):
    for axis, dim in sides:
        count = lax.axis_size(axis)
        forward = [(i, i + 1) for i in range(count - 1)]
        backward = [(target, source) for source, target in forward]
        low = lax.ppermute(
            lax.slice_in_dim(block, block.shape[dim] - width, None, axis=dim), axis, forward
        )
        high = lax.ppermute(lax.slice_in_dim(block, 0, width, axis=dim), axis, backward)
        block = jnp.concatenate([low, block, high], axis=dim)
    return block


def band_matrix(kernel, row_count, col_count, base_shift):
    row_ids = lax.broadcasted_iota(jnp.int32, (row_count, col_count, 1), 0)
    col_ids = lax.broadcasted_iota(jnp.int32, (row_count, col_count, 1), 1)
    tap_ids = lax.broadcasted_iota(jnp.int32, (1, 1, kernel.shape[0]), 2)
    hit = row_ids - col_ids + base_shift == tap_ids
    taps = kernel.astype(jnp.float32)[None, None, :]
    matrix = jnp.sum(jnp.where(hit, taps, jnp.float32(0.0)), axis=2)
    return matrix.astype(jnp.bfloat16)


def operators(kernels, plane_count, width_x, width_y):
    reach = kernels.shape[1] // 2
    along_x = band_matrix(kernels[0], width_x + 2 * reach, width_x, 0).T
    along_x = jnp.broadcast_to(along_x[None], (plane_count,) + along_x.shape)
    return lax.optimization_barrier((
        along_x,
        band_matrix(kernels[1], width_y, width_y, reach),
        band_matrix(kernels[2], plane_count + 2 * reach, plane_count, 0).T,
    ))


def pass_xy(extended, matrices):
    width_y = extended.shape[2]
    after_x = jnp.einsum(
        "zpa,zay->zpy", matrices[0], extended, preferred_element_type=jnp.float32
    ).astype(jnp.bfloat16)
    after_y = jnp.dot(after_x.reshape(-1, width_y), matrices[1], preferred_element_type=jnp.float32)
    return after_y.reshape(after_x.shape).astype(jnp.bfloat16)


def pass_z(extended, matrix):
    planes = extended.shape[0]
    out = jnp.dot(matrix, extended.reshape(planes, -1), preferred_element_type=jnp.float32)
    return out.reshape((matrix.shape[0],) + extended.shape[1:])


def stacked_operators(kernels, plane_count, width_x, width_y):
    reach = kernels.shape[2] // 2
    views = range(kernels.shape[0])
    along_x = jnp.stack([band_matrix(kernels[v, 0], width_x + 2 * reach, width_x, 0).T for v in views])
    along_x = jnp.broadcast_to(along_x[:, None], (along_x.shape[0], plane_count) + along_x.shape[1:])
    return lax.optimization_barrier((
        along_x,
        jnp.stack([band_matrix(kernels[v, 1], width_y, width_y, reach) for v in views]),
        jnp.stack([band_matrix(kernels[v, 2], plane_count + 2 * reach, plane_count, 0).T for v in views]),
    ))


def pass_y_views(after_x, matrices):
    shape = after_x.shape
    flat = after_x.reshape(shape[0], -1, shape[-1])
    after_y = jnp.einsum("vmy,vyq->vmq", flat, matrices, preferred_element_type=jnp.float32)
    return after_y.reshape(shape).astype(jnp.bfloat16)


def pass_z_views(after_y, matrices, reach):
    below, above = z_rims(after_y, reach, 1)
    widened = jnp.concatenate([below, after_y, above], axis=1)
    return jnp.einsum("vpa,vaxy->vpxy", matrices, widened, preferred_element_type=jnp.float32)


def z_rims(volume, reach, axis):
    slabs = lax.axis_size("view") // 2
    slab = lax.axis_index("view") // 2
    planes = volume.shape[axis]
    shape = list(volume.shape)
    shape[axis] = reach
    below = jnp.zeros(shape, volume.dtype)
    above = below
    for phase in (0, 1):
        route = []
        for low in range(phase, slabs - 1, 2):
            for bit in (0, 1):
                route += [(2 * low + bit, 2 * low + 2 + bit), (2 * low + 2 + bit, 2 * low + bit)]
        if not route:
            continue
        is_lower = slab % 2 == phase
        top = lax.slice_in_dim(volume, planes - reach, planes, axis=axis)
        bottom = lax.slice_in_dim(volume, 0, reach, axis=axis)
        payload = jnp.where(is_lower, top, bottom)
        got = lax.ppermute(payload, "view", route)
        below = jnp.where(is_lower, below, got)
        above = jnp.where(is_lower, got, above)
    return below, above


def x_rims(block, reach, axis):
    tiles = lax.axis_size("tile")
    views = lax.axis_size("view")
    route = []
    for tile in range(tiles - 1):
        for slab in range(views // 2):
            right_core = tile * views + 2 * slab + 1
            left_core = (tile + 1) * views + 2 * slab
            route += [(right_core, left_core), (left_core, right_core)]
    first = lax.axis_index("view") % 2 == 0
    width = block.shape[axis]
    front = lax.slice_in_dim(block, 0, reach, axis=axis)
    back = lax.slice_in_dim(block, width - reach, width, axis=axis)
    outward = jnp.where(first, front, back)
    inward = jnp.where(first, back, front)
    across = lax.ppermute(outward, ("tile", "view"), route)
    beside = from_partner(inward, "view", 0)
    low = jnp.where(first, across, beside)
    high = jnp.where(first, beside, across)
    return low, high


def local(acquired, psf_taps, block_source):
    planes, width_x, width_y = acquired.shape
    block_count = width_x // BX
    capacity = block_count // 2
    reach = psf_taps.shape[2] // 2
    tile_index = lax.axis_index("tile")
    tile_total = lax.axis_size("tile")
    view_bit = lax.axis_index("view") % 2
    sources = block_source[0]
    blocks = acquired.reshape(planes, block_count, BX, width_y)
    half_x = width_x // 2
    half_rows = planes // 2
    half_blocks = block_count // 2
    first = view_bit == 0
    starts = []
    for target, half in ((tile_index, 0), (tile_index, 1), (tile_index + 1, 0), (tile_index - 1, 1)):
        target = jnp.clip(target, 0, tile_total - 1)
        starts.append(target * block_count + half * half_blocks)
    groups = [lax.dynamic_slice_in_dim(sources, st, half_blocks) for st in starts]
    first = view_bit == 0
    slots = jnp.where(
        first,
        jnp.concatenate([groups[0], groups[1], groups[3], groups[2]]),
        jnp.concatenate([groups[1], groups[0], groups[2], groups[3]]),
    )
    row_ids = jnp.arange(slots.shape[0] * BX, dtype=jnp.int32)
    row_slots = slots[row_ids // BX]
    source_x = (row_slots % block_count) * BX + row_ids % BX
    chosen_rows = (row_slots // block_count == tile_index)[:, None] & (
        source_x[:, None] == jnp.arange(width_x, dtype=jnp.int32)[None, :]
    )
    selection = jnp.broadcast_to(chosen_rows.astype(acquired.dtype)[None], (planes,) + chosen_rows.shape)
    partials = jnp.einsum(
        "zrx,zxy->zry", selection, acquired, preferred_element_type=jnp.float32
    ).astype(acquired.dtype)
    partials = partials.reshape(planes, 4, half_x, width_y)
    own_keep = partials[:, 0]
    own_give = partials[:, 1]
    cross_keep = partials[:, 2]
    cross_pass = partials[:, 3]
    got = from_partner(jnp.stack([own_give, cross_pass]), "view", 0)
    tiles = lax.axis_size("tile")
    views = lax.axis_size("view")
    route = []
    for tile in range(tiles - 1):
        for slab in range(views // 2):
            right_core = tile * views + 2 * slab + 1
            left_core = (tile + 1) * views + 2 * slab
            route += [(right_core, left_core), (left_core, right_core)]
    outgoing = jnp.stack([cross_keep, got[1]])
    outgoing, psf_taps = lax.optimization_barrier((outgoing, psf_taps))
    arrived = lax.ppermute(outgoing, ("tile", "view"), route)
    local = jnp.stack([own_keep, got[0]]) + arrived[::-1]
    views_measured = jnp.where(first, local, local[::-1])
    observed = views_measured.astype(jnp.float32)
    estimate = 0.5 * (observed[0] + observed[1])
    kernels = (psf_taps / jnp.sum(psf_taps, axis=2, keepdims=True)).astype(jnp.bfloat16)
    view_count = kernels.shape[0]
    forward_ops = stacked_operators(kernels, planes, half_x, width_y)
    adjoint_ops = stacked_operators(kernels[:, :, ::-1], planes, half_x, width_y)
    for iteration in range(ITERS):
        estimate_low = estimate.astype(jnp.bfloat16)
        low, high = x_rims(estimate_low, reach, 1)
        extended = jnp.concatenate([low, estimate_low, high], axis=1)
        after_x = jnp.einsum(
            "vzpa,zay->vzpy", forward_ops[0], extended, preferred_element_type=jnp.float32
        ).astype(jnp.bfloat16)
        blurred = pass_z_views(pass_y_views(after_x, forward_ops[1]), forward_ops[2], reach)
        quotients = (observed / blurred).astype(jnp.bfloat16)
        low, high = x_rims(quotients, reach, 2)
        widened = jnp.concatenate([low, quotients, high], axis=2)
        after_x = jnp.einsum(
            "vzpa,vzay->vzpy", adjoint_ops[0], widened, preferred_element_type=jnp.float32
        ).astype(jnp.bfloat16)
        backs = pass_z_views(pass_y_views(after_x, adjoint_ops[1]), adjoint_ops[2], reach)
        estimate = estimate * (0.5 * (backs[0] + backs[1]))
    keep = lax.dynamic_slice_in_dim(estimate, view_bit * half_rows, half_rows, 0)
    give = lax.dynamic_slice_in_dim(estimate, (1 - view_bit) * half_rows, half_rows, 0)
    got = from_partner(give, "view", 0)
    both = jnp.concatenate([keep, got, keep], axis=1)
    return lax.dynamic_slice_in_dim(both, view_bit * half_x, width_x, 1)


def solution(mesh):
    in_specs = (P(("timepoin", "view"), "tile", None), P(), P(("timepoin", "view"), None))
    out_specs = P(("timepoin", "view"), "tile", None)
    return jax.shard_map(local, mesh=mesh, in_specs=in_specs, out_specs=out_specs, check_vma=False)
```

```python
import jax
import jax.numpy as jnp
from jax import lax
from jax.sharding import PartitionSpec as P

BX = 4
ITERS = 2


def shifted(block, axis, distance):
    devices = range(lax.axis_size(axis))
    route = [(i - distance, i) for i in devices if i - distance in devices]
    return lax.ppermute(block, axis, route)


def from_partner(block, axis, distance):
    count = lax.axis_size(axis)
    route = []
    for low in range(count):
        high = low | 1 << distance
        if high != low and high < count:
            route += [(low, high), (high, low)]
    return lax.ppermute(block, axis, route)


def extended_2(block, sides, width):
    for axis, dim in sides:
        count = lax.axis_size(axis)
        forward = [(i, i + 1) for i in range(count - 1)]
        backward = [(target, source) for source, target in forward]
        low = lax.ppermute(
            lax.slice_in_dim(block, block.shape[dim] - width, None, axis=dim), axis, forward
        )
        high = lax.ppermute(lax.slice_in_dim(block, 0, width, axis=dim), axis, backward)
        block = jnp.concatenate([low, block, high], axis=dim)
    return block


def band_matrix(kernel, row_count, col_count, base_shift):
    row_ids = lax.broadcasted_iota(jnp.int32, (row_count, col_count, 1), 0)
    col_ids = lax.broadcasted_iota(jnp.int32, (row_count, col_count, 1), 1)
    tap_ids = lax.broadcasted_iota(jnp.int32, (1, 1, kernel.shape[0]), 2)
    hit = row_ids - col_ids + base_shift == tap_ids
    taps = kernel.astype(jnp.float32)[None, None, :]
    matrix = jnp.sum(jnp.where(hit, taps, jnp.float32(0.0)), axis=2)
    return matrix.astype(jnp.bfloat16)


def operators(kernels, plane_count, width_x, width_y):
    reach = kernels.shape[1] // 2
    along_x = band_matrix(kernels[0], width_x + 2 * reach, width_x, 0).T
    along_x = jnp.broadcast_to(along_x[None], (plane_count,) + along_x.shape)
    return lax.optimization_barrier((
        along_x,
        band_matrix(kernels[1], width_y, width_y, reach),
        band_matrix(kernels[2], plane_count + 2 * reach, plane_count, 0).T,
    ))


def pass_xy(extended, matrices):
    width_y = extended.shape[2]
    after_x = jnp.einsum(
        "zpa,zay->zpy", matrices[0], extended, preferred_element_type=jnp.float32
    ).astype(jnp.bfloat16)
    after_y = jnp.dot(after_x.reshape(-1, width_y), matrices[1], preferred_element_type=jnp.float32)
    return after_y.reshape(after_x.shape).astype(jnp.bfloat16)


def pass_z(extended, matrix):
    planes = extended.shape[0]
    out = jnp.dot(matrix, extended.reshape(planes, -1), preferred_element_type=jnp.float32)
    return out.reshape((matrix.shape[0],) + extended.shape[1:])


def stacked_operators(kernels, plane_count, width_x, width_y):
    reach = kernels.shape[2] // 2
    views = range(kernels.shape[0])
    along_x = jnp.stack([band_matrix(kernels[v, 0], width_x + 2 * reach, width_x, 0).T for v in views])
    return lax.optimization_barrier((
        along_x,
        jnp.stack([band_matrix(kernels[v, 1], width_y, width_y, reach) for v in views]),
        jnp.stack([band_matrix(kernels[v, 2], plane_count + 2 * reach, plane_count, 0).T for v in views]),
    ))


def pass_y_views(after_x, matrices):
    shape = after_x.shape
    flat = after_x.reshape(shape[0], -1, shape[-1])
    after_y = jnp.einsum("vmy,vyq->vmq", flat, matrices, preferred_element_type=jnp.float32)
    return after_y.reshape(shape).astype(jnp.bfloat16)


def pass_z_views(after_y, matrices, reach):
    below, above = z_rims(after_y, reach, 1)
    widened = jnp.concatenate([below, after_y, above], axis=1)
    return jnp.einsum("vpa,vaxy->vpxy", matrices, widened, preferred_element_type=jnp.float32)


def z_rims(volume, reach, axis):
    slabs = lax.axis_size("view") // 2
    slab = lax.axis_index("view") // 2
    planes = volume.shape[axis]
    shape = list(volume.shape)
    shape[axis] = reach
    below = jnp.zeros(shape, volume.dtype)
    above = below
    for phase in (0, 1):
        route = []
        for low in range(phase, slabs - 1, 2):
            for bit in (0, 1):
                route += [(2 * low + bit, 2 * low + 2 + bit), (2 * low + 2 + bit, 2 * low + bit)]
        if not route:
            continue
        is_lower = slab % 2 == phase
        top = lax.slice_in_dim(volume, planes - reach, planes, axis=axis)
        bottom = lax.slice_in_dim(volume, 0, reach, axis=axis)
        payload = jnp.where(is_lower, top, bottom)
        got = lax.ppermute(payload, "view", route)
        below = jnp.where(is_lower, below, got)
        above = jnp.where(is_lower, got, above)
    return below, above


def x_rims(block, reach, axis):
    tiles = lax.axis_size("tile")
    views = lax.axis_size("view")
    route = []
    for tile in range(tiles - 1):
        for slab in range(views // 2):
            right_core = tile * views + 2 * slab + 1
            left_core = (tile + 1) * views + 2 * slab
            route += [(right_core, left_core), (left_core, right_core)]
    first = lax.axis_index("view") % 2 == 0
    width = block.shape[axis]
    front = lax.slice_in_dim(block, 0, reach, axis=axis)
    back = lax.slice_in_dim(block, width - reach, width, axis=axis)
    outward = jnp.where(first, front, back)
    inward = jnp.where(first, back, front)
    across = lax.ppermute(outward, ("tile", "view"), route)
    beside = from_partner(inward, "view", 0)
    low = jnp.where(first, across, beside)
    high = jnp.where(first, beside, across)
    return low, high


def local(acquired, psf_taps, block_source):
    planes, width_x, width_y = acquired.shape
    block_count = width_x // BX
    capacity = block_count // 2
    reach = psf_taps.shape[2] // 2
    tile_index = lax.axis_index("tile")
    tile_total = lax.axis_size("tile")
    view_bit = lax.axis_index("view") % 2
    sources = block_source[0]
    blocks = acquired.reshape(planes, block_count, BX, width_y)
    half_x = width_x // 2
    half_rows = planes // 2
    half_blocks = block_count // 2
    first = view_bit == 0
    starts = []
    for target, half in ((tile_index, 0), (tile_index, 1), (tile_index + 1, 0), (tile_index - 1, 1)):
        target = jnp.clip(target, 0, tile_total - 1)
        starts.append(target * block_count + half * half_blocks)
    slots = jnp.concatenate([lax.dynamic_slice_in_dim(sources, st, half_blocks) for st in starts])
    row_ids = jnp.arange(slots.shape[0] * BX, dtype=jnp.int32)
    row_slots = slots[row_ids // BX]
    source_x = (row_slots % block_count) * BX + row_ids % BX
    chosen_rows = (row_slots // block_count == tile_index)[:, None] & (
        source_x[:, None] == jnp.arange(width_x, dtype=jnp.int32)[None, :]
    )
    selection = jnp.broadcast_to(chosen_rows.astype(acquired.dtype)[None], (planes,) + chosen_rows.shape)
    partials = jnp.einsum(
        "zrx,zxy->zry", selection, acquired, preferred_element_type=jnp.float32
    ).astype(acquired.dtype)
    partials = partials.reshape(planes, 4, half_x, width_y)
    own_keep = jnp.where(first, partials[:, 0], partials[:, 1])
    own_give = jnp.where(first, partials[:, 1], partials[:, 0])
    cross_keep = jnp.where(first, partials[:, 3], partials[:, 2])
    cross_pass = jnp.where(first, partials[:, 2], partials[:, 3])
    got = from_partner(jnp.stack([own_give, cross_pass]), "view", 0)
    tiles = lax.axis_size("tile")
    views = lax.axis_size("view")
    route = []
    for tile in range(tiles - 1):
        for slab in range(views // 2):
            right_core = tile * views + 2 * slab + 1
            left_core = (tile + 1) * views + 2 * slab
            route += [(right_core, left_core), (left_core, right_core)]
    outgoing = jnp.stack([cross_keep, got[1]])
    outgoing, psf_taps = lax.optimization_barrier((outgoing, psf_taps))
    arrived = lax.ppermute(outgoing, ("tile", "view"), route)
    local = jnp.stack([own_keep, got[0]]) + arrived[::-1]
    views_measured = jnp.where(first, local, local[::-1])
    observed = views_measured.astype(jnp.float32)
    estimate = 0.5 * (observed[0] + observed[1])
    kernels = (psf_taps / jnp.sum(psf_taps, axis=2, keepdims=True)).astype(jnp.bfloat16)
    view_count = kernels.shape[0]
    forward_ops = stacked_operators(kernels, planes, half_x, width_y)
    adjoint_ops = stacked_operators(kernels[:, :, ::-1], planes, half_x, width_y)
    for iteration in range(ITERS):
        estimate_low = estimate.astype(jnp.bfloat16)
        low, high = x_rims(estimate_low, reach, 1)
        extended = jnp.concatenate([low, estimate_low, high], axis=1)
        after_x = jnp.einsum(
            "vpa,zay->vzpy", forward_ops[0], extended, preferred_element_type=jnp.float32
        ).astype(jnp.bfloat16)
        blurred = pass_z_views(pass_y_views(after_x, forward_ops[1]), forward_ops[2], reach)
        quotients = (observed / blurred).astype(jnp.bfloat16)
        low, high = x_rims(quotients, reach, 2)
        widened = jnp.concatenate([low, quotients, high], axis=2)
        after_x = jnp.einsum(
            "vpa,vzay->vzpy", adjoint_ops[0], widened, preferred_element_type=jnp.float32
        ).astype(jnp.bfloat16)
        backs = pass_z_views(pass_y_views(after_x, adjoint_ops[1]), adjoint_ops[2], reach)
        estimate = estimate * (0.5 * (backs[0] + backs[1]))
    keep = lax.dynamic_slice_in_dim(estimate, view_bit * half_rows, half_rows, 0)
    give = lax.dynamic_slice_in_dim(estimate, (1 - view_bit) * half_rows, half_rows, 0)
    got = from_partner(give, "view", 0)
    both = jnp.concatenate([keep, got, keep], axis=1)
    return lax.dynamic_slice_in_dim(both, view_bit * half_x, width_x, 1)


def solution(mesh):
    in_specs = (P(("timepoin", "view"), "tile", None), P(), P(("timepoin", "view"), None))
    out_specs = P(("timepoin", "view"), "tile", None)
    return jax.shard_map(local, mesh=mesh, in_specs=in_specs, out_specs=out_specs, check_vma=False)
```

```python
import jax
import jax.numpy as jnp
from jax import lax
from jax.sharding import PartitionSpec as P

BX = 4
ITERS = 2


def shifted(block, axis, distance):
    devices = range(lax.axis_size(axis))
    route = [(i - distance, i) for i in devices if i - distance in devices]
    return lax.ppermute(block, axis, route)


def from_partner(block, axis, distance):
    count = lax.axis_size(axis)
    route = []
    for low in range(count):
        high = low | 1 << distance
        if high != low and high < count:
            route += [(low, high), (high, low)]
    return lax.ppermute(block, axis, route)


def extended_2(block, sides, width):
    for axis, dim in sides:
        count = lax.axis_size(axis)
        forward = [(i, i + 1) for i in range(count - 1)]
        backward = [(target, source) for source, target in forward]
        low = lax.ppermute(
            lax.slice_in_dim(block, block.shape[dim] - width, None, axis=dim), axis, forward
        )
        high = lax.ppermute(lax.slice_in_dim(block, 0, width, axis=dim), axis, backward)
        block = jnp.concatenate([low, block, high], axis=dim)
    return block


def band_matrix(kernel, row_count, col_count, base_shift):
    row_ids = lax.broadcasted_iota(jnp.int32, (row_count, col_count, 1), 0)
    col_ids = lax.broadcasted_iota(jnp.int32, (row_count, col_count, 1), 1)
    tap_ids = lax.broadcasted_iota(jnp.int32, (1, 1, kernel.shape[0]), 2)
    hit = row_ids - col_ids + base_shift == tap_ids
    taps = kernel.astype(jnp.float32)[None, None, :]
    matrix = jnp.sum(jnp.where(hit, taps, jnp.float32(0.0)), axis=2)
    return matrix.astype(jnp.bfloat16)


def operators(kernels, plane_count, width_x, width_y):
    reach = kernels.shape[1] // 2
    along_x = band_matrix(kernels[0], width_x + 2 * reach, width_x, 0).T
    along_x = jnp.broadcast_to(along_x[None], (plane_count,) + along_x.shape)
    return lax.optimization_barrier((
        along_x,
        band_matrix(kernels[1], width_y, width_y, reach),
        band_matrix(kernels[2], plane_count + 2 * reach, plane_count, 0).T,
    ))


def pass_xy(extended, matrices):
    width_y = extended.shape[2]
    after_x = jnp.einsum(
        "zpa,zay->zpy", matrices[0], extended, preferred_element_type=jnp.float32
    ).astype(jnp.bfloat16)
    after_y = jnp.dot(after_x.reshape(-1, width_y), matrices[1], preferred_element_type=jnp.float32)
    return after_y.reshape(after_x.shape).astype(jnp.bfloat16)


def pass_z(extended, matrix):
    planes = extended.shape[0]
    out = jnp.dot(matrix, extended.reshape(planes, -1), preferred_element_type=jnp.float32)
    return out.reshape((matrix.shape[0],) + extended.shape[1:])


def stacked_operators(kernels, plane_count, width_x, width_y):
    reach = kernels.shape[2] // 2
    views = range(kernels.shape[0])
    along_x = jnp.stack([band_matrix(kernels[v, 0], width_x + 2 * reach, width_x, 0).T for v in views])
    along_x = jnp.broadcast_to(along_x[:, None], (along_x.shape[0], plane_count) + along_x.shape[1:])
    return ((
        along_x,
        jnp.stack([band_matrix(kernels[v, 1], width_y, width_y, reach) for v in views]),
        jnp.stack([band_matrix(kernels[v, 2], plane_count + 2 * reach, plane_count, 0).T for v in views]),
    ))


def pass_y_views(after_x, matrices):
    shape = after_x.shape
    flat = after_x.reshape(shape[0], -1, shape[-1])
    after_y = jnp.einsum("vmy,vyq->vmq", flat, matrices, preferred_element_type=jnp.float32)
    return after_y.reshape(shape).astype(jnp.bfloat16)


def pass_z_views(after_y, matrices, reach):
    below, above = z_rims(after_y, reach, 1)
    widened = jnp.concatenate([below, after_y, above], axis=1)
    return jnp.einsum("vpa,vaxy->vpxy", matrices, widened, preferred_element_type=jnp.float32)


def z_rims(volume, reach, axis):
    slabs = lax.axis_size("view") // 2
    slab = lax.axis_index("view") // 2
    planes = volume.shape[axis]
    shape = list(volume.shape)
    shape[axis] = reach
    below = jnp.zeros(shape, volume.dtype)
    above = below
    for phase in (0, 1):
        route = []
        for low in range(phase, slabs - 1, 2):
            for bit in (0, 1):
                route += [(2 * low + bit, 2 * low + 2 + bit), (2 * low + 2 + bit, 2 * low + bit)]
        if not route:
            continue
        is_lower = slab % 2 == phase
        top = lax.slice_in_dim(volume, planes - reach, planes, axis=axis)
        bottom = lax.slice_in_dim(volume, 0, reach, axis=axis)
        payload = jnp.where(is_lower, top, bottom)
        got = lax.ppermute(payload, "view", route)
        below = jnp.where(is_lower, below, got)
        above = jnp.where(is_lower, got, above)
    return below, above


def x_rims(block, reach, axis):
    tiles = lax.axis_size("tile")
    views = lax.axis_size("view")
    route = []
    for tile in range(tiles - 1):
        for slab in range(views // 2):
            right_core = tile * views + 2 * slab + 1
            left_core = (tile + 1) * views + 2 * slab
            route += [(right_core, left_core), (left_core, right_core)]
    first = lax.axis_index("view") % 2 == 0
    width = block.shape[axis]
    front = lax.slice_in_dim(block, 0, reach, axis=axis)
    back = lax.slice_in_dim(block, width - reach, width, axis=axis)
    outward = jnp.where(first, front, back)
    inward = jnp.where(first, back, front)
    across = lax.ppermute(outward, ("tile", "view"), route)
    beside = from_partner(inward, "view", 0)
    low = jnp.where(first, across, beside)
    high = jnp.where(first, beside, across)
    return low, high


def local(acquired, psf_taps, block_source):
    planes, width_x, width_y = acquired.shape
    block_count = width_x // BX
    capacity = block_count // 2
    reach = psf_taps.shape[2] // 2
    tile_index = lax.axis_index("tile")
    tile_total = lax.axis_size("tile")
    view_bit = lax.axis_index("view") % 2
    sources = block_source[0]
    blocks = acquired.reshape(planes, block_count, BX, width_y)
    half_x = width_x // 2
    half_rows = planes // 2
    half_blocks = block_count // 2
    first = view_bit == 0
    starts = []
    for target, half in ((tile_index, 0), (tile_index, 1), (tile_index + 1, 0), (tile_index - 1, 1)):
        target = jnp.clip(target, 0, tile_total - 1)
        starts.append(target * block_count + half * half_blocks)
    slots = jnp.concatenate([lax.dynamic_slice_in_dim(sources, st, half_blocks) for st in starts])
    row_ids = jnp.arange(slots.shape[0] * BX, dtype=jnp.int32)
    row_slots = slots[row_ids // BX]
    source_x = (row_slots % block_count) * BX + row_ids % BX
    chosen_rows = (row_slots // block_count == tile_index)[:, None] & (
        source_x[:, None] == jnp.arange(width_x, dtype=jnp.int32)[None, :]
    )
    selection = jnp.broadcast_to(chosen_rows.astype(acquired.dtype)[None], (planes,) + chosen_rows.shape)
    partials = jnp.einsum(
        "zrx,zxy->zry", selection, acquired, preferred_element_type=jnp.float32
    ).astype(acquired.dtype)
    partials = partials.reshape(planes, 4, half_x, width_y)
    own_keep = jnp.where(first, partials[:, 0], partials[:, 1])
    own_give = jnp.where(first, partials[:, 1], partials[:, 0])
    cross_keep = jnp.where(first, partials[:, 3], partials[:, 2])
    cross_pass = jnp.where(first, partials[:, 2], partials[:, 3])
    got = from_partner(jnp.stack([own_give, cross_pass]), "view", 0)
    tiles = lax.axis_size("tile")
    views = lax.axis_size("view")
    route = []
    for tile in range(tiles - 1):
        for slab in range(views // 2):
            right_core = tile * views + 2 * slab + 1
            left_core = (tile + 1) * views + 2 * slab
            route += [(right_core, left_core), (left_core, right_core)]
    outgoing = jnp.stack([cross_keep, got[1]])
    outgoing, psf_taps = lax.optimization_barrier((outgoing, psf_taps))
    arrived = lax.ppermute(outgoing, ("tile", "view"), route)
    local = jnp.stack([own_keep, got[0]]) + arrived[::-1]
    views_measured = jnp.where(first, local, local[::-1])
    observed = views_measured.astype(jnp.float32)
    estimate = 0.5 * (observed[0] + observed[1])
    kernels = (psf_taps / jnp.sum(psf_taps, axis=2, keepdims=True)).astype(jnp.bfloat16)
    view_count = kernels.shape[0]
    forward_ops = stacked_operators(kernels, planes, half_x, width_y)
    adjoint_ops = stacked_operators(kernels[:, :, ::-1], planes, half_x, width_y)
    for iteration in range(ITERS):
        estimate_low = estimate.astype(jnp.bfloat16)
        low, high = x_rims(estimate_low, reach, 1)
        extended = jnp.concatenate([low, estimate_low, high], axis=1)
        after_x = jnp.einsum(
            "vzpa,zay->vzpy", forward_ops[0], extended, preferred_element_type=jnp.float32
        ).astype(jnp.bfloat16)
        blurred = pass_z_views(pass_y_views(after_x, forward_ops[1]), forward_ops[2], reach)
        quotients = (observed / blurred).astype(jnp.bfloat16)
        low, high = x_rims(quotients, reach, 2)
        widened = jnp.concatenate([low, quotients, high], axis=2)
        after_x = jnp.einsum(
            "vzpa,vzay->vzpy", adjoint_ops[0], widened, preferred_element_type=jnp.float32
        ).astype(jnp.bfloat16)
        backs = pass_z_views(pass_y_views(after_x, adjoint_ops[1]), adjoint_ops[2], reach)
        estimate = estimate * (0.5 * (backs[0] + backs[1]))
    keep = lax.dynamic_slice_in_dim(estimate, view_bit * half_rows, half_rows, 0)
    give = lax.dynamic_slice_in_dim(estimate, (1 - view_bit) * half_rows, half_rows, 0)
    got = from_partner(give, "view", 0)
    both = jnp.concatenate([keep, got, keep], axis=1)
    return lax.dynamic_slice_in_dim(both, view_bit * half_x, width_x, 1)


def solution(mesh):
    in_specs = (P(("timepoin", "view"), "tile", None), P(), P(("timepoin", "view"), None))
    out_specs = P(("timepoin", "view"), "tile", None)
    return jax.shard_map(local, mesh=mesh, in_specs=in_specs, out_specs=out_specs, check_vma=False)
```

```python
import jax
import jax.numpy as jnp
from jax import lax
from jax.sharding import PartitionSpec as P

BX = 4
ITERS = 2


def shifted(block, axis, distance):
    devices = range(lax.axis_size(axis))
    route = [(i - distance, i) for i in devices if i - distance in devices]
    return lax.ppermute(block, axis, route)


def from_partner(block, axis, distance):
    count = lax.axis_size(axis)
    route = []
    for low in range(count):
        high = low | 1 << distance
        if high != low and high < count:
            route += [(low, high), (high, low)]
    return lax.ppermute(block, axis, route)


def extended_2(block, sides, width):
    for axis, dim in sides:
        count = lax.axis_size(axis)
        forward = [(i, i + 1) for i in range(count - 1)]
        backward = [(target, source) for source, target in forward]
        low = lax.ppermute(
            lax.slice_in_dim(block, block.shape[dim] - width, None, axis=dim), axis, forward
        )
        high = lax.ppermute(lax.slice_in_dim(block, 0, width, axis=dim), axis, backward)
        block = jnp.concatenate([low, block, high], axis=dim)
    return block


def band_matrix(kernel, row_count, col_count, base_shift):
    row_ids = lax.broadcasted_iota(jnp.int32, (row_count, col_count, 1), 0)
    col_ids = lax.broadcasted_iota(jnp.int32, (row_count, col_count, 1), 1)
    tap_ids = lax.broadcasted_iota(jnp.int32, (1, 1, kernel.shape[0]), 2)
    hit = row_ids - col_ids + base_shift == tap_ids
    taps = kernel.astype(jnp.float32)[None, None, :]
    matrix = jnp.sum(jnp.where(hit, taps, jnp.float32(0.0)), axis=2)
    return matrix.astype(jnp.bfloat16)


def operators(kernels, plane_count, width_x, width_y):
    reach = kernels.shape[1] // 2
    along_x = band_matrix(kernels[0], width_x + 2 * reach, width_x, 0).T
    along_x = jnp.broadcast_to(along_x[None], (plane_count,) + along_x.shape)
    return lax.optimization_barrier((
        along_x,
        band_matrix(kernels[1], width_y, width_y, reach),
        band_matrix(kernels[2], plane_count + 2 * reach, plane_count, 0).T,
    ))


def pass_xy(extended, matrices):
    width_y = extended.shape[2]
    after_x = jnp.einsum(
        "zpa,zay->zpy", matrices[0], extended, preferred_element_type=jnp.float32
    ).astype(jnp.bfloat16)
    after_y = jnp.dot(after_x.reshape(-1, width_y), matrices[1], preferred_element_type=jnp.float32)
    return after_y.reshape(after_x.shape).astype(jnp.bfloat16)


def pass_z(extended, matrix):
    planes = extended.shape[0]
    out = jnp.dot(matrix, extended.reshape(planes, -1), preferred_element_type=jnp.float32)
    return out.reshape((matrix.shape[0],) + extended.shape[1:])


def stacked_operators(kernels, plane_count, width_x, width_y):
    reach = kernels.shape[2] // 2
    views = range(kernels.shape[0])
    along_x = jnp.stack([band_matrix(kernels[v, 0], width_x + 2 * reach, width_x, 0).T for v in views])
    along_x = jnp.broadcast_to(along_x[:, None], (along_x.shape[0], plane_count) + along_x.shape[1:])
    return lax.optimization_barrier((
        along_x,
        jnp.stack([band_matrix(kernels[v, 1], width_y, width_y, reach) for v in views]),
        jnp.stack([band_matrix(kernels[v, 2], plane_count + 2 * reach, plane_count, 0).T for v in views]),
    ))


def pass_y_views(after_x, matrices):
    shape = after_x.shape
    flat = after_x.reshape(shape[0], -1, shape[-1])
    after_y = jnp.einsum("vmy,vyq->vmq", flat, matrices, preferred_element_type=jnp.float32)
    return after_y.reshape(shape).astype(jnp.bfloat16)


def pass_z_views(after_y, matrices, reach):
    below, above = z_rims(after_y, reach, 1)
    widened = jnp.concatenate([below, after_y, above], axis=1)
    return jnp.einsum("vpa,vaxy->vpxy", matrices, widened, preferred_element_type=jnp.float32)


def z_rims(volume, reach, axis):
    slabs = lax.axis_size("view") // 2
    slab = lax.axis_index("view") // 2
    planes = volume.shape[axis]
    shape = list(volume.shape)
    shape[axis] = reach
    below = jnp.zeros(shape, volume.dtype)
    above = below
    for phase in (0, 1):
        route = []
        for low in range(phase, slabs - 1, 2):
            for bit in (0, 1):
                route += [(2 * low + bit, 2 * low + 2 + bit), (2 * low + 2 + bit, 2 * low + bit)]
        if not route:
            continue
        is_lower = slab % 2 == phase
        top = lax.slice_in_dim(volume, planes - reach, planes, axis=axis)
        bottom = lax.slice_in_dim(volume, 0, reach, axis=axis)
        payload = jnp.where(is_lower, top, bottom)
        got = lax.ppermute(payload, "view", route)
        below = jnp.where(is_lower, below, got)
        above = jnp.where(is_lower, got, above)
    return below, above


def x_rims(block, reach, axis):
    tiles = lax.axis_size("tile")
    views = lax.axis_size("view")
    route = []
    for tile in range(tiles - 1):
        for slab in range(views // 2):
            right_core = tile * views + 2 * slab + 1
            left_core = (tile + 1) * views + 2 * slab
            route += [(right_core, left_core), (left_core, right_core)]
    first = lax.axis_index("view") % 2 == 0
    width = block.shape[axis]
    front = lax.slice_in_dim(block, 0, reach, axis=axis)
    back = lax.slice_in_dim(block, width - reach, width, axis=axis)
    inward = jnp.where(first, back, front)
    whole = lax.ppermute(block, ("tile", "view"), route)
    beside = from_partner(inward, "view", 0)
    low = jnp.where(first, lax.slice_in_dim(whole, width - reach, width, axis=axis), beside)
    high = jnp.where(first, beside, lax.slice_in_dim(whole, 0, reach, axis=axis))
    return low, high


def local(acquired, psf_taps, block_source):
    planes, width_x, width_y = acquired.shape
    block_count = width_x // BX
    capacity = block_count // 2
    reach = psf_taps.shape[2] // 2
    tile_index = lax.axis_index("tile")
    tile_total = lax.axis_size("tile")
    view_bit = lax.axis_index("view") % 2
    sources = block_source[0]
    blocks = acquired.reshape(planes, block_count, BX, width_y)
    half_x = width_x // 2
    half_rows = planes // 2
    half_blocks = block_count // 2
    first = view_bit == 0
    starts = []
    for target, half in ((tile_index, 0), (tile_index, 1), (tile_index + 1, 0), (tile_index - 1, 1)):
        target = jnp.clip(target, 0, tile_total - 1)
        starts.append(target * block_count + half * half_blocks)
    slots = jnp.concatenate([lax.dynamic_slice_in_dim(sources, st, half_blocks) for st in starts])
    row_ids = jnp.arange(slots.shape[0] * BX, dtype=jnp.int32)
    row_slots = slots[row_ids // BX]
    source_x = (row_slots % block_count) * BX + row_ids % BX
    chosen_rows = (row_slots // block_count == tile_index)[:, None] & (
        source_x[:, None] == jnp.arange(width_x, dtype=jnp.int32)[None, :]
    )
    selection = jnp.broadcast_to(chosen_rows.astype(acquired.dtype)[None], (planes,) + chosen_rows.shape)
    partials = jnp.einsum(
        "zrx,zxy->zry", selection, acquired, preferred_element_type=jnp.float32
    ).astype(acquired.dtype)
    partials = partials.reshape(planes, 4, half_x, width_y)
    own_keep = jnp.where(first, partials[:, 0], partials[:, 1])
    own_give = jnp.where(first, partials[:, 1], partials[:, 0])
    cross_keep = jnp.where(first, partials[:, 3], partials[:, 2])
    cross_pass = jnp.where(first, partials[:, 2], partials[:, 3])
    got = from_partner(jnp.stack([own_give, cross_pass]), "view", 0)
    tiles = lax.axis_size("tile")
    views = lax.axis_size("view")
    route = []
    for tile in range(tiles - 1):
        for slab in range(views // 2):
            right_core = tile * views + 2 * slab + 1
            left_core = (tile + 1) * views + 2 * slab
            route += [(right_core, left_core), (left_core, right_core)]
    outgoing = jnp.stack([cross_keep, got[1]])
    outgoing, psf_taps = lax.optimization_barrier((outgoing, psf_taps))
    arrived = lax.ppermute(outgoing, ("tile", "view"), route)
    local = jnp.stack([own_keep, got[0]]) + arrived[::-1]
    views_measured = jnp.where(first, local, local[::-1])
    observed = views_measured.astype(jnp.float32)
    estimate = 0.5 * (observed[0] + observed[1])
    kernels = (psf_taps / jnp.sum(psf_taps, axis=2, keepdims=True)).astype(jnp.bfloat16)
    view_count = kernels.shape[0]
    forward_ops = stacked_operators(kernels, planes, half_x, width_y)
    adjoint_ops = stacked_operators(kernels[:, :, ::-1], planes, half_x, width_y)
    for iteration in range(ITERS):
        estimate_low = estimate.astype(jnp.bfloat16)
        low, high = x_rims(estimate_low, reach, 1)
        extended = jnp.concatenate([low, estimate_low, high], axis=1)
        after_x = jnp.einsum(
            "vzpa,zay->vzpy", forward_ops[0], extended, preferred_element_type=jnp.float32
        ).astype(jnp.bfloat16)
        blurred = pass_z_views(pass_y_views(after_x, forward_ops[1]), forward_ops[2], reach)
        quotients = (observed / blurred).astype(jnp.bfloat16)
        low, high = x_rims(quotients, reach, 2)
        widened = jnp.concatenate([low, quotients, high], axis=2)
        after_x = jnp.einsum(
            "vzpa,vzay->vzpy", adjoint_ops[0], widened, preferred_element_type=jnp.float32
        ).astype(jnp.bfloat16)
        backs = pass_z_views(pass_y_views(after_x, adjoint_ops[1]), adjoint_ops[2], reach)
        estimate = estimate * (0.5 * (backs[0] + backs[1]))
    keep = lax.dynamic_slice_in_dim(estimate, view_bit * half_rows, half_rows, 0)
    give = lax.dynamic_slice_in_dim(estimate, (1 - view_bit) * half_rows, half_rows, 0)
    got = from_partner(give, "view", 0)
    both = jnp.concatenate([keep, got, keep], axis=1)
    return lax.dynamic_slice_in_dim(both, view_bit * half_x, width_x, 1)


def solution(mesh):
    in_specs = (P(("timepoin", "view"), "tile", None), P(), P(("timepoin", "view"), None))
    out_specs = P(("timepoin", "view"), "tile", None)
    return jax.shard_map(local, mesh=mesh, in_specs=in_specs, out_specs=out_specs, check_vma=False)
```
